32 devices in a mesh: groups: 2 (over x), seq: 8 (over z, y), head: 2 (over core).
Axes of the slice: x: 2, y: 2, z: 4, core: 2. Of those that a mesh axis runs over, the one named last changes fastest.
Arguments:
- x_input: bfloat16 [2048, 4096], P(('groups', 'seq'), 'head'), parts along dimension 0, may hold values from -6 to 6
- b_rows: bfloat16 [2048, 128], P(('groups', 'seq')), parts along dimension 0, may hold values from -0.5 to 0.5
- c_rows: bfloat16 [2048, 128], P(('groups', 'seq')), parts along dimension 0, may hold values from -0.5 to 0.5
- decay_log: float32 [64, 1024], P(('groups', 'head'), 'seq'), parts along dimension 0, may hold values from -1 to 0
- skip_gain: float32 [32], P('head'), may hold values from 0.5 to 1.5
- doc_lengths: int32 [8], P('groups'), parts along dimension 0, may hold values from 1 to 512, 1024 in all
- queries: bfloat16 [2048, 2048], P(('groups', 'seq'), 'head'), parts along dimension 0, may hold values from -9 to 9
- attention_key_rows: bfloat16 [2048, 512], P(('groups', 'seq'), 'head'), parts along dimension 0, may hold values from -9 to 9
- values: bfloat16 [2048, 512], P(('groups', 'seq'), 'head'), parts along dimension 0, may hold values from -6 to 6
- mixer_cot: bfloat16 [2048, 4096], P(('groups', 'seq'), 'head'), parts along dimension 0, may hold values from -6 to 6
- attention_output_cotangent: bfloat16 [2048, 2048], P(('groups', 'seq'), 'head'), parts along dimension 0, may hold values from -6 to 6
Outputs:
- mixer_out: bfloat16 [2048, 4096], P(('groups', 'seq'), 'head'), parts along dimension 0
- attn_out: bfloat16 [2048, 2048], P(('groups', 'seq'), 'head'), parts along dimension 0
- x_grad: bfloat16 [2048, 4096], P(('groups', 'seq'), 'head'), parts along dimension 0
- b_grad: float32 [2048, 128], P(('groups', 'seq')), parts along dimension 0
- c_grad: float32 [2048, 128], P(('groups', 'seq')), parts along dimension 0
- decay_grad: float32 [64, 1024], P(('groups', 'head'), 'seq'), parts along dimension 0
- q_grad: bfloat16 [2048, 2048], P(('groups', 'seq'), 'head'), parts along dimension 0
- key_gradient: bfloat16 [2048, 512], P(('groups', 'seq'), 'head'), parts along dimension 0
- value_gradient: bfloat16 [2048, 512], P(('groups', 'seq'), 'head'), parts along dimension 0
The draws below stay inside these ranges and needn't reach their ends.
There are 2 independent parts, one for each index of `groups`. The reference program is written for one: setup_inputs(seed, part) draws one part's arguments, and reference() takes and returns one part's arrays. A program takes and returns all parts, laid end to end along the dimension named above; an argument that names none is the same for every part. Nothing has to cross between parts.
Inputs may be any that keep to these rules, and one draw needn't show every extreme that they name: `doc_lengths`: the lengths of the documents packed into the stream, in order; they sum to 1024.
All inputs are finite; a program needn't handle non-finite values.
Results may differ from the reference program's by a relative error of at most 0.023.
Values may be sent and summed in bfloat16 or wider, within the bound.
No kernel may reach another device: no remote copies, remote signals or barrier semaphores. Data moves between devices by JAX's collectives and lax.ppermute only.
A program may use at most 128 MiB of HBM per device.

```python
import math
import jax
import jax.numpy as jnp
import numpy as np
from jax import lax

TOK_DEV = 128
DOCS = 4
HM = 32
P_SIZE = 128
NS = 128
QUERY_HEADS = 16
KEY_VALUE_HEADS = 4
HEAD_SIZE = 128
STREAM_LENGTH = 1024


def draw_queries(key, part):
    base_offset = jax.random.fold_in(key, 1)
    sampled_values = jnp.clip(jax.random.normal(base_offset, (STREAM_LENGTH, QUERY_HEADS * HEAD_SIZE), jnp.float32), -6.0, 6.0)
    return sampled_values.astype(jnp.bfloat16)


def draw_attention_key_rows(key, part):
    base_offset = jax.random.fold_in(key, 2)
    sampled_values = jnp.clip(jax.random.normal(base_offset, (STREAM_LENGTH, KEY_VALUE_HEADS * HEAD_SIZE), jnp.float32), -6.0, 6.0)
    return sampled_values.astype(jnp.bfloat16)


def draw_decay_log(key, part):
    random_subkeys = jax.random.split(jax.random.fold_in(key, 3), 7)
    head_flags = jax.random.randint(random_subkeys[0], (HM,), 0, 10)
    is_fast = head_flags < 5
    fast_rate = jnp.exp(jax.random.uniform(random_subkeys[1], (HM,), jnp.float32, math.log(1.0 / 50.0), math.log(1.0 / 30.0)))
    slow_rate = jnp.exp(jax.random.uniform(random_subkeys[2], (HM,), jnp.float32, math.log(0.2), math.log(0.8))) / STREAM_LENGTH
    per_head_rate = jnp.where(is_fast, fast_rate, slow_rate)
    small_noise = jax.random.uniform(random_subkeys[3], (HM, STREAM_LENGTH), jnp.float32, 0.5, 1.5)
    block_rate = jnp.exp(jax.random.uniform(random_subkeys[4], (STREAM_LENGTH // TOK_DEV,), jnp.float32, math.log(0.5), math.log(2.0)))
    spread_width = jnp.repeat(block_rate, TOK_DEV)
    spike_rows = jax.random.permutation(random_subkeys[5], STREAM_LENGTH)[:2]
    spike_loss = jax.random.uniform(random_subkeys[6], (2,), jnp.float32, 0.2, 0.5)
    spike_list = jnp.zeros((STREAM_LENGTH,), jnp.float32).at[spike_rows].set(jnp.log(1.0 - spike_loss))
    return -per_head_rate[:, None] * small_noise * spread_width[None, :] + spike_list[None, :]


def levels(own_key, dims, cuts, smallest, top_value):
    level, own = 1.0, jax.random.fold_in(own_key, 6)
    for dim, blocks in cuts:
        heights = jnp.exp(jax.random.uniform(jax.random.fold_in(own, dim), (blocks,), jnp.float32, smallest / len(cuts), top_value / len(cuts)))
        level = level * jnp.repeat(heights, dims[dim] // blocks).reshape([-1 if axis == dim else 1 for axis in range(len(dims))])
    return level


def split_up(number_of, total, most, skew):
    weights = [(1 << 20) // math.isqrt(grade ** skew) + 1 for grade in range(2, number_of + 1)]
    surplus, given = total - most - (number_of - 1), [1] * (number_of - 1)
    while surplus > 0:
        free = [i for i in range(number_of - 1) if given[i] < most]
        mass, remaining = sum([weights[i] for i in free]), surplus
        for i in free:
            more = min(most - given[i], max(1, remaining * weights[i] // mass), surplus)
            given[i] = given[i] + more
            surplus = surplus - more
    return np.array([most] + given)


def ragged_sizes(rng, amount, total, bound, slope):
    if amount == 2:
        one = jax.random.randint(rng, (), max(1, total - bound), min(bound, total - 1) + 1)
        return jnp.stack([one, total - one])
    sizes = jnp.asarray(split_up(amount, total, bound, slope), jnp.int32)
    twos = (amount - 1) // 2
    giver, taker = sizes[1:1 + 2 * twos:2], sizes[2:2 + 2 * twos:2]
    room = jnp.minimum(giver - 1, bound - taker)
    passed = jax.random.randint(jax.random.fold_in(rng, 1), (twos,), 0, 1 << 20) % (room + 1)
    sizes = sizes.at[1:1 + 2 * twos:2].set(giver - passed).at[2:2 + 2 * twos:2].set(taker + passed)
    return sizes[jax.random.permutation(jax.random.fold_in(rng, 2), amount)]


def noise(stream_key, extent, scale, bound, cuts=(), kind=jnp.bfloat16):
    values = scale * jax.random.normal(stream_key, extent, jnp.float32)
    if cuts:
        values = values * levels(stream_key, extent, cuts, -0.22, 0.18)
    return jnp.clip(values, -bound, bound).astype(kind)


def setup_inputs(seed: int = 0, part: int = 0) -> dict:
    streams_of = jax.random.split(jax.random.key(seed), 12)
    part_keys = jax.random.split(jax.random.fold_in(streams_of[11], part), 12)
    x_input = noise(part_keys[0], (STREAM_LENGTH, HM * P_SIZE), 1.0, 6.0, ((0, 8), (1, 2)))
    b_rows = noise(part_keys[1], (STREAM_LENGTH, NS), NS ** -0.5, 0.5, ((0, 8),))
    c_rows = noise(part_keys[2], (STREAM_LENGTH, NS), NS ** -0.5, 0.5, ((0, 8),))
    decay_log = draw_decay_log(jax.random.fold_in(jax.random.fold_in(streams_of[11], part), 71), part)
    skip_gain = jnp.clip(0.5 + 1.0 * jax.random.uniform(streams_of[4], (HM,), jnp.float32) ** levels(streams_of[4], (HM,), ((0, 2),), -0.2, 0.2), 0.5, 1.5)
    doc_lengths = ragged_sizes(part_keys[5], DOCS, STREAM_LENGTH, STREAM_LENGTH // 2, 2).astype(jnp.int32)
    queries = draw_queries(jax.random.fold_in(jax.random.fold_in(streams_of[11], part), 71), part)
    attention_key_rows = draw_attention_key_rows(jax.random.fold_in(jax.random.fold_in(streams_of[11], part), 71), part)
    values = noise(part_keys[8], (STREAM_LENGTH, KEY_VALUE_HEADS * HEAD_SIZE), 1.0, 6.0, ((0, 8), (1, 2)))
    mixer_cot = noise(part_keys[9], (STREAM_LENGTH, HM * P_SIZE), 1.0, 6.0, ((0, 8), (1, 2)))
    attention_output_cotangent = noise(part_keys[10], (STREAM_LENGTH, QUERY_HEADS * HEAD_SIZE), 1.0, 6.0, ((0, 8), (1, 2)))
    return dict(x_input=x_input, b_rows=b_rows, c_rows=c_rows, decay_log=decay_log, skip_gain=skip_gain, doc_lengths=doc_lengths, queries=queries, attention_key_rows=attention_key_rows, values=values, mixer_cot=mixer_cot, attention_output_cotangent=attention_output_cotangent)


precise = lax.Precision.HIGHEST
big_negative = -1e+30

def doc_index(positions, lengths):
    ends = jnp.cumsum(lengths)
    return lax.optimization_barrier(jnp.sum((positions[:, None] >= ends[None, :]).astype(jnp.int32), axis=1)).astype(jnp.int32)

def cumulate(decay):
    return jnp.cumsum(decay, axis=1)

def local_state(inputs, b_float, cumulated, segment):
    weights = jnp.exp(cumulated[:, -1:] - cumulated) * (segment == segment[-1]).astype(inputs.dtype)[None, :]
    return jnp.einsum('hs,sn,shp->hnp', weights, b_float, inputs, precision=precise)

def carry_factor(cumulated, segment, before):
    return jnp.exp(cumulated[:, -1]) * (segment[-1] == before).astype(cumulated.dtype)

def mixer_stretch(inputs, b_float, c_float, decay, gains, segment, before, state_in):
    cumulated = cumulate(decay)
    width = inputs.shape[0]
    steps = jnp.arange(width)
    allowed = (steps[:, None] >= steps[None, :]) & (segment[:, None] == segment[None, :])
    gaps = jnp.where(allowed[None], cumulated[:, :, None] - cumulated[:, None, :], big_negative)
    kernel = jnp.exp(gaps) * jnp.dot(c_float, b_float.T, precision=precise)[None]
    inner = jnp.einsum('hts,shp->thp', kernel, inputs, precision=precise)
    keeps = (segment == before).astype(inputs.dtype)
    entering = jnp.einsum('tn,hnp->thp', c_float, state_in, precision=precise)
    reach = jnp.exp(cumulated).T * keeps[:, None]
    outputs = inner + reach[:, :, None] * entering + gains[None, :, None] * inputs
    factor = carry_factor(cumulated, segment, before)
    state_out = factor[:, None, None] * state_in + local_state(inputs, b_float, cumulated, segment)
    return (outputs, state_out)

def mixer_sequence(inputs, b_float, c_float, decay, gains, segments):
    stretches = STREAM_LENGTH // TOK_DEV
    input_blocks = inputs.reshape(stretches, TOK_DEV, HM, P_SIZE)
    b_blocks = b_float.reshape(stretches, TOK_DEV, NS)
    c_blocks = c_float.reshape(stretches, TOK_DEV, NS)
    decay_blocks = decay.reshape(HM, stretches, TOK_DEV).transpose(1, 0, 2)
    seg_blocks = segments.reshape(stretches, TOK_DEV)
    lasts = segments[TOK_DEV - 1::TOK_DEV][:stretches - 1].astype(jnp.int32)
    befores = jnp.concatenate([jnp.full((1,), -1, jnp.int32), lasts])

    def advance(carried, pieces):
        inp, brow, crow, dec, seg, before = pieces
        outputs, state_next = mixer_stretch(inp, brow, crow, dec, gains, seg, before, carried)
        return (state_next, outputs)
    start_state = jnp.zeros((HM, NS, P_SIZE), inputs.dtype)
    unused, outputs = lax.scan(advance, start_state, (input_blocks, b_blocks, c_blocks, decay_blocks, seg_blocks, befores))
    return outputs.reshape(STREAM_LENGTH, HM, P_SIZE)

def attention(queries, attention_key_rows, values, attention_output_cotangent, segments):
    logit_scale = 1.0 / math.sqrt(HEAD_SIZE)
    heads_per_group = QUERY_HEADS // KEY_VALUE_HEADS
    window_span = min(512, STREAM_LENGTH)
    positions = jnp.arange(STREAM_LENGTH, dtype=jnp.int32)
    every_key = attention_key_rows.reshape(STREAM_LENGTH, KEY_VALUE_HEADS, HEAD_SIZE).astype(jnp.float32)
    every_value = values.reshape(STREAM_LENGTH, KEY_VALUE_HEADS, HEAD_SIZE).astype(jnp.float32)
    key_gradient_total = jnp.zeros((STREAM_LENGTH, KEY_VALUE_HEADS, HEAD_SIZE), jnp.float32)
    value_gradient_total = jnp.zeros((STREAM_LENGTH, KEY_VALUE_HEADS, HEAD_SIZE), jnp.float32)
    outs_list = []
    query_grads = []
    for number in range(STREAM_LENGTH // window_span):
        lower_limit = number * window_span
        upper_limit = lower_limit + window_span
        row_entries = queries[lower_limit:upper_limit].reshape(window_span, KEY_VALUE_HEADS, heads_per_group, HEAD_SIZE).astype(jnp.float32)
        cotangent_rows = attention_output_cotangent[lower_limit:upper_limit].reshape(window_span, KEY_VALUE_HEADS, heads_per_group, HEAD_SIZE).astype(jnp.float32)
        key_part = every_key[:upper_limit]
        value_part = every_value[:upper_limit]
        allowed = (positions[None, :upper_limit] <= positions[lower_limit:upper_limit, None]) & (segments[None, :upper_limit] == segments[lower_limit:upper_limit, None])
        scores = jnp.einsum('tgrd,kgd->grtk', row_entries, key_part) * logit_scale
        scores = jnp.where(allowed[None, None], scores, big_negative)
        row_peak = lax.optimization_barrier(jnp.max(scores, axis=-1))
        row_total = lax.optimization_barrier(jnp.sum(jnp.where(allowed[None, None], jnp.exp(scores - row_peak[..., None]), 0.0), axis=-1))
        log_norm = row_peak + jnp.log(row_total)
        probs_full = jnp.where(allowed[None, None], jnp.exp(scores - log_norm[..., None]), 0.0)
        weights = lax.optimization_barrier(probs_full.astype(jnp.bfloat16)).astype(jnp.float32)
        result_output_rows = jnp.einsum('grtk,kgd->tgrd', weights, value_part).astype(jnp.bfloat16)
        row_products = jnp.einsum('bkfh,bkfh->kfb', cotangent_rows, result_output_rows.astype(jnp.float32))
        grad_prob = jnp.einsum('tgrd,kgd->grtk', cotangent_rows, value_part)
        grad_score = probs_full * (grad_prob - row_products[..., None])
        grad_score = lax.optimization_barrier(grad_score.astype(jnp.bfloat16)).astype(jnp.float32)
        grad_rows = jnp.einsum('grtk,kgd->tgrd', grad_score, key_part) * logit_scale
        key_gradient_total = key_gradient_total.at[:upper_limit].add(jnp.einsum('grtk,tgrd->kgd', grad_score, row_entries))
        value_gradient_total = value_gradient_total.at[:upper_limit].add(jnp.einsum('grtk,tgrd->kgd', weights, cotangent_rows))
        outs_list.append(result_output_rows.reshape(window_span, QUERY_HEADS * HEAD_SIZE))
        query_grads.append(grad_rows.astype(jnp.bfloat16).reshape(window_span, QUERY_HEADS * HEAD_SIZE))
    attn_out = jnp.concatenate(outs_list, axis=0)
    q_grad = jnp.concatenate(query_grads, axis=0)
    key_gradient = (key_gradient_total * logit_scale).astype(jnp.bfloat16).reshape(STREAM_LENGTH, KEY_VALUE_HEADS * HEAD_SIZE)
    value_gradient = value_gradient_total.astype(jnp.bfloat16).reshape(STREAM_LENGTH, KEY_VALUE_HEADS * HEAD_SIZE)
    return (attn_out, q_grad, key_gradient, value_gradient)

def reference(x_input, b_rows, c_rows, decay_log, skip_gain, doc_lengths, queries, attention_key_rows, values, mixer_cot, attention_output_cotangent):
    positions = jnp.arange(STREAM_LENGTH, dtype=jnp.int32)
    segments = doc_index(positions, doc_lengths)
    inputs = x_input.astype(jnp.float32).reshape(STREAM_LENGTH, HM, P_SIZE)

    def mixer_all(inp, brow, crow, dec):
        return mixer_sequence(inp, brow, crow, dec, skip_gain, segments)
    mixed, pull = jax.vjp(mixer_all, inputs, b_rows.astype(jnp.float32), c_rows.astype(jnp.float32), decay_log)
    grad_x, grad_b, grad_c, grad_decay = pull(mixer_cot.astype(jnp.float32).reshape(STREAM_LENGTH, HM, P_SIZE))
    attn_out, q_grad, key_gradient, value_gradient = attention(queries, attention_key_rows, values, attention_output_cotangent, segments)
    mixer_out = mixed.reshape(STREAM_LENGTH, HM * P_SIZE).astype(jnp.bfloat16)
    x_grad = grad_x.reshape(STREAM_LENGTH, HM * P_SIZE).astype(jnp.bfloat16)
    return (mixer_out, attn_out, x_grad, grad_b, grad_c, grad_decay, q_grad, key_gradient, value_gradient)
```

```python
import math

import jax
import jax.numpy as jnp
from jax import lax
from jax.sharding import PartitionSpec as P

P_SIZE = 128
HEAD_SIZE = 128


precise = lax.Precision.HIGHEST
big_negative = -1e30


def entering_2(part, axis, combine, identity, reverse):
    count = lax.axis_size(axis)
    place = lax.axis_index(axis)
    ahead = count - 1 - place if reverse else place
    early = jax.tree.map(lambda a, e: jnp.zeros_like(a) + jnp.asarray(e, a.dtype), part, identity)
    span = part
    shift = 1
    while shift < count:
        if reverse:
            pairs = [(i, i - shift) for i in range(shift, count)]
        else:
            pairs = [(i, i + shift) for i in range(count - shift)]
        got = lax.ppermute(span, axis, pairs)
        have = ahead >= shift
        got = jax.tree.map(lambda g, e: jnp.where(have, g, jnp.asarray(e, g.dtype)), got, identity)
        early = combine(got, early)
        if 2 * shift < count:
            span = combine(got, span)
        shift *= 2
    return early


def doc_index(positions, lengths):
    ends = jnp.cumsum(lengths)
    return jnp.sum((positions[:, None] >= ends[None, :]).astype(jnp.int32), axis=1)


def cumulate(decay):
    return jnp.cumsum(decay, axis=1)


def local_state(inputs, b_float, cumulated, segment):
    weights = (
        jnp.exp(cumulated[:, -1:] - cumulated)
        * (segment == segment[-1]).astype(inputs.dtype)[None, :]
    )
    return jnp.einsum("hs,sn,shp->hnp", weights, b_float, inputs, precision=precise)


def carry_factor(cumulated, segment, before):
    return jnp.exp(cumulated[:, -1]) * (segment[-1] == before).astype(cumulated.dtype)


def mixer_stretch(inputs, b_float, c_float, decay, gains, segment, before, state_in):
    cumulated = cumulate(decay)
    width = inputs.shape[0]
    steps = jnp.arange(width)
    allowed = (steps[:, None] >= steps[None, :]) & (segment[:, None] == segment[None, :])
    gaps = jnp.where(allowed[None], cumulated[:, :, None] - cumulated[:, None, :], big_negative)
    kernel = jnp.exp(gaps) * jnp.dot(c_float, b_float.T, precision=precise)[None]
    inner = jnp.einsum("hts,shp->thp", kernel, inputs, precision=precise)
    keeps = (segment == before).astype(inputs.dtype)
    entering = jnp.einsum("tn,hnp->thp", c_float, state_in, precision=precise)
    reach = jnp.exp(cumulated).T * keeps[:, None]
    outputs = inner + reach[:, :, None] * entering + gains[None, :, None] * inputs
    factor = carry_factor(cumulated, segment, before)
    state_out = factor[:, None, None] * state_in + local_state(inputs, b_float, cumulated, segment)
    return (outputs, state_out)


def combine_states(earlier, later):
    return (earlier[0] * later[0], later[0][:, None, None] * earlier[1] + later[1])


def on_device(
    x_input,
    b_rows,
    c_rows,
    decay_log,
    skip_gain,
    doc_lengths,
    queries,
    attention_key_rows,
    values,
    mixer_cot,
    attention_output_cotangent,
):
    tokens = x_input.shape[0]
    offset = lax.axis_index("seq") * tokens
    total_len = tokens * lax.axis_size("seq")
    positions = offset + jnp.arange(tokens, dtype=jnp.int32)
    segment = doc_index(positions, doc_lengths)
    previous = doc_index(jnp.reshape(offset - 1, (1,)), doc_lengths)[0]
    before = jnp.where(offset > 0, previous, -1)
    heads_here = skip_gain.shape[0]
    inputs = x_input.astype(jnp.float32).reshape(tokens, heads_here, P_SIZE)
    b_float = b_rows.astype(jnp.float32)
    c_float = c_rows.astype(jnp.float32)
    cot_float = mixer_cot.astype(jnp.float32).reshape(tokens, heads_here, P_SIZE)

    def stretch_of(inp, brow, crow, decay, state_in):
        return mixer_stretch(inp, brow, crow, decay, skip_gain, segment, before, state_in)

    cumulated = cumulate(decay_log)
    factor = carry_factor(cumulated, segment, before)
    summary = local_state(inputs, b_float, cumulated, segment)
    zero_state = jnp.zeros_like(summary)
    identity = (jnp.ones_like(factor), zero_state)
    state_in = entering_2((factor, summary), "seq", combine_states, identity, False)[1]
    (mixed, state_out), pull = jax.vjp(stretch_of, inputs, b_float, c_float, decay_log, state_in)
    adjoint_local = pull((cot_float, zero_state))[4]
    adjoint_out = entering_2((factor, adjoint_local), "seq", combine_states, identity, True)[1]
    grad_x, grad_b, grad_c, grad_decay, unused = pull((cot_float, adjoint_out))
    head_count = lax.axis_size("head")
    if head_count == 2:
        other_b, other_c = lax.ppermute((grad_b, grad_c), "head", [(0, 1), (1, 0)])
        grad_b, grad_c = grad_b + other_b, grad_c + other_c
    else:
        grad_b, grad_c = lax.psum((grad_b, grad_c), "head")
    mixer_out = mixed.reshape(tokens, heads_here * P_SIZE).astype(jnp.bfloat16)
    x_grad = grad_x.reshape(tokens, heads_here * P_SIZE).astype(jnp.bfloat16)
    logit_scale = 1.0 / math.sqrt(HEAD_SIZE)
    groups = attention_key_rows.shape[1] // HEAD_SIZE
    heads_per_group = queries.shape[1] // HEAD_SIZE // groups
    key_span = min(512, total_len)
    blocks = total_len // key_span
    last_pos = offset + tokens - 1
    query_grid = queries.reshape(tokens, groups, heads_per_group, HEAD_SIZE)
    cotangent_table = attention_output_cotangent.reshape(tokens, groups, heads_per_group, HEAD_SIZE)
    key_width = attention_key_rows.shape[1]
    kv_all = lax.all_gather(
        jnp.concatenate([attention_key_rows, values], axis=1), "seq", axis=0, tiled=True
    )
    key_all, value_all = kv_all[:, :key_width], kv_all[:, key_width:]

    def block_view(number):
        anchor = number * key_span
        key_blk = lax.dynamic_slice_in_dim(key_all, anchor, key_span, 0).reshape(
            key_span, groups, HEAD_SIZE
        )
        value_blk = lax.dynamic_slice_in_dim(value_all, anchor, key_span, 0).reshape(
            key_span, groups, HEAD_SIZE
        )
        key_pos = anchor + jnp.arange(key_span, dtype=jnp.int32)
        allowed = (key_pos[None, :] <= positions[:, None]) & (
            doc_index(key_pos, doc_lengths)[None, :] == segment[:, None]
        )
        scores = (
            jnp.einsum("tgrd,kgd->grtk", query_grid, key_blk, preferred_element_type=jnp.float32)
            * logit_scale
        )
        scores = jnp.where(allowed[None, None], scores, big_negative)
        return (anchor, key_blk, value_blk, allowed, scores)

    def visit(number, carried, work):
        return lax.cond(
            number * key_span <= last_pos,
            lambda inner: work(number, inner),
            lambda inner: inner,
            carried,
        )

    def stats_step(number, carried):
        row_peak, row_total = carried
        anchor, key_blk, value_blk, allowed, scores = block_view(number)
        new_peak = jnp.maximum(row_peak, jnp.max(scores, axis=-1))
        fresh = jnp.sum(
            jnp.where(allowed[None, None], jnp.exp(scores - new_peak[..., None]), 0.0), axis=-1
        )
        return (new_peak, row_total * jnp.exp(row_peak - new_peak) + fresh)

    stat_shape = (groups, heads_per_group, tokens)
    row_peak, row_total = lax.fori_loop(
        0,
        blocks,
        lambda number, carried: visit(number, carried, stats_step),
        (jnp.full(stat_shape, big_negative, jnp.float32), jnp.zeros(stat_shape, jnp.float32)),
    )
    log_norm = row_peak + jnp.log(row_total)

    def output_step(number, totals):
        anchor, key_blk, value_blk, allowed, scores = block_view(number)
        weights = jnp.where(allowed[None, None], jnp.exp(scores - log_norm[..., None]), 0.0).astype(
            jnp.bfloat16
        )
        return totals + jnp.einsum(
            "grtk,kgd->tgrd", weights, value_blk, preferred_element_type=jnp.float32
        )

    attention_table = lax.fori_loop(
        0,
        blocks,
        lambda number, carried: visit(number, carried, output_step),
        jnp.zeros((tokens, groups, heads_per_group, HEAD_SIZE), jnp.float32),
    ).astype(jnp.bfloat16)
    row_products = jnp.einsum(
        "bkfh,bkfh->kfb", cotangent_table, attention_table, preferred_element_type=jnp.float32
    )

    def grad_terms(allowed, scores, value_blk):
        probs_full = jnp.where(allowed[None, None], jnp.exp(scores - log_norm[..., None]), 0.0)
        grad_prob = jnp.einsum(
            "tgrd,kgd->grtk", cotangent_table, value_blk, preferred_element_type=jnp.float32
        )
        grad_score = (probs_full * (grad_prob - row_products[..., None])).astype(jnp.bfloat16)
        return (probs_full.astype(jnp.bfloat16), grad_score)

    query_zero = jnp.zeros((tokens, groups, heads_per_group, HEAD_SIZE), jnp.float32)

    def full_step(number, carried):
        grad_query, term_key, term_value = carried
        anchor, key_blk, value_blk, allowed, scores = block_view(number)
        weights, grad_score = grad_terms(allowed, scores, value_blk)
        grad_query = grad_query + jnp.einsum(
            "grtk,kgd->tgrd", grad_score, key_blk, preferred_element_type=jnp.float32
        )
        key_part = jnp.einsum(
            "grtk,tgrd->kgd", grad_score, query_grid, preferred_element_type=jnp.float32
        ).reshape(key_span, groups * HEAD_SIZE)
        value_part = jnp.einsum(
            "grtk,tgrd->kgd", weights, cotangent_table, preferred_element_type=jnp.float32
        ).reshape(key_span, groups * HEAD_SIZE)
        term_key = lax.dynamic_update_slice_in_dim(term_key, key_part, anchor, 0)
        term_value = lax.dynamic_update_slice_in_dim(term_value, value_part, anchor, 0)
        return (grad_query, term_key, term_value)

    term_zero = jnp.zeros((total_len, groups * HEAD_SIZE), jnp.float32)
    grad_query, term_key, term_value = lax.fori_loop(
        0,
        blocks,
        lambda number, carried: visit(number, carried, full_step),
        (query_zero, term_zero, term_zero),
    )
    kv_total = lax.psum_scatter(
        jnp.concatenate([term_key, term_value], axis=1), "seq", scatter_dimension=0, tiled=True
    )
    key_gradient_total = kv_total[:, : groups * HEAD_SIZE]
    value_gradient_total = kv_total[:, groups * HEAD_SIZE :]
    attn_out = attention_table.reshape(tokens, groups * heads_per_group * HEAD_SIZE)
    q_grad = (
        (grad_query * logit_scale)
        .reshape(tokens, groups * heads_per_group * HEAD_SIZE)
        .astype(jnp.bfloat16)
    )
    key_gradient = (key_gradient_total * logit_scale).astype(jnp.bfloat16)
    value_gradient = value_gradient_total.astype(jnp.bfloat16)
    return (
        mixer_out,
        attn_out,
        x_grad,
        grad_b,
        grad_c,
        grad_decay,
        q_grad,
        key_gradient,
        value_gradient,
    )


def solution(mesh):
    placed = (
        P(("groups", "seq"), "head"),
        P(("groups", "seq"), None),
        P(("groups", "seq"), None),
        P(("groups", "head"), "seq"),
        P("head"),
        P("groups"),
        P(("groups", "seq"), "head"),
        P(("groups", "seq"), "head"),
        P(("groups", "seq"), "head"),
        P(("groups", "seq"), "head"),
        P(("groups", "seq"), "head"),
    )
    return jax.shard_map(
        on_device,
        mesh=mesh,
        in_specs=placed,
        out_specs=(
            P(("groups", "seq"), "head"),
            P(("groups", "seq"), "head"),
            P(("groups", "seq"), "head"),
            P(("groups", "seq"), None),
            P(("groups", "seq"), None),
            P(("groups", "head"), "seq"),
            P(("groups", "seq"), "head"),
            P(("groups", "seq"), "head"),
            P(("groups", "seq"), "head"),
        ),
        check_vma=False,
    )
```

```python
import math

import jax
import jax.numpy as jnp
from jax import lax
from jax.sharding import PartitionSpec as P

P_SIZE = 128
HEAD_SIZE = 128
TOK_SPAN = 128


precise = lax.Precision.HIGHEST
big_negative = -1e30


def entering_2(part, axis, combine, identity, reverse):
    count = lax.axis_size(axis)
    place = lax.axis_index(axis)
    ahead = count - 1 - place if reverse else place
    early = jax.tree.map(lambda a, e: jnp.zeros_like(a) + jnp.asarray(e, a.dtype), part, identity)
    span = part
    shift = 1
    while shift < count:
        if reverse:
            pairs = [(i, i - shift) for i in range(shift, count)]
        else:
            pairs = [(i, i + shift) for i in range(count - shift)]
        got = lax.ppermute(span, axis, pairs)
        have = ahead >= shift
        got = jax.tree.map(lambda g, e: jnp.where(have, g, jnp.asarray(e, g.dtype)), got, identity)
        early = combine(got, early)
        if 2 * shift < count:
            span = combine(got, span)
        shift *= 2
    return early


def doc_index(positions, lengths):
    ends = jnp.cumsum(lengths)
    return jnp.sum((positions[:, None] >= ends[None, :]).astype(jnp.int32), axis=1)


def cumulate(decay):
    return jnp.cumsum(decay, axis=1)


def local_state(inputs, b_float, cumulated, segment):
    weights = (
        jnp.exp(cumulated[:, -1:] - cumulated)
        * (segment == segment[-1]).astype(inputs.dtype)[None, :]
    )
    return jnp.einsum("hs,sn,shp->hnp", weights, b_float, inputs, precision=precise)


def carry_factor(cumulated, segment, before):
    return jnp.exp(cumulated[:, -1]) * (segment[-1] == before).astype(cumulated.dtype)


def mixer_stretch(inputs, b_float, c_float, decay, gains, segment, before, state_in):
    cumulated = cumulate(decay)
    width = inputs.shape[0]
    steps = jnp.arange(width)
    allowed = (steps[:, None] >= steps[None, :]) & (segment[:, None] == segment[None, :])
    gaps = jnp.where(allowed[None], cumulated[:, :, None] - cumulated[:, None, :], big_negative)
    kernel = jnp.exp(gaps) * jnp.dot(c_float, b_float.T, precision=precise)[None]
    inner = jnp.einsum("hts,shp->thp", kernel, inputs, precision=precise)
    keeps = (segment == before).astype(inputs.dtype)
    entering = jnp.einsum("tn,hnp->thp", c_float, state_in, precision=precise)
    reach = jnp.exp(cumulated).T * keeps[:, None]
    outputs = inner + reach[:, :, None] * entering + gains[None, :, None] * inputs
    factor = carry_factor(cumulated, segment, before)
    state_out = factor[:, None, None] * state_in + local_state(inputs, b_float, cumulated, segment)
    return (outputs, state_out)


def combine_states(earlier, later):
    return (earlier[0] * later[0], later[0][:, None, None] * earlier[1] + later[1])


def mixer_whole(inputs, b_float, c_float, decay, gains, segment):
    width = TOK_SPAN
    count = inputs.shape[0] // width
    heads = inputs.shape[1]
    inp = inputs.reshape(count, width, heads, P_SIZE)
    b_blocks = b_float.reshape(count, width, -1)
    c_blocks = c_float.reshape(count, width, -1)
    dec = decay.reshape(heads, count, width).transpose(1, 0, 2)
    seg = segment.reshape(count, width)
    befores = jnp.concatenate([jnp.full((1,), -1, seg.dtype), seg[:-1, -1]])
    cumulated = jnp.cumsum(dec, axis=2)
    factor = jax.vmap(carry_factor)(cumulated, seg, befores)
    summary = jax.vmap(local_state)(inp, b_blocks, cumulated, seg)

    def advance(carried, pieces):
        fac, summ = pieces
        return (fac[:, None, None] * carried + summ, carried)

    unused, state_in = lax.scan(advance, jnp.zeros_like(summary[0]), (factor, summary))

    def stretch(i, brow, crow, d, sg, bf, st):
        return mixer_stretch(i, brow, crow, d, gains, sg, bf, st)[0]

    outputs = jax.vmap(stretch)(inp, b_blocks, c_blocks, dec, seg, befores, state_in)
    return outputs.reshape(count * width, heads, P_SIZE)


def mamba_by_heads(x_input, b_all, c_all, decay_log, skip_gain, doc_lengths, mixer_cot):
    seq_count = lax.axis_size("seq")
    place = lax.axis_index("seq")
    tokens = x_input.shape[0]
    heads_here = skip_gain.shape[0]
    own = heads_here // seq_count
    total = tokens * seq_count
    pair = lax.all_to_all(
        jnp.stack([x_input, mixer_cot]), "seq", split_axis=2, concat_axis=1, tiled=True
    )
    decay = lax.all_to_all(decay_log, "seq", split_axis=0, concat_axis=1, tiled=True)
    gains = lax.dynamic_slice_in_dim(skip_gain, place * own, own)
    segment = doc_index(jnp.arange(total, dtype=jnp.int32), doc_lengths)
    inputs = pair[0].astype(jnp.float32).reshape(total, own, P_SIZE)
    cot = pair[1].astype(jnp.float32).reshape(total, own, P_SIZE)

    def whole_of(i, brow, crow, d):
        return mixer_whole(i, brow, crow, d, gains, segment)

    mixed, pull = jax.vjp(
        whole_of, inputs, b_all.astype(jnp.float32), c_all.astype(jnp.float32), decay
    )
    grad_x, grad_b, grad_c, grad_decay = pull(cot)
    back = jnp.stack(
        [
            mixed.reshape(total, own * P_SIZE).astype(jnp.bfloat16),
            grad_x.reshape(total, own * P_SIZE).astype(jnp.bfloat16),
        ]
    )
    back = lax.all_to_all(back, "seq", split_axis=1, concat_axis=2, tiled=True)
    grad_decay = lax.all_to_all(grad_decay, "seq", split_axis=1, concat_axis=0, tiled=True)
    return back[0], back[1], jnp.concatenate([grad_b, grad_c], axis=1), grad_decay


def mamba_by_stretch(
    x_input, b_rows, c_rows, decay_log, skip_gain, doc_lengths, mixer_cot, segment, offset
):
    tokens = x_input.shape[0]
    previous = doc_index(jnp.reshape(offset - 1, (1,)), doc_lengths)[0]
    before = jnp.where(offset > 0, previous, -1)
    heads_here = skip_gain.shape[0]
    inputs = x_input.astype(jnp.float32).reshape(tokens, heads_here, P_SIZE)
    b_float = b_rows.astype(jnp.float32)
    c_float = c_rows.astype(jnp.float32)
    cot_float = mixer_cot.astype(jnp.float32).reshape(tokens, heads_here, P_SIZE)

    def stretch_of(inp, brow, crow, decay, state_in):
        return mixer_stretch(inp, brow, crow, decay, skip_gain, segment, before, state_in)

    cumulated = cumulate(decay_log)
    factor = carry_factor(cumulated, segment, before)
    summary = local_state(inputs, b_float, cumulated, segment)
    zero_state = jnp.zeros_like(summary)
    identity = (jnp.ones_like(factor), zero_state)
    state_in = entering_2((factor, summary), "seq", combine_states, identity, False)[1]
    (mixed, state_out), pull = jax.vjp(stretch_of, inputs, b_float, c_float, decay_log, state_in)
    adjoint_local = pull((cot_float, zero_state))[4]
    adjoint_out = entering_2((factor, adjoint_local), "seq", combine_states, identity, True)[1]
    grad_x, grad_b, grad_c, grad_decay, unused = pull((cot_float, adjoint_out))
    head_count = lax.axis_size("head")
    if head_count == 2:
        other_b, other_c = lax.ppermute((grad_b, grad_c), "head", [(0, 1), (1, 0)])
        grad_b, grad_c = grad_b + other_b, grad_c + other_c
    else:
        grad_b, grad_c = lax.psum((grad_b, grad_c), "head")
    mixer_out = mixed.reshape(tokens, heads_here * P_SIZE).astype(jnp.bfloat16)
    x_grad = grad_x.reshape(tokens, heads_here * P_SIZE).astype(jnp.bfloat16)
    return (mixer_out, x_grad, grad_b, grad_c, grad_decay)


def on_device(
    x_input,
    b_rows,
    c_rows,
    decay_log,
    skip_gain,
    doc_lengths,
    queries,
    attention_key_rows,
    values,
    mixer_cot,
    attention_output_cotangent,
):
    tokens = x_input.shape[0]
    offset = lax.axis_index("seq") * tokens
    total_len = tokens * lax.axis_size("seq")
    positions = offset + jnp.arange(tokens, dtype=jnp.int32)
    segment = doc_index(positions, doc_lengths)
    heads_here = skip_gain.shape[0]
    by_heads = heads_here % lax.axis_size("seq") == 0
    key_width = attention_key_rows.shape[1]
    state_width = b_rows.shape[1]
    pieces = [attention_key_rows, values] + ([b_rows, c_rows] if by_heads else [])
    gathered = lax.all_gather(jnp.concatenate(pieces, axis=1), "seq", axis=0, tiled=True)
    key_all, value_all = gathered[:, :key_width], gathered[:, key_width : 2 * key_width]
    if by_heads:
        b_all = gathered[:, 2 * key_width : 2 * key_width + state_width]
        c_all = gathered[:, 2 * key_width + state_width :]
        mixer_out, x_grad, bc_part, grad_decay = mamba_by_heads(
            x_input, b_all, c_all, decay_log, skip_gain, doc_lengths, mixer_cot
        )
    else:
        mixer_out, x_grad, grad_b, grad_c, grad_decay = mamba_by_stretch(
            x_input, b_rows, c_rows, decay_log, skip_gain, doc_lengths, mixer_cot, segment, offset
        )
    logit_scale = 1.0 / math.sqrt(HEAD_SIZE)
    groups = attention_key_rows.shape[1] // HEAD_SIZE
    heads_per_group = queries.shape[1] // HEAD_SIZE // groups
    key_span = min(512, total_len)
    blocks = total_len // key_span
    last_pos = offset + tokens - 1
    query_grid = queries.reshape(tokens, groups, heads_per_group, HEAD_SIZE)
    cotangent_table = attention_output_cotangent.reshape(tokens, groups, heads_per_group, HEAD_SIZE)

    def block_view(number):
        anchor = number * key_span
        key_blk = lax.dynamic_slice_in_dim(key_all, anchor, key_span, 0).reshape(
            key_span, groups, HEAD_SIZE
        )
        value_blk = lax.dynamic_slice_in_dim(value_all, anchor, key_span, 0).reshape(
            key_span, groups, HEAD_SIZE
        )
        key_pos = anchor + jnp.arange(key_span, dtype=jnp.int32)
        allowed = (key_pos[None, :] <= positions[:, None]) & (
            doc_index(key_pos, doc_lengths)[None, :] == segment[:, None]
        )
        scores = (
            jnp.einsum("tgrd,kgd->grtk", query_grid, key_blk, preferred_element_type=jnp.float32)
            * logit_scale
        )
        scores = jnp.where(allowed[None, None], scores, big_negative)
        return (anchor, key_blk, value_blk, allowed, scores)

    def visit(number, carried, work):
        return lax.cond(
            number * key_span <= last_pos,
            lambda inner: work(number, inner),
            lambda inner: inner,
            carried,
        )

    def stats_step(number, carried):
        row_peak, row_total = carried
        anchor, key_blk, value_blk, allowed, scores = block_view(number)
        new_peak = jnp.maximum(row_peak, jnp.max(scores, axis=-1))
        fresh = jnp.sum(
            jnp.where(allowed[None, None], jnp.exp(scores - new_peak[..., None]), 0.0), axis=-1
        )
        return (new_peak, row_total * jnp.exp(row_peak - new_peak) + fresh)

    stat_shape = (groups, heads_per_group, tokens)
    row_peak, row_total = lax.fori_loop(
        0,
        blocks,
        lambda number, carried: visit(number, carried, stats_step),
        (jnp.full(stat_shape, big_negative, jnp.float32), jnp.zeros(stat_shape, jnp.float32)),
    )
    log_norm = row_peak + jnp.log(row_total)

    def output_step(number, totals):
        anchor, key_blk, value_blk, allowed, scores = block_view(number)
        weights = jnp.where(allowed[None, None], jnp.exp(scores - log_norm[..., None]), 0.0).astype(
            jnp.bfloat16
        )
        return totals + jnp.einsum(
            "grtk,kgd->tgrd", weights, value_blk, preferred_element_type=jnp.float32
        )

    attention_table = lax.fori_loop(
        0,
        blocks,
        lambda number, carried: visit(number, carried, output_step),
        jnp.zeros((tokens, groups, heads_per_group, HEAD_SIZE), jnp.float32),
    ).astype(jnp.bfloat16)
    row_products = jnp.einsum(
        "bkfh,bkfh->kfb", cotangent_table, attention_table, preferred_element_type=jnp.float32
    )

    def grad_terms(allowed, scores, value_blk):
        probs_full = jnp.where(allowed[None, None], jnp.exp(scores - log_norm[..., None]), 0.0)
        grad_prob = jnp.einsum(
            "tgrd,kgd->grtk", cotangent_table, value_blk, preferred_element_type=jnp.float32
        )
        grad_score = (probs_full * (grad_prob - row_products[..., None])).astype(jnp.bfloat16)
        return (probs_full.astype(jnp.bfloat16), grad_score)

    query_zero = jnp.zeros((tokens, groups, heads_per_group, HEAD_SIZE), jnp.float32)

    def full_step(number, carried):
        grad_query, term_key, term_value = carried
        anchor, key_blk, value_blk, allowed, scores = block_view(number)
        weights, grad_score = grad_terms(allowed, scores, value_blk)
        grad_query = grad_query + jnp.einsum(
            "grtk,kgd->tgrd", grad_score, key_blk, preferred_element_type=jnp.float32
        )
        key_part = jnp.einsum(
            "grtk,tgrd->kgd", grad_score, query_grid, preferred_element_type=jnp.float32
        ).reshape(key_span, groups * HEAD_SIZE)
        value_part = jnp.einsum(
            "grtk,tgrd->kgd", weights, cotangent_table, preferred_element_type=jnp.float32
        ).reshape(key_span, groups * HEAD_SIZE)
        term_key = lax.dynamic_update_slice_in_dim(term_key, key_part, anchor, 0)
        term_value = lax.dynamic_update_slice_in_dim(term_value, value_part, anchor, 0)
        return (grad_query, term_key, term_value)

    term_zero = jnp.zeros((total_len, groups * HEAD_SIZE), jnp.float32)
    grad_query, term_key, term_value = lax.fori_loop(
        0,
        blocks,
        lambda number, carried: visit(number, carried, full_step),
        (query_zero, term_zero, term_zero),
    )
    sums = [term_key, term_value] + ([bc_part] if by_heads else [])
    kv_total = lax.psum_scatter(
        jnp.concatenate(sums, axis=1), "seq", scatter_dimension=0, tiled=True
    )
    key_gradient_total = kv_total[:, : groups * HEAD_SIZE]
    value_gradient_total = kv_total[:, groups * HEAD_SIZE : 2 * groups * HEAD_SIZE]
    if by_heads:
        bc_sum = kv_total[:, 2 * groups * HEAD_SIZE :]
        if lax.axis_size("head") == 2:
            bc_sum = bc_sum + lax.ppermute(bc_sum, "head", [(0, 1), (1, 0)])
        else:
            bc_sum = lax.psum(bc_sum, "head")
        grad_b, grad_c = bc_sum[:, :state_width], bc_sum[:, state_width:]
    attn_out = attention_table.reshape(tokens, groups * heads_per_group * HEAD_SIZE)
    q_grad = (
        (grad_query * logit_scale)
        .reshape(tokens, groups * heads_per_group * HEAD_SIZE)
        .astype(jnp.bfloat16)
    )
    key_gradient = (key_gradient_total * logit_scale).astype(jnp.bfloat16)
    value_gradient = value_gradient_total.astype(jnp.bfloat16)
    return (
        mixer_out,
        attn_out,
        x_grad,
        grad_b,
        grad_c,
        grad_decay,
        q_grad,
        key_gradient,
        value_gradient,
    )


def solution(mesh):
    placed = (
        P(("groups", "seq"), "head"),
        P(("groups", "seq"), None),
        P(("groups", "seq"), None),
        P(("groups", "head"), "seq"),
        P("head"),
        P("groups"),
        P(("groups", "seq"), "head"),
        P(("groups", "seq"), "head"),
        P(("groups", "seq"), "head"),
        P(("groups", "seq"), "head"),
        P(("groups", "seq"), "head"),
    )
    return jax.shard_map(
        on_device,
        mesh=mesh,
        in_specs=placed,
        out_specs=(
            P(("groups", "seq"), "head"),
            P(("groups", "seq"), "head"),
            P(("groups", "seq"), "head"),
            P(("groups", "seq"), None),
            P(("groups", "seq"), None),
            P(("groups", "head"), "seq"),
            P(("groups", "seq"), "head"),
            P(("groups", "seq"), "head"),
            P(("groups", "seq"), "head"),
        ),
        check_vma=False,
    )
```

```python
import math

import jax
import jax.numpy as jnp
from jax import lax
from jax.sharding import PartitionSpec as P

P_SIZE = 128
HEAD_SIZE = 128
TOK_SPAN = 128


precise = lax.Precision.HIGHEST
big_negative = -1e30


def entering_2(part, axis, combine, identity, reverse):
    count = lax.axis_size(axis)
    place = lax.axis_index(axis)
    ahead = count - 1 - place if reverse else place
    early = jax.tree.map(lambda a, e: jnp.zeros_like(a) + jnp.asarray(e, a.dtype), part, identity)
    span = part
    shift = 1
    while shift < count:
        if reverse:
            pairs = [(i, i - shift) for i in range(shift, count)]
        else:
            pairs = [(i, i + shift) for i in range(count - shift)]
        got = lax.ppermute(span, axis, pairs)
        have = ahead >= shift
        got = jax.tree.map(lambda g, e: jnp.where(have, g, jnp.asarray(e, g.dtype)), got, identity)
        early = combine(got, early)
        if 2 * shift < count:
            span = combine(got, span)
        shift *= 2
    return early


def doc_index(positions, lengths):
    ends = jnp.cumsum(lengths)
    return jnp.sum((positions[:, None] >= ends[None, :]).astype(jnp.int32), axis=1)


def cumulate(decay):
    return jnp.cumsum(decay, axis=1)


def local_state(inputs, b_float, cumulated, segment):
    weights = (
        jnp.exp(cumulated[:, -1:] - cumulated)
        * (segment == segment[-1]).astype(inputs.dtype)[None, :]
    )
    return jnp.einsum("hs,sn,shp->hnp", weights, b_float, inputs, precision=precise)


def carry_factor(cumulated, segment, before):
    return jnp.exp(cumulated[:, -1]) * (segment[-1] == before).astype(cumulated.dtype)


def mixer_stretch(inputs, b_float, c_float, decay, gains, segment, before, state_in):
    cumulated = cumulate(decay)
    width = inputs.shape[0]
    steps = jnp.arange(width)
    allowed = (steps[:, None] >= steps[None, :]) & (segment[:, None] == segment[None, :])
    gaps = jnp.where(allowed[None], cumulated[:, :, None] - cumulated[:, None, :], big_negative)
    kernel = jnp.exp(gaps) * jnp.dot(c_float, b_float.T, precision=precise)[None]
    inner = jnp.einsum("hts,shp->thp", kernel, inputs, precision=precise)
    keeps = (segment == before).astype(inputs.dtype)
    entering = jnp.einsum("tn,hnp->thp", c_float, state_in, precision=precise)
    reach = jnp.exp(cumulated).T * keeps[:, None]
    outputs = inner + reach[:, :, None] * entering + gains[None, :, None] * inputs
    factor = carry_factor(cumulated, segment, before)
    state_out = factor[:, None, None] * state_in + local_state(inputs, b_float, cumulated, segment)
    return (outputs, state_out)


def combine_states(earlier, later):
    return (earlier[0] * later[0], later[0][:, None, None] * earlier[1] + later[1])


def mixer_whole(inputs, b_float, c_float, decay, gains, segment):
    width = TOK_SPAN
    count = inputs.shape[0] // width
    heads = inputs.shape[1]
    inp = inputs.reshape(count, width, heads, P_SIZE)
    b_blocks = b_float.reshape(count, width, -1)
    c_blocks = c_float.reshape(count, width, -1)
    dec = decay.reshape(heads, count, width).transpose(1, 0, 2)
    seg = segment.reshape(count, width)
    befores = jnp.concatenate([jnp.full((1,), -1, seg.dtype), seg[:-1, -1]])
    cumulated = jnp.cumsum(dec, axis=2)
    factor = jax.vmap(carry_factor)(cumulated, seg, befores)
    summary = jax.vmap(local_state)(inp, b_blocks, cumulated, seg)

    columns = jnp.arange(count)[:, None]
    row = jnp.zeros((count, heads), factor.dtype)
    rows = [row]
    for k in range(1, count):
        row = jnp.where(columns < k - 1, row * factor[k - 1][None, :], (columns == k - 1).astype(factor.dtype))
        rows.append(row)
    reach = jnp.stack(rows)
    state_in = jnp.einsum("kjh,jhnp->khnp", reach, summary, precision=precise)

    def stretch(i, brow, crow, d, sg, bf, st):
        return mixer_stretch(i, brow, crow, d, gains, sg, bf, st)[0]

    outputs = jax.vmap(stretch)(inp, b_blocks, c_blocks, dec, seg, befores, state_in)
    return outputs.reshape(count * width, heads, P_SIZE)


def mamba_by_heads(x_input, b_all, c_all, decay_log, skip_gain, doc_lengths, mixer_cot):
    seq_count = lax.axis_size("seq")
    place = lax.axis_index("seq")
    tokens = x_input.shape[0]
    heads_here = skip_gain.shape[0]
    own = heads_here // seq_count
    total = tokens * seq_count
    pair = lax.all_to_all(
        jnp.stack([x_input, mixer_cot]), "seq", split_axis=2, concat_axis=1, tiled=True
    )
    decay = lax.all_to_all(decay_log, "seq", split_axis=0, concat_axis=1, tiled=True)
    gains = lax.dynamic_slice_in_dim(skip_gain, place * own, own)
    segment = doc_index(jnp.arange(total, dtype=jnp.int32), doc_lengths)
    inputs = pair[0].astype(jnp.float32).reshape(total, own, P_SIZE)
    cot = pair[1].astype(jnp.float32).reshape(total, own, P_SIZE)

    def whole_of(i, brow, crow, d):
        return mixer_whole(i, brow, crow, d, gains, segment)

    mixed, pull = jax.vjp(
        whole_of, inputs, b_all.astype(jnp.float32), c_all.astype(jnp.float32), decay
    )
    grad_x, grad_b, grad_c, grad_decay = pull(cot)
    back = jnp.stack(
        [
            mixed.reshape(total, own * P_SIZE).astype(jnp.bfloat16),
            grad_x.reshape(total, own * P_SIZE).astype(jnp.bfloat16),
        ]
    )
    back = lax.all_to_all(back, "seq", split_axis=1, concat_axis=2, tiled=True)
    grad_decay = lax.all_to_all(grad_decay, "seq", split_axis=1, concat_axis=0, tiled=True)
    return back[0], back[1], jnp.concatenate([grad_b, grad_c], axis=1), grad_decay


def mamba_by_stretch(
    x_input, b_rows, c_rows, decay_log, skip_gain, doc_lengths, mixer_cot, segment, offset
):
    tokens = x_input.shape[0]
    previous = doc_index(jnp.reshape(offset - 1, (1,)), doc_lengths)[0]
    before = jnp.where(offset > 0, previous, -1)
    heads_here = skip_gain.shape[0]
    inputs = x_input.astype(jnp.float32).reshape(tokens, heads_here, P_SIZE)
    b_float = b_rows.astype(jnp.float32)
    c_float = c_rows.astype(jnp.float32)
    cot_float = mixer_cot.astype(jnp.float32).reshape(tokens, heads_here, P_SIZE)

    def stretch_of(inp, brow, crow, decay, state_in):
        return mixer_stretch(inp, brow, crow, decay, skip_gain, segment, before, state_in)

    cumulated = cumulate(decay_log)
    factor = carry_factor(cumulated, segment, before)
    summary = local_state(inputs, b_float, cumulated, segment)
    zero_state = jnp.zeros_like(summary)
    identity = (jnp.ones_like(factor), zero_state)
    state_in = entering_2((factor, summary), "seq", combine_states, identity, False)[1]
    (mixed, state_out), pull = jax.vjp(stretch_of, inputs, b_float, c_float, decay_log, state_in)
    adjoint_local = pull((cot_float, zero_state))[4]
    adjoint_out = entering_2((factor, adjoint_local), "seq", combine_states, identity, True)[1]
    grad_x, grad_b, grad_c, grad_decay, unused = pull((cot_float, adjoint_out))
    head_count = lax.axis_size("head")
    if head_count == 2:
        other_b, other_c = lax.ppermute((grad_b, grad_c), "head", [(0, 1), (1, 0)])
        grad_b, grad_c = grad_b + other_b, grad_c + other_c
    else:
        grad_b, grad_c = lax.psum((grad_b, grad_c), "head")
    mixer_out = mixed.reshape(tokens, heads_here * P_SIZE).astype(jnp.bfloat16)
    x_grad = grad_x.reshape(tokens, heads_here * P_SIZE).astype(jnp.bfloat16)
    return (mixer_out, x_grad, grad_b, grad_c, grad_decay)


def on_device(
    x_input,
    b_rows,
    c_rows,
    decay_log,
    skip_gain,
    doc_lengths,
    queries,
    attention_key_rows,
    values,
    mixer_cot,
    attention_output_cotangent,
):
    tokens = x_input.shape[0]
    offset = lax.axis_index("seq") * tokens
    total_len = tokens * lax.axis_size("seq")
    positions = offset + jnp.arange(tokens, dtype=jnp.int32)
    segment = doc_index(positions, doc_lengths)
    heads_here = skip_gain.shape[0]
    by_heads = heads_here % lax.axis_size("seq") == 0
    key_width = attention_key_rows.shape[1]
    state_width = b_rows.shape[1]
    pieces = [attention_key_rows, values] + ([b_rows, c_rows] if by_heads else [])
    gathered = lax.all_gather(jnp.concatenate(pieces, axis=1), "seq", axis=0, tiled=True)
    key_all, value_all = gathered[:, :key_width], gathered[:, key_width : 2 * key_width]
    if by_heads:
        b_all = gathered[:, 2 * key_width : 2 * key_width + state_width]
        c_all = gathered[:, 2 * key_width + state_width :]
        mixer_out, x_grad, bc_part, grad_decay = mamba_by_heads(
            x_input, b_all, c_all, decay_log, skip_gain, doc_lengths, mixer_cot
        )
    else:
        mixer_out, x_grad, grad_b, grad_c, grad_decay = mamba_by_stretch(
            x_input, b_rows, c_rows, decay_log, skip_gain, doc_lengths, mixer_cot, segment, offset
        )
    logit_scale = 1.0 / math.sqrt(HEAD_SIZE)
    groups = attention_key_rows.shape[1] // HEAD_SIZE
    heads_per_group = queries.shape[1] // HEAD_SIZE // groups
    key_span = min(512, total_len)
    blocks = total_len // key_span
    last_pos = offset + tokens - 1
    query_grid = queries.reshape(tokens, groups, heads_per_group, HEAD_SIZE)
    cotangent_table = attention_output_cotangent.reshape(tokens, groups, heads_per_group, HEAD_SIZE)

    def block_view(number):
        anchor = number * key_span
        key_blk = lax.dynamic_slice_in_dim(key_all, anchor, key_span, 0).reshape(
            key_span, groups, HEAD_SIZE
        )
        value_blk = lax.dynamic_slice_in_dim(value_all, anchor, key_span, 0).reshape(
            key_span, groups, HEAD_SIZE
        )
        key_pos = anchor + jnp.arange(key_span, dtype=jnp.int32)
        allowed = (key_pos[None, :] <= positions[:, None]) & (
            doc_index(key_pos, doc_lengths)[None, :] == segment[:, None]
        )
        scores = (
            jnp.einsum("tgrd,kgd->grtk", query_grid, key_blk, preferred_element_type=jnp.float32)
            * logit_scale
        )
        scores = jnp.where(allowed[None, None], scores, big_negative)
        return (anchor, key_blk, value_blk, allowed, scores)

    def visit(number, carried, work):
        return lax.cond(
            number * key_span <= last_pos,
            lambda inner: work(number, inner),
            lambda inner: inner,
            carried,
        )

    def stats_step(number, carried):
        row_peak, row_total = carried
        anchor, key_blk, value_blk, allowed, scores = block_view(number)
        new_peak = jnp.maximum(row_peak, jnp.max(scores, axis=-1))
        fresh = jnp.sum(
            jnp.where(allowed[None, None], jnp.exp(scores - new_peak[..., None]), 0.0), axis=-1
        )
        return (new_peak, row_total * jnp.exp(row_peak - new_peak) + fresh)

    stat_shape = (groups, heads_per_group, tokens)
    row_peak, row_total = lax.fori_loop(
        0,
        blocks,
        lambda number, carried: visit(number, carried, stats_step),
        (jnp.full(stat_shape, big_negative, jnp.float32), jnp.zeros(stat_shape, jnp.float32)),
    )
    log_norm = row_peak + jnp.log(row_total)

    def output_step(number, totals):
        anchor, key_blk, value_blk, allowed, scores = block_view(number)
        weights = jnp.where(allowed[None, None], jnp.exp(scores - log_norm[..., None]), 0.0).astype(
            jnp.bfloat16
        )
        return totals + jnp.einsum(
            "grtk,kgd->tgrd", weights, value_blk, preferred_element_type=jnp.float32
        )

    attention_table = lax.fori_loop(
        0,
        blocks,
        lambda number, carried: visit(number, carried, output_step),
        jnp.zeros((tokens, groups, heads_per_group, HEAD_SIZE), jnp.float32),
    ).astype(jnp.bfloat16)
    row_products = jnp.einsum(
        "bkfh,bkfh->kfb", cotangent_table, attention_table, preferred_element_type=jnp.float32
    )

    def grad_terms(allowed, scores, value_blk):
        probs_full = jnp.where(allowed[None, None], jnp.exp(scores - log_norm[..., None]), 0.0)
        grad_prob = jnp.einsum(
            "tgrd,kgd->grtk", cotangent_table, value_blk, preferred_element_type=jnp.float32
        )
        grad_score = (probs_full * (grad_prob - row_products[..., None])).astype(jnp.bfloat16)
        return (probs_full.astype(jnp.bfloat16), grad_score)

    query_zero = jnp.zeros((tokens, groups, heads_per_group, HEAD_SIZE), jnp.float32)

    def full_step(number, carried):
        grad_query, term_key, term_value = carried
        anchor, key_blk, value_blk, allowed, scores = block_view(number)
        weights, grad_score = grad_terms(allowed, scores, value_blk)
        grad_query = grad_query + jnp.einsum(
            "grtk,kgd->tgrd", grad_score, key_blk, preferred_element_type=jnp.float32
        )
        key_part = jnp.einsum(
            "grtk,tgrd->kgd", grad_score, query_grid, preferred_element_type=jnp.float32
        ).reshape(key_span, groups * HEAD_SIZE)
        value_part = jnp.einsum(
            "grtk,tgrd->kgd", weights, cotangent_table, preferred_element_type=jnp.float32
        ).reshape(key_span, groups * HEAD_SIZE)
        term_key = lax.dynamic_update_slice_in_dim(term_key, key_part, anchor, 0)
        term_value = lax.dynamic_update_slice_in_dim(term_value, value_part, anchor, 0)
        return (grad_query, term_key, term_value)

    term_zero = jnp.zeros((total_len, groups * HEAD_SIZE), jnp.float32)
    grad_query, term_key, term_value = lax.fori_loop(
        0,
        blocks,
        lambda number, carried: visit(number, carried, full_step),
        (query_zero, term_zero, term_zero),
    )
    kv_total = lax.psum_scatter(
        jnp.concatenate([term_key, term_value], axis=1), "seq", scatter_dimension=0, tiled=True
    )
    key_gradient_total = kv_total[:, : groups * HEAD_SIZE]
    value_gradient_total = kv_total[:, groups * HEAD_SIZE :]
    if by_heads:
        bc_sum = lax.psum_scatter(bc_part, "seq", scatter_dimension=0, tiled=True)
        if lax.axis_size("head") == 2:
            bc_sum = bc_sum + lax.ppermute(bc_sum, "head", [(0, 1), (1, 0)])
        else:
            bc_sum = lax.psum(bc_sum, "head")
        grad_b, grad_c = bc_sum[:, :state_width], bc_sum[:, state_width:]
    attn_out = attention_table.reshape(tokens, groups * heads_per_group * HEAD_SIZE)
    q_grad = (
        (grad_query * logit_scale)
        .reshape(tokens, groups * heads_per_group * HEAD_SIZE)
        .astype(jnp.bfloat16)
    )
    key_gradient = (key_gradient_total * logit_scale).astype(jnp.bfloat16)
    value_gradient = value_gradient_total.astype(jnp.bfloat16)
    return (
        mixer_out,
        attn_out,
        x_grad,
        grad_b,
        grad_c,
        grad_decay,
        q_grad,
        key_gradient,
        value_gradient,
    )


def solution(mesh):
    placed = (
        P(("groups", "seq"), "head"),
        P(("groups", "seq"), None),
        P(("groups", "seq"), None),
        P(("groups", "head"), "seq"),
        P("head"),
        P("groups"),
        P(("groups", "seq"), "head"),
        P(("groups", "seq"), "head"),
        P(("groups", "seq"), "head"),
        P(("groups", "seq"), "head"),
        P(("groups", "seq"), "head"),
    )
    return jax.shard_map(
        on_device,
        mesh=mesh,
        in_specs=placed,
        out_specs=(
            P(("groups", "seq"), "head"),
            P(("groups", "seq"), "head"),
            P(("groups", "seq"), "head"),
            P(("groups", "seq"), None),
            P(("groups", "seq"), None),
            P(("groups", "head"), "seq"),
            P(("groups", "seq"), "head"),
            P(("groups", "seq"), "head"),
            P(("groups", "seq"), "head"),
        ),
        check_vma=False,
    )
```

```python
import math

import jax
import jax.numpy as jnp
from jax import lax
from jax.sharding import PartitionSpec as P

P_SIZE = 128
HEAD_SIZE = 128
TOK_SPAN = 128


precise = lax.Precision.HIGHEST
big_negative = -1e30


def entering_2(part, axis, combine, identity, reverse):
    count = lax.axis_size(axis)
    place = lax.axis_index(axis)
    ahead = count - 1 - place if reverse else place
    early = jax.tree.map(lambda a, e: jnp.zeros_like(a) + jnp.asarray(e, a.dtype), part, identity)
    span = part
    shift = 1
    while shift < count:
        if reverse:
            pairs = [(i, i - shift) for i in range(shift, count)]
        else:
            pairs = [(i, i + shift) for i in range(count - shift)]
        got = lax.ppermute(span, axis, pairs)
        have = ahead >= shift
        got = jax.tree.map(lambda g, e: jnp.where(have, g, jnp.asarray(e, g.dtype)), got, identity)
        early = combine(got, early)
        if 2 * shift < count:
            span = combine(got, span)
        shift *= 2
    return early


def doc_index(positions, lengths):
    ends = jnp.cumsum(lengths)
    return jnp.sum((positions[:, None] >= ends[None, :]).astype(jnp.int32), axis=1)


def cumulate(decay):
    return jnp.cumsum(decay, axis=1)


def local_state(inputs, b_float, cumulated, segment):
    weights = (
        jnp.exp(cumulated[:, -1:] - cumulated)
        * (segment == segment[-1]).astype(inputs.dtype)[None, :]
    )
    return jnp.einsum("hs,sn,shp->hnp", weights, b_float, inputs, precision=precise)


def carry_factor(cumulated, segment, before):
    return jnp.exp(cumulated[:, -1]) * (segment[-1] == before).astype(cumulated.dtype)


def mixer_stretch(inputs, b_float, c_float, decay, gains, segment, before, state_in):
    cumulated = cumulate(decay)
    width = inputs.shape[0]
    steps = jnp.arange(width)
    allowed = (steps[:, None] >= steps[None, :]) & (segment[:, None] == segment[None, :])
    gaps = jnp.where(allowed[None], cumulated[:, :, None] - cumulated[:, None, :], big_negative)
    kernel = jnp.exp(gaps) * jnp.dot(c_float, b_float.T, precision=precise)[None]
    inner = jnp.einsum("hts,shp->thp", kernel, inputs, precision=precise)
    keeps = (segment == before).astype(inputs.dtype)
    entering = jnp.einsum("tn,hnp->thp", c_float, state_in, precision=precise)
    reach = jnp.exp(cumulated).T * keeps[:, None]
    outputs = inner + reach[:, :, None] * entering + gains[None, :, None] * inputs
    factor = carry_factor(cumulated, segment, before)
    state_out = factor[:, None, None] * state_in + local_state(inputs, b_float, cumulated, segment)
    return (outputs, state_out)


def combine_states(earlier, later):
    return (earlier[0] * later[0], later[0][:, None, None] * earlier[1] + later[1])


def mixer_whole(inputs, b_float, c_float, decay, gains, segment):
    width = TOK_SPAN
    count = inputs.shape[0] // width
    heads = inputs.shape[1]
    inp = inputs.reshape(count, width, heads, P_SIZE)
    b_blocks = b_float.reshape(count, width, -1)
    c_blocks = c_float.reshape(count, width, -1)
    dec = decay.reshape(heads, count, width).transpose(1, 0, 2)
    seg = segment.reshape(count, width)
    befores = jnp.concatenate([jnp.full((1,), -1, seg.dtype), seg[:-1, -1]])
    cumulated = jnp.cumsum(dec, axis=2)
    factor = jax.vmap(carry_factor)(cumulated, seg, befores)
    summary = jax.vmap(local_state)(inp, b_blocks, cumulated, seg)

    columns = jnp.arange(count)[:, None]
    row = jnp.zeros((count, heads), factor.dtype)
    rows = [row]
    for k in range(1, count):
        row = jnp.where(columns < k - 1, row * factor[k - 1][None, :], (columns == k - 1).astype(factor.dtype))
        rows.append(row)
    reach = jnp.stack(rows)
    state_in = jnp.einsum("kjh,jhnp->khnp", reach, summary, precision=precise)

    def stretch(i, brow, crow, d, sg, bf, st):
        return mixer_stretch(i, brow, crow, d, gains, sg, bf, st)[0]

    outputs = jax.vmap(stretch)(inp, b_blocks, c_blocks, dec, seg, befores, state_in)
    return outputs.reshape(count * width, heads, P_SIZE)


def mamba_by_heads(x_input, b_all, c_all, decay_log, skip_gain, doc_lengths, mixer_cot):
    seq_count = lax.axis_size("seq")
    place = lax.axis_index("seq")
    tokens = x_input.shape[0]
    heads_here = skip_gain.shape[0]
    own = heads_here // seq_count
    total = tokens * seq_count
    pair = lax.all_to_all(
        jnp.stack([x_input, mixer_cot]), "seq", split_axis=2, concat_axis=1, tiled=True
    )
    decay = lax.all_to_all(decay_log, "seq", split_axis=0, concat_axis=1, tiled=True)
    gains = lax.dynamic_slice_in_dim(skip_gain, place * own, own)
    segment = doc_index(jnp.arange(total, dtype=jnp.int32), doc_lengths)
    inputs = pair[0].astype(jnp.float32).reshape(total, own, P_SIZE)
    cot = pair[1].astype(jnp.float32).reshape(total, own, P_SIZE)

    def whole_of(i, brow, crow, d):
        return mixer_whole(i, brow, crow, d, gains, segment)

    mixed, pull = jax.vjp(
        whole_of, inputs, b_all.astype(jnp.float32), c_all.astype(jnp.float32), decay
    )
    grad_x, grad_b, grad_c, grad_decay = pull(cot)
    back = jnp.stack(
        [
            mixed.reshape(total, own * P_SIZE).astype(jnp.bfloat16),
            grad_x.reshape(total, own * P_SIZE).astype(jnp.bfloat16),
        ]
    )
    back = lax.all_to_all(back, "seq", split_axis=1, concat_axis=2, tiled=True)
    decay_cols = lax.dynamic_update_slice_in_dim(
        jnp.zeros((total, heads_here), jnp.float32), grad_decay.T, place * own, 1
    )
    return back[0], back[1], jnp.concatenate([grad_b, grad_c, decay_cols], axis=1)


def mamba_by_stretch(
    x_input, b_rows, c_rows, decay_log, skip_gain, doc_lengths, mixer_cot, segment, offset
):
    tokens = x_input.shape[0]
    previous = doc_index(jnp.reshape(offset - 1, (1,)), doc_lengths)[0]
    before = jnp.where(offset > 0, previous, -1)
    heads_here = skip_gain.shape[0]
    inputs = x_input.astype(jnp.float32).reshape(tokens, heads_here, P_SIZE)
    b_float = b_rows.astype(jnp.float32)
    c_float = c_rows.astype(jnp.float32)
    cot_float = mixer_cot.astype(jnp.float32).reshape(tokens, heads_here, P_SIZE)

    def stretch_of(inp, brow, crow, decay, state_in):
        return mixer_stretch(inp, brow, crow, decay, skip_gain, segment, before, state_in)

    cumulated = cumulate(decay_log)
    factor = carry_factor(cumulated, segment, before)
    summary = local_state(inputs, b_float, cumulated, segment)
    zero_state = jnp.zeros_like(summary)
    identity = (jnp.ones_like(factor), zero_state)
    state_in = entering_2((factor, summary), "seq", combine_states, identity, False)[1]
    (mixed, state_out), pull = jax.vjp(stretch_of, inputs, b_float, c_float, decay_log, state_in)
    adjoint_local = pull((cot_float, zero_state))[4]
    adjoint_out = entering_2((factor, adjoint_local), "seq", combine_states, identity, True)[1]
    grad_x, grad_b, grad_c, grad_decay, unused = pull((cot_float, adjoint_out))
    head_count = lax.axis_size("head")
    if head_count == 2:
        other_b, other_c = lax.ppermute((grad_b, grad_c), "head", [(0, 1), (1, 0)])
        grad_b, grad_c = grad_b + other_b, grad_c + other_c
    else:
        grad_b, grad_c = lax.psum((grad_b, grad_c), "head")
    mixer_out = mixed.reshape(tokens, heads_here * P_SIZE).astype(jnp.bfloat16)
    x_grad = grad_x.reshape(tokens, heads_here * P_SIZE).astype(jnp.bfloat16)
    return (mixer_out, x_grad, grad_b, grad_c, grad_decay)


def on_device(
    x_input,
    b_rows,
    c_rows,
    decay_log,
    skip_gain,
    doc_lengths,
    queries,
    attention_key_rows,
    values,
    mixer_cot,
    attention_output_cotangent,
):
    tokens = x_input.shape[0]
    offset = lax.axis_index("seq") * tokens
    total_len = tokens * lax.axis_size("seq")
    positions = offset + jnp.arange(tokens, dtype=jnp.int32)
    segment = doc_index(positions, doc_lengths)
    heads_here = skip_gain.shape[0]
    by_heads = heads_here % lax.axis_size("seq") == 0
    key_width = attention_key_rows.shape[1]
    state_width = b_rows.shape[1]
    pieces = [attention_key_rows, values] + ([b_rows, c_rows] if by_heads else [])
    gathered = lax.all_gather(jnp.concatenate(pieces, axis=1), "seq", axis=0, tiled=True)
    key_all, value_all = gathered[:, :key_width], gathered[:, key_width : 2 * key_width]
    if by_heads:
        b_all = gathered[:, 2 * key_width : 2 * key_width + state_width]
        c_all = gathered[:, 2 * key_width + state_width :]
        mixer_out, x_grad, bc_part = mamba_by_heads(
            x_input, b_all, c_all, decay_log, skip_gain, doc_lengths, mixer_cot
        )
    else:
        mixer_out, x_grad, grad_b, grad_c, grad_decay = mamba_by_stretch(
            x_input, b_rows, c_rows, decay_log, skip_gain, doc_lengths, mixer_cot, segment, offset
        )
    logit_scale = 1.0 / math.sqrt(HEAD_SIZE)
    groups = attention_key_rows.shape[1] // HEAD_SIZE
    heads_per_group = queries.shape[1] // HEAD_SIZE // groups
    key_span = min(512, total_len)
    blocks = total_len // key_span
    last_pos = offset + tokens - 1
    query_grid = queries.reshape(tokens, groups, heads_per_group, HEAD_SIZE)
    cotangent_table = attention_output_cotangent.reshape(tokens, groups, heads_per_group, HEAD_SIZE)

    def block_view(number):
        anchor = number * key_span
        key_blk = lax.dynamic_slice_in_dim(key_all, anchor, key_span, 0).reshape(
            key_span, groups, HEAD_SIZE
        )
        value_blk = lax.dynamic_slice_in_dim(value_all, anchor, key_span, 0).reshape(
            key_span, groups, HEAD_SIZE
        )
        key_pos = anchor + jnp.arange(key_span, dtype=jnp.int32)
        allowed = (key_pos[None, :] <= positions[:, None]) & (
            doc_index(key_pos, doc_lengths)[None, :] == segment[:, None]
        )
        scores = (
            jnp.einsum("tgrd,kgd->grtk", query_grid, key_blk, preferred_element_type=jnp.float32)
            * logit_scale
        )
        scores = jnp.where(allowed[None, None], scores, big_negative)
        return (anchor, key_blk, value_blk, allowed, scores)

    def visit(number, carried, work):
        return lax.cond(
            number * key_span <= last_pos,
            lambda inner: work(number, inner),
            lambda inner: inner,
            carried,
        )

    def stats_step(number, carried):
        row_peak, row_total = carried
        anchor, key_blk, value_blk, allowed, scores = block_view(number)
        new_peak = jnp.maximum(row_peak, jnp.max(scores, axis=-1))
        fresh = jnp.sum(
            jnp.where(allowed[None, None], jnp.exp(scores - new_peak[..., None]), 0.0), axis=-1
        )
        return (new_peak, row_total * jnp.exp(row_peak - new_peak) + fresh)

    stat_shape = (groups, heads_per_group, tokens)
    row_peak, row_total = lax.fori_loop(
        0,
        blocks,
        lambda number, carried: visit(number, carried, stats_step),
        (jnp.full(stat_shape, big_negative, jnp.float32), jnp.zeros(stat_shape, jnp.float32)),
    )
    log_norm = row_peak + jnp.log(row_total)

    def output_step(number, totals):
        anchor, key_blk, value_blk, allowed, scores = block_view(number)
        weights = jnp.where(allowed[None, None], jnp.exp(scores - log_norm[..., None]), 0.0).astype(
            jnp.bfloat16
        )
        return totals + jnp.einsum(
            "grtk,kgd->tgrd", weights, value_blk, preferred_element_type=jnp.float32
        )

    attention_table = lax.fori_loop(
        0,
        blocks,
        lambda number, carried: visit(number, carried, output_step),
        jnp.zeros((tokens, groups, heads_per_group, HEAD_SIZE), jnp.float32),
    ).astype(jnp.bfloat16)
    row_products = jnp.einsum(
        "bkfh,bkfh->kfb", cotangent_table, attention_table, preferred_element_type=jnp.float32
    )

    def grad_terms(allowed, scores, value_blk):
        probs_full = jnp.where(allowed[None, None], jnp.exp(scores - log_norm[..., None]), 0.0)
        grad_prob = jnp.einsum(
            "tgrd,kgd->grtk", cotangent_table, value_blk, preferred_element_type=jnp.float32
        )
        grad_score = (probs_full * (grad_prob - row_products[..., None])).astype(jnp.bfloat16)
        return (probs_full.astype(jnp.bfloat16), grad_score)

    query_zero = jnp.zeros((tokens, groups, heads_per_group, HEAD_SIZE), jnp.float32)

    def full_step(number, carried):
        grad_query, term_key, term_value = carried
        anchor, key_blk, value_blk, allowed, scores = block_view(number)
        weights, grad_score = grad_terms(allowed, scores, value_blk)
        grad_query = grad_query + jnp.einsum(
            "grtk,kgd->tgrd", grad_score, key_blk, preferred_element_type=jnp.float32
        )
        key_part = jnp.einsum(
            "grtk,tgrd->kgd", grad_score, query_grid, preferred_element_type=jnp.float32
        ).reshape(key_span, groups * HEAD_SIZE)
        value_part = jnp.einsum(
            "grtk,tgrd->kgd", weights, cotangent_table, preferred_element_type=jnp.float32
        ).reshape(key_span, groups * HEAD_SIZE)
        term_key = lax.dynamic_update_slice_in_dim(term_key, key_part, anchor, 0)
        term_value = lax.dynamic_update_slice_in_dim(term_value, value_part, anchor, 0)
        return (grad_query, term_key, term_value)

    term_zero = jnp.zeros((total_len, groups * HEAD_SIZE), jnp.float32)
    grad_query, term_key, term_value = lax.fori_loop(
        0,
        blocks,
        lambda number, carried: visit(number, carried, full_step),
        (query_zero, term_zero, term_zero),
    )
    kv_total = lax.psum_scatter(
        jnp.concatenate([term_key, term_value], axis=1), "seq", scatter_dimension=0, tiled=True
    )
    key_gradient_total = kv_total[:, : groups * HEAD_SIZE]
    value_gradient_total = kv_total[:, groups * HEAD_SIZE :]
    if by_heads:
        bc_sum = lax.psum_scatter(bc_part, "seq", scatter_dimension=0, tiled=True)
        grad_decay = bc_sum[:, 2 * state_width :].T
        bc_sum = bc_sum[:, : 2 * state_width]
        if lax.axis_size("head") == 2:
            bc_sum = bc_sum + lax.ppermute(bc_sum, "head", [(0, 1), (1, 0)])
        else:
            bc_sum = lax.psum(bc_sum, "head")
        grad_b, grad_c = bc_sum[:, :state_width], bc_sum[:, state_width:]
    attn_out = attention_table.reshape(tokens, groups * heads_per_group * HEAD_SIZE)
    q_grad = (
        (grad_query * logit_scale)
        .reshape(tokens, groups * heads_per_group * HEAD_SIZE)
        .astype(jnp.bfloat16)
    )
    key_gradient = (key_gradient_total * logit_scale).astype(jnp.bfloat16)
    value_gradient = value_gradient_total.astype(jnp.bfloat16)
    return (
        mixer_out,
        attn_out,
        x_grad,
        grad_b,
        grad_c,
        grad_decay,
        q_grad,
        key_gradient,
        value_gradient,
    )


def solution(mesh):
    placed = (
        P(("groups", "seq"), "head"),
        P(("groups", "seq"), None),
        P(("groups", "seq"), None),
        P(("groups", "head"), "seq"),
        P("head"),
        P("groups"),
        P(("groups", "seq"), "head"),
        P(("groups", "seq"), "head"),
        P(("groups", "seq"), "head"),
        P(("groups", "seq"), "head"),
        P(("groups", "seq"), "head"),
    )
    return jax.shard_map(
        on_device,
        mesh=mesh,
        in_specs=placed,
        out_specs=(
            P(("groups", "seq"), "head"),
            P(("groups", "seq"), "head"),
            P(("groups", "seq"), "head"),
            P(("groups", "seq"), None),
            P(("groups", "seq"), None),
            P(("groups", "head"), "seq"),
            P(("groups", "seq"), "head"),
            P(("groups", "seq"), "head"),
            P(("groups", "seq"), "head"),
        ),
        check_vma=False,
    )
```

```python
import math

import jax
import jax.numpy as jnp
from jax import lax
from jax.sharding import PartitionSpec as P

P_SIZE = 128
HEAD_SIZE = 128
TOK_SPAN = 128


precise = lax.Precision.HIGHEST
big_negative = -1e30


def entering_2(part, axis, combine, identity, reverse):
    count = lax.axis_size(axis)
    place = lax.axis_index(axis)
    ahead = count - 1 - place if reverse else place
    early = jax.tree.map(lambda a, e: jnp.zeros_like(a) + jnp.asarray(e, a.dtype), part, identity)
    span = part
    shift = 1
    while shift < count:
        if reverse:
            pairs = [(i, i - shift) for i in range(shift, count)]
        else:
            pairs = [(i, i + shift) for i in range(count - shift)]
        got = lax.ppermute(span, axis, pairs)
        have = ahead >= shift
        got = jax.tree.map(lambda g, e: jnp.where(have, g, jnp.asarray(e, g.dtype)), got, identity)
        early = combine(got, early)
        if 2 * shift < count:
            span = combine(got, span)
        shift *= 2
    return early


def doc_index(positions, lengths):
    ends = jnp.cumsum(lengths)
    return jnp.sum((positions[:, None] >= ends[None, :]).astype(jnp.int32), axis=1)


def cumulate(decay):
    return jnp.cumsum(decay, axis=1)


def local_state(inputs, b_float, cumulated, segment):
    weights = (
        jnp.exp(cumulated[:, -1:] - cumulated)
        * (segment == segment[-1]).astype(inputs.dtype)[None, :]
    )
    return jnp.einsum("hs,sn,shp->hnp", weights, b_float, inputs, precision=precise)


def carry_factor(cumulated, segment, before):
    return jnp.exp(cumulated[:, -1]) * (segment[-1] == before).astype(cumulated.dtype)


def mixer_stretch(inputs, b_float, c_float, decay, gains, segment, before, state_in):
    cumulated = cumulate(decay)
    width = inputs.shape[0]
    steps = jnp.arange(width)
    allowed = (steps[:, None] >= steps[None, :]) & (segment[:, None] == segment[None, :])
    gaps = jnp.where(allowed[None], cumulated[:, :, None] - cumulated[:, None, :], big_negative)
    kernel = jnp.exp(gaps) * jnp.dot(c_float, b_float.T, precision=precise)[None]
    inner = jnp.einsum("hts,shp->thp", kernel, inputs, precision=precise)
    keeps = (segment == before).astype(inputs.dtype)
    entering = jnp.einsum("tn,hnp->thp", c_float, state_in, precision=precise)
    reach = jnp.exp(cumulated).T * keeps[:, None]
    outputs = inner + reach[:, :, None] * entering + gains[None, :, None] * inputs
    factor = carry_factor(cumulated, segment, before)
    state_out = factor[:, None, None] * state_in + local_state(inputs, b_float, cumulated, segment)
    return (outputs, state_out)


def combine_states(earlier, later):
    return (earlier[0] * later[0], later[0][:, None, None] * earlier[1] + later[1])


def mixer_whole(inputs, b_float, c_float, decay, gains, segment):
    width = TOK_SPAN
    count = inputs.shape[0] // width
    heads = inputs.shape[1]
    inp = inputs.reshape(count, width, heads, P_SIZE)
    b_blocks = b_float.reshape(count, width, -1)
    c_blocks = c_float.reshape(count, width, -1)
    dec = decay.reshape(heads, count, width).transpose(1, 0, 2)
    seg = segment.reshape(count, width)
    befores = jnp.concatenate([jnp.full((1,), -1, seg.dtype), seg[:-1, -1]])
    cumulated = jnp.cumsum(dec, axis=2)
    factor = jax.vmap(carry_factor)(cumulated, seg, befores)
    summary = jax.vmap(local_state)(inp, b_blocks, cumulated, seg)

    columns = jnp.arange(count)[:, None]
    row = jnp.zeros((count, heads), factor.dtype)
    rows = [row]
    for k in range(1, count):
        row = jnp.where(columns < k - 1, row * factor[k - 1][None, :], (columns == k - 1).astype(factor.dtype))
        rows.append(row)
    reach = jnp.stack(rows)
    state_in = jnp.einsum("kjh,jhnp->khnp", reach, summary, precision=precise)

    def stretch(i, brow, crow, d, sg, bf, st):
        return mixer_stretch(i, brow, crow, d, gains, sg, bf, st)[0]

    outputs = jax.vmap(stretch)(inp, b_blocks, c_blocks, dec, seg, befores, state_in)
    return outputs.reshape(count * width, heads, P_SIZE)


def mamba_by_heads(x_input, b_all, c_all, decay_log, skip_gain, doc_lengths, mixer_cot):
    seq_count = lax.axis_size("seq")
    place = lax.axis_index("seq")
    tokens = x_input.shape[0]
    heads_here = skip_gain.shape[0]
    own = heads_here // seq_count
    total = tokens * seq_count
    pair = lax.all_to_all(
        jnp.stack([x_input, mixer_cot]), "seq", split_axis=2, concat_axis=1, tiled=True
    )
    decay = lax.all_to_all(decay_log, "seq", split_axis=0, concat_axis=1, tiled=True)
    gains = lax.dynamic_slice_in_dim(skip_gain, place * own, own)
    segment = doc_index(jnp.arange(total, dtype=jnp.int32), doc_lengths)
    inputs = pair[0].astype(jnp.float32).reshape(total, own, P_SIZE)
    cot = pair[1].astype(jnp.float32).reshape(total, own, P_SIZE)

    def whole_of(i, brow, crow, d):
        return mixer_whole(i, brow, crow, d, gains, segment)

    mixed, pull = jax.vjp(
        whole_of, inputs, b_all.astype(jnp.float32), c_all.astype(jnp.float32), decay
    )
    grad_x, grad_b, grad_c, grad_decay = pull(cot)
    back = jnp.stack(
        [
            mixed.reshape(total, own * P_SIZE).astype(jnp.bfloat16),
            grad_x.reshape(total, own * P_SIZE).astype(jnp.bfloat16),
        ]
    )
    back = lax.all_to_all(back, "seq", split_axis=1, concat_axis=2, tiled=True)
    decay_cols = lax.dynamic_update_slice_in_dim(
        jnp.zeros((total, heads_here), jnp.float32), grad_decay.T, place * own, 1
    )
    return back[0], back[1], jnp.concatenate([grad_b, grad_c, decay_cols], axis=1)


def mamba_by_stretch(
    x_input, b_rows, c_rows, decay_log, skip_gain, doc_lengths, mixer_cot, segment, offset
):
    tokens = x_input.shape[0]
    previous = doc_index(jnp.reshape(offset - 1, (1,)), doc_lengths)[0]
    before = jnp.where(offset > 0, previous, -1)
    heads_here = skip_gain.shape[0]
    inputs = x_input.astype(jnp.float32).reshape(tokens, heads_here, P_SIZE)
    b_float = b_rows.astype(jnp.float32)
    c_float = c_rows.astype(jnp.float32)
    cot_float = mixer_cot.astype(jnp.float32).reshape(tokens, heads_here, P_SIZE)

    def stretch_of(inp, brow, crow, decay, state_in):
        return mixer_stretch(inp, brow, crow, decay, skip_gain, segment, before, state_in)

    cumulated = cumulate(decay_log)
    factor = carry_factor(cumulated, segment, before)
    summary = local_state(inputs, b_float, cumulated, segment)
    zero_state = jnp.zeros_like(summary)
    identity = (jnp.ones_like(factor), zero_state)
    state_in = entering_2((factor, summary), "seq", combine_states, identity, False)[1]
    (mixed, state_out), pull = jax.vjp(stretch_of, inputs, b_float, c_float, decay_log, state_in)
    adjoint_local = pull((cot_float, zero_state))[4]
    adjoint_out = entering_2((factor, adjoint_local), "seq", combine_states, identity, True)[1]
    grad_x, grad_b, grad_c, grad_decay, unused = pull((cot_float, adjoint_out))
    head_count = lax.axis_size("head")
    if head_count == 2:
        other_b, other_c = lax.ppermute((grad_b, grad_c), "head", [(0, 1), (1, 0)])
        grad_b, grad_c = grad_b + other_b, grad_c + other_c
    else:
        grad_b, grad_c = lax.psum((grad_b, grad_c), "head")
    mixer_out = mixed.reshape(tokens, heads_here * P_SIZE).astype(jnp.bfloat16)
    x_grad = grad_x.reshape(tokens, heads_here * P_SIZE).astype(jnp.bfloat16)
    return (mixer_out, x_grad, grad_b, grad_c, grad_decay)


def on_device(
    x_input,
    b_rows,
    c_rows,
    decay_log,
    skip_gain,
    doc_lengths,
    queries,
    attention_key_rows,
    values,
    mixer_cot,
    attention_output_cotangent,
):
    tokens = x_input.shape[0]
    offset = lax.axis_index("seq") * tokens
    total_len = tokens * lax.axis_size("seq")
    positions = offset + jnp.arange(tokens, dtype=jnp.int32)
    segment = doc_index(positions, doc_lengths)
    heads_here = skip_gain.shape[0]
    by_heads = heads_here % lax.axis_size("seq") == 0
    key_width = attention_key_rows.shape[1]
    state_width = b_rows.shape[1]
    pieces = [attention_key_rows, values] + ([b_rows, c_rows] if by_heads else [])
    gathered = lax.all_gather(jnp.concatenate(pieces, axis=1), "seq", axis=0, tiled=True)
    key_all, value_all = gathered[:, :key_width], gathered[:, key_width : 2 * key_width]
    if by_heads:
        b_all = gathered[:, 2 * key_width : 2 * key_width + state_width]
        c_all = gathered[:, 2 * key_width + state_width :]
        mixer_out, x_grad, bc_part = mamba_by_heads(
            x_input, b_all, c_all, decay_log, skip_gain, doc_lengths, mixer_cot
        )
    else:
        mixer_out, x_grad, grad_b, grad_c, grad_decay = mamba_by_stretch(
            x_input, b_rows, c_rows, decay_log, skip_gain, doc_lengths, mixer_cot, segment, offset
        )
    logit_scale = 1.0 / math.sqrt(HEAD_SIZE)
    groups = attention_key_rows.shape[1] // HEAD_SIZE
    heads_per_group = queries.shape[1] // HEAD_SIZE // groups
    key_span = min(512, total_len)
    blocks = total_len // key_span
    last_pos = offset + tokens - 1
    query_grid = queries.reshape(tokens, groups, heads_per_group, HEAD_SIZE)
    cotangent_table = attention_output_cotangent.reshape(tokens, groups, heads_per_group, HEAD_SIZE)

    def block_view(number):
        anchor = number * key_span
        key_blk = lax.dynamic_slice_in_dim(key_all, anchor, key_span, 0).reshape(
            key_span, groups, HEAD_SIZE
        )
        value_blk = lax.dynamic_slice_in_dim(value_all, anchor, key_span, 0).reshape(
            key_span, groups, HEAD_SIZE
        )
        key_pos = anchor + jnp.arange(key_span, dtype=jnp.int32)
        allowed = (key_pos[None, :] <= positions[:, None]) & (
            doc_index(key_pos, doc_lengths)[None, :] == segment[:, None]
        )
        scores = (
            jnp.einsum("tgrd,kgd->grtk", query_grid, key_blk, preferred_element_type=jnp.float32)
            * logit_scale
        )
        scores = jnp.where(allowed[None, None], scores, big_negative)
        return (anchor, key_blk, value_blk, allowed, scores)

    def visit(number, carried, work):
        return lax.cond(
            number * key_span <= last_pos,
            lambda inner: work(number, inner),
            lambda inner: inner,
            carried,
        )

    def stats_step(number, carried):
        row_peak, row_total = carried
        anchor, key_blk, value_blk, allowed, scores = block_view(number)
        new_peak = jnp.maximum(row_peak, jnp.max(scores, axis=-1))
        fresh = jnp.sum(
            jnp.where(allowed[None, None], jnp.exp(scores - new_peak[..., None]), 0.0), axis=-1
        )
        return (new_peak, row_total * jnp.exp(row_peak - new_peak) + fresh)

    stat_shape = (groups, heads_per_group, tokens)
    row_peak, row_total = lax.fori_loop(
        0,
        blocks,
        lambda number, carried: visit(number, carried, stats_step),
        (jnp.full(stat_shape, big_negative, jnp.float32), jnp.zeros(stat_shape, jnp.float32)),
    )
    log_norm = row_peak + jnp.log(row_total)

    def output_step(number, totals):
        anchor, key_blk, value_blk, allowed, scores = block_view(number)
        weights = jnp.where(allowed[None, None], jnp.exp(scores - log_norm[..., None]), 0.0).astype(
            jnp.bfloat16
        )
        return totals + jnp.einsum(
            "grtk,kgd->tgrd", weights, value_blk, preferred_element_type=jnp.float32
        )

    attention_table = lax.fori_loop(
        0,
        blocks,
        lambda number, carried: visit(number, carried, output_step),
        jnp.zeros((tokens, groups, heads_per_group, HEAD_SIZE), jnp.float32),
    ).astype(jnp.bfloat16)
    row_products = jnp.einsum(
        "bkfh,bkfh->kfb", cotangent_table, attention_table, preferred_element_type=jnp.float32
    )

    def grad_terms(allowed, scores, value_blk):
        probs_full = jnp.where(allowed[None, None], jnp.exp(scores - log_norm[..., None]), 0.0)
        grad_prob = jnp.einsum(
            "tgrd,kgd->grtk", cotangent_table, value_blk, preferred_element_type=jnp.float32
        )
        grad_score = (probs_full * (grad_prob - row_products[..., None])).astype(jnp.bfloat16)
        return (probs_full.astype(jnp.bfloat16), grad_score)

    query_zero = jnp.zeros((tokens, groups, heads_per_group, HEAD_SIZE), jnp.float32)

    def full_step(number, carried):
        grad_query, term_key, term_value = carried
        anchor, key_blk, value_blk, allowed, scores = block_view(number)
        weights, grad_score = grad_terms(allowed, scores, value_blk)
        grad_query = grad_query + jnp.einsum(
            "grtk,kgd->tgrd", grad_score, key_blk, preferred_element_type=jnp.float32
        )
        key_part = jnp.einsum(
            "grtk,tgrd->kgd", grad_score, query_grid, preferred_element_type=jnp.float32
        ).reshape(key_span, groups * HEAD_SIZE)
        value_part = jnp.einsum(
            "grtk,tgrd->kgd", weights, cotangent_table, preferred_element_type=jnp.float32
        ).reshape(key_span, groups * HEAD_SIZE)
        term_key = lax.dynamic_update_slice_in_dim(term_key, key_part, anchor, 0)
        term_value = lax.dynamic_update_slice_in_dim(term_value, value_part, anchor, 0)
        return (grad_query, term_key, term_value)

    term_zero = jnp.zeros((total_len, groups * HEAD_SIZE), jnp.float32)
    grad_query, term_key, term_value = lax.fori_loop(
        0,
        blocks,
        lambda number, carried: visit(number, carried, full_step),
        (query_zero, term_zero, term_zero),
    )
    seq_count = lax.axis_size("seq")
    kv_terms = jnp.concatenate([term_key, term_value], axis=1).astype(jnp.bfloat16)
    kv_terms = lax.all_to_all(
        kv_terms.reshape(seq_count, tokens, 2 * groups * HEAD_SIZE),
        "seq",
        split_axis=0,
        concat_axis=0,
        tiled=True,
    )
    kv_total = jnp.sum(kv_terms.astype(jnp.float32), axis=0)
    key_gradient_total = kv_total[:, : groups * HEAD_SIZE]
    value_gradient_total = kv_total[:, groups * HEAD_SIZE :]
    if by_heads:
        bc_sum = lax.psum_scatter(bc_part, "seq", scatter_dimension=0, tiled=True)
        grad_decay = bc_sum[:, 2 * state_width :].T
        bc_sum = bc_sum[:, : 2 * state_width]
        if lax.axis_size("head") == 2:
            bc_sum = bc_sum + lax.ppermute(bc_sum, "head", [(0, 1), (1, 0)])
        else:
            bc_sum = lax.psum(bc_sum, "head")
        grad_b, grad_c = bc_sum[:, :state_width], bc_sum[:, state_width:]
    attn_out = attention_table.reshape(tokens, groups * heads_per_group * HEAD_SIZE)
    q_grad = (
        (grad_query * logit_scale)
        .reshape(tokens, groups * heads_per_group * HEAD_SIZE)
        .astype(jnp.bfloat16)
    )
    key_gradient = (key_gradient_total * logit_scale).astype(jnp.bfloat16)
    value_gradient = value_gradient_total.astype(jnp.bfloat16)
    return (
        mixer_out,
        attn_out,
        x_grad,
        grad_b,
        grad_c,
        grad_decay,
        q_grad,
        key_gradient,
        value_gradient,
    )


def solution(mesh):
    placed = (
        P(("groups", "seq"), "head"),
        P(("groups", "seq"), None),
        P(("groups", "seq"), None),
        P(("groups", "head"), "seq"),
        P("head"),
        P("groups"),
        P(("groups", "seq"), "head"),
        P(("groups", "seq"), "head"),
        P(("groups", "seq"), "head"),
        P(("groups", "seq"), "head"),
        P(("groups", "seq"), "head"),
    )
    return jax.shard_map(
        on_device,
        mesh=mesh,
        in_specs=placed,
        out_specs=(
            P(("groups", "seq"), "head"),
            P(("groups", "seq"), "head"),
            P(("groups", "seq"), "head"),
            P(("groups", "seq"), None),
            P(("groups", "seq"), None),
            P(("groups", "head"), "seq"),
            P(("groups", "seq"), "head"),
            P(("groups", "seq"), "head"),
            P(("groups", "seq"), "head"),
        ),
        check_vma=False,
    )
```

```python
import math

import jax
import jax.numpy as jnp
from jax import lax
from jax.sharding import PartitionSpec as P

P_SIZE = 128
HEAD_SIZE = 128
TOK_SPAN = 128


precise = lax.Precision.HIGHEST
big_negative = -1e30


def entering_2(part, axis, combine, identity, reverse):
    count = lax.axis_size(axis)
    place = lax.axis_index(axis)
    ahead = count - 1 - place if reverse else place
    early = jax.tree.map(lambda a, e: jnp.zeros_like(a) + jnp.asarray(e, a.dtype), part, identity)
    span = part
    shift = 1
    while shift < count:
        if reverse:
            pairs = [(i, i - shift) for i in range(shift, count)]
        else:
            pairs = [(i, i + shift) for i in range(count - shift)]
        got = lax.ppermute(span, axis, pairs)
        have = ahead >= shift
        got = jax.tree.map(lambda g, e: jnp.where(have, g, jnp.asarray(e, g.dtype)), got, identity)
        early = combine(got, early)
        if 2 * shift < count:
            span = combine(got, span)
        shift *= 2
    return early


def doc_index(positions, lengths):
    ends = jnp.cumsum(lengths)
    return jnp.sum((positions[:, None] >= ends[None, :]).astype(jnp.int32), axis=1)


def cumulate(decay):
    return jnp.cumsum(decay, axis=1)


def local_state(inputs, b_float, cumulated, segment):
    weights = (
        jnp.exp(cumulated[:, -1:] - cumulated)
        * (segment == segment[-1]).astype(inputs.dtype)[None, :]
    )
    return jnp.einsum("hs,sn,shp->hnp", weights, b_float, inputs, precision=precise)


def carry_factor(cumulated, segment, before):
    return jnp.exp(cumulated[:, -1]) * (segment[-1] == before).astype(cumulated.dtype)


def mixer_stretch(inputs, b_float, c_float, decay, gains, segment, before, state_in):
    cumulated = cumulate(decay)
    width = inputs.shape[0]
    steps = jnp.arange(width)
    allowed = (steps[:, None] >= steps[None, :]) & (segment[:, None] == segment[None, :])
    gaps = jnp.where(allowed[None], cumulated[:, :, None] - cumulated[:, None, :], big_negative)
    kernel = jnp.exp(gaps) * jnp.dot(c_float, b_float.T, precision=precise)[None]
    inner = jnp.einsum("hts,shp->thp", kernel, inputs, precision=precise)
    keeps = (segment == before).astype(inputs.dtype)
    entering = jnp.einsum("tn,hnp->thp", c_float, state_in, precision=precise)
    reach = jnp.exp(cumulated).T * keeps[:, None]
    outputs = inner + reach[:, :, None] * entering + gains[None, :, None] * inputs
    factor = carry_factor(cumulated, segment, before)
    state_out = factor[:, None, None] * state_in + local_state(inputs, b_float, cumulated, segment)
    return (outputs, state_out)


def combine_states(earlier, later):
    return (earlier[0] * later[0], later[0][:, None, None] * earlier[1] + later[1])


def mixer_whole(inputs, b_float, c_float, decay, gains, segment):
    width = TOK_SPAN
    count = inputs.shape[0] // width
    heads = inputs.shape[1]
    inp = inputs.reshape(count, width, heads, P_SIZE)
    b_blocks = b_float.reshape(count, width, -1)
    c_blocks = c_float.reshape(count, width, -1)
    dec = decay.reshape(heads, count, width).transpose(1, 0, 2)
    seg = segment.reshape(count, width)
    befores = jnp.concatenate([jnp.full((1,), -1, seg.dtype), seg[:-1, -1]])
    cumulated = jnp.cumsum(dec, axis=2)
    factor = jax.vmap(carry_factor)(cumulated, seg, befores)
    summary = jax.vmap(local_state)(inp, b_blocks, cumulated, seg)

    columns = jnp.arange(count)[:, None]
    row = jnp.zeros((count, heads), factor.dtype)
    rows = [row]
    for k in range(1, count):
        row = jnp.where(columns < k - 1, row * factor[k - 1][None, :], (columns == k - 1).astype(factor.dtype))
        rows.append(row)
    reach = jnp.stack(rows)
    state_in = jnp.einsum("kjh,jhnp->khnp", reach, summary, precision=precise)

    def stretch(i, brow, crow, d, sg, bf, st):
        return mixer_stretch(i, brow, crow, d, gains, sg, bf, st)[0]

    outputs = jax.vmap(stretch)(inp, b_blocks, c_blocks, dec, seg, befores, state_in)
    return outputs.reshape(count * width, heads, P_SIZE)


def mamba_by_heads(x_input, b_all, c_all, decay_log, skip_gain, doc_lengths, mixer_cot):
    seq_count = lax.axis_size("seq")
    place = lax.axis_index("seq")
    tokens = x_input.shape[0]
    heads_here = skip_gain.shape[0]
    own = heads_here // seq_count
    total = tokens * seq_count
    pair = lax.all_to_all(
        jnp.stack([x_input, mixer_cot]), "seq", split_axis=2, concat_axis=1, tiled=True
    )
    decay = lax.all_to_all(decay_log, "seq", split_axis=0, concat_axis=1, tiled=True)
    gains = lax.dynamic_slice_in_dim(skip_gain, place * own, own)
    segment = doc_index(jnp.arange(total, dtype=jnp.int32), doc_lengths)
    inputs = pair[0].astype(jnp.float32).reshape(total, own, P_SIZE)
    cot = pair[1].astype(jnp.float32).reshape(total, own, P_SIZE)

    def whole_of(i, brow, crow, d):
        return mixer_whole(i, brow, crow, d, gains, segment)

    mixed, pull = jax.vjp(
        whole_of, inputs, b_all.astype(jnp.float32), c_all.astype(jnp.float32), decay
    )
    grad_x, grad_b, grad_c, grad_decay = pull(cot)
    back = jnp.stack(
        [
            mixed.reshape(total, own * P_SIZE).astype(jnp.bfloat16),
            grad_x.reshape(total, own * P_SIZE).astype(jnp.bfloat16),
        ]
    )
    back = lax.all_to_all(back, "seq", split_axis=1, concat_axis=2, tiled=True)
    decay_cols = lax.dynamic_update_slice_in_dim(
        jnp.zeros((total, heads_here), jnp.float32), grad_decay.T, place * own, 1
    )
    return back[0], back[1], jnp.concatenate([grad_b, grad_c, decay_cols], axis=1)


def mamba_by_stretch(
    x_input, b_rows, c_rows, decay_log, skip_gain, doc_lengths, mixer_cot, segment, offset
):
    tokens = x_input.shape[0]
    previous = doc_index(jnp.reshape(offset - 1, (1,)), doc_lengths)[0]
    before = jnp.where(offset > 0, previous, -1)
    heads_here = skip_gain.shape[0]
    inputs = x_input.astype(jnp.float32).reshape(tokens, heads_here, P_SIZE)
    b_float = b_rows.astype(jnp.float32)
    c_float = c_rows.astype(jnp.float32)
    cot_float = mixer_cot.astype(jnp.float32).reshape(tokens, heads_here, P_SIZE)

    def stretch_of(inp, brow, crow, decay, state_in):
        return mixer_stretch(inp, brow, crow, decay, skip_gain, segment, before, state_in)

    cumulated = cumulate(decay_log)
    factor = carry_factor(cumulated, segment, before)
    summary = local_state(inputs, b_float, cumulated, segment)
    zero_state = jnp.zeros_like(summary)
    identity = (jnp.ones_like(factor), zero_state)
    state_in = entering_2((factor, summary), "seq", combine_states, identity, False)[1]
    (mixed, state_out), pull = jax.vjp(stretch_of, inputs, b_float, c_float, decay_log, state_in)
    adjoint_local = pull((cot_float, zero_state))[4]
    adjoint_out = entering_2((factor, adjoint_local), "seq", combine_states, identity, True)[1]
    grad_x, grad_b, grad_c, grad_decay, unused = pull((cot_float, adjoint_out))
    head_count = lax.axis_size("head")
    if head_count == 2:
        other_b, other_c = lax.ppermute((grad_b, grad_c), "head", [(0, 1), (1, 0)])
        grad_b, grad_c = grad_b + other_b, grad_c + other_c
    else:
        grad_b, grad_c = lax.psum((grad_b, grad_c), "head")
    mixer_out = mixed.reshape(tokens, heads_here * P_SIZE).astype(jnp.bfloat16)
    x_grad = grad_x.reshape(tokens, heads_here * P_SIZE).astype(jnp.bfloat16)
    return (mixer_out, x_grad, grad_b, grad_c, grad_decay)


def on_device(
    x_input,
    b_rows,
    c_rows,
    decay_log,
    skip_gain,
    doc_lengths,
    queries,
    attention_key_rows,
    values,
    mixer_cot,
    attention_output_cotangent,
):
    tokens = x_input.shape[0]
    offset = lax.axis_index("seq") * tokens
    total_len = tokens * lax.axis_size("seq")
    positions = offset + jnp.arange(tokens, dtype=jnp.int32)
    segment = doc_index(positions, doc_lengths)
    heads_here = skip_gain.shape[0]
    by_heads = heads_here % lax.axis_size("seq") == 0
    key_width = attention_key_rows.shape[1]
    state_width = b_rows.shape[1]
    pieces = [attention_key_rows, values] + ([b_rows, c_rows] if by_heads else [])
    joined = jnp.concatenate(pieces, axis=1)
    if by_heads:
        gathered = lax.all_to_all(
            jnp.broadcast_to(joined[None], (lax.axis_size("seq"),) + joined.shape),
            "seq",
            split_axis=0,
            concat_axis=0,
            tiled=True,
        ).reshape(total_len, joined.shape[1])
    else:
        gathered = lax.all_gather(joined, "seq", axis=0, tiled=True)
    key_all, value_all = gathered[:, :key_width], gathered[:, key_width : 2 * key_width]
    if by_heads:
        b_all = gathered[:, 2 * key_width : 2 * key_width + state_width]
        c_all = gathered[:, 2 * key_width + state_width :]
        mixer_out, x_grad, bc_part = mamba_by_heads(
            x_input, b_all, c_all, decay_log, skip_gain, doc_lengths, mixer_cot
        )
    else:
        mixer_out, x_grad, grad_b, grad_c, grad_decay = mamba_by_stretch(
            x_input, b_rows, c_rows, decay_log, skip_gain, doc_lengths, mixer_cot, segment, offset
        )
    logit_scale = 1.0 / math.sqrt(HEAD_SIZE)
    groups = attention_key_rows.shape[1] // HEAD_SIZE
    heads_per_group = queries.shape[1] // HEAD_SIZE // groups
    key_span = min(512, total_len)
    blocks = total_len // key_span
    last_pos = offset + tokens - 1
    query_grid = queries.reshape(tokens, groups, heads_per_group, HEAD_SIZE)
    cotangent_table = attention_output_cotangent.reshape(tokens, groups, heads_per_group, HEAD_SIZE)

    def block_view(number):
        anchor = number * key_span
        key_blk = lax.dynamic_slice_in_dim(key_all, anchor, key_span, 0).reshape(
            key_span, groups, HEAD_SIZE
        )
        value_blk = lax.dynamic_slice_in_dim(value_all, anchor, key_span, 0).reshape(
            key_span, groups, HEAD_SIZE
        )
        key_pos = anchor + jnp.arange(key_span, dtype=jnp.int32)
        allowed = (key_pos[None, :] <= positions[:, None]) & (
            doc_index(key_pos, doc_lengths)[None, :] == segment[:, None]
        )
        scores = (
            jnp.einsum("tgrd,kgd->grtk", query_grid, key_blk, preferred_element_type=jnp.float32)
            * logit_scale
        )
        scores = jnp.where(allowed[None, None], scores, big_negative)
        return (anchor, key_blk, value_blk, allowed, scores)

    def visit(number, carried, work):
        return lax.cond(
            number * key_span <= last_pos,
            lambda inner: work(number, inner),
            lambda inner: inner,
            carried,
        )

    def stats_step(number, carried):
        row_peak, row_total = carried
        anchor, key_blk, value_blk, allowed, scores = block_view(number)
        new_peak = jnp.maximum(row_peak, jnp.max(scores, axis=-1))
        fresh = jnp.sum(
            jnp.where(allowed[None, None], jnp.exp(scores - new_peak[..., None]), 0.0), axis=-1
        )
        return (new_peak, row_total * jnp.exp(row_peak - new_peak) + fresh)

    stat_shape = (groups, heads_per_group, tokens)
    row_peak, row_total = lax.fori_loop(
        0,
        blocks,
        lambda number, carried: visit(number, carried, stats_step),
        (jnp.full(stat_shape, big_negative, jnp.float32), jnp.zeros(stat_shape, jnp.float32)),
    )
    log_norm = row_peak + jnp.log(row_total)

    def output_step(number, totals):
        anchor, key_blk, value_blk, allowed, scores = block_view(number)
        weights = jnp.where(allowed[None, None], jnp.exp(scores - log_norm[..., None]), 0.0).astype(
            jnp.bfloat16
        )
        return totals + jnp.einsum(
            "grtk,kgd->tgrd", weights, value_blk, preferred_element_type=jnp.float32
        )

    attention_table = lax.fori_loop(
        0,
        blocks,
        lambda number, carried: visit(number, carried, output_step),
        jnp.zeros((tokens, groups, heads_per_group, HEAD_SIZE), jnp.float32),
    ).astype(jnp.bfloat16)
    row_products = jnp.einsum(
        "bkfh,bkfh->kfb", cotangent_table, attention_table, preferred_element_type=jnp.float32
    )

    def grad_terms(allowed, scores, value_blk):
        probs_full = jnp.where(allowed[None, None], jnp.exp(scores - log_norm[..., None]), 0.0)
        grad_prob = jnp.einsum(
            "tgrd,kgd->grtk", cotangent_table, value_blk, preferred_element_type=jnp.float32
        )
        grad_score = (probs_full * (grad_prob - row_products[..., None])).astype(jnp.bfloat16)
        return (probs_full.astype(jnp.bfloat16), grad_score)

    query_zero = jnp.zeros((tokens, groups, heads_per_group, HEAD_SIZE), jnp.float32)

    def full_step(number, carried):
        grad_query, term_key, term_value = carried
        anchor, key_blk, value_blk, allowed, scores = block_view(number)
        weights, grad_score = grad_terms(allowed, scores, value_blk)
        grad_query = grad_query + jnp.einsum(
            "grtk,kgd->tgrd", grad_score, key_blk, preferred_element_type=jnp.float32
        )
        key_part = jnp.einsum(
            "grtk,tgrd->kgd", grad_score, query_grid, preferred_element_type=jnp.float32
        ).reshape(key_span, groups * HEAD_SIZE)
        value_part = jnp.einsum(
            "grtk,tgrd->kgd", weights, cotangent_table, preferred_element_type=jnp.float32
        ).reshape(key_span, groups * HEAD_SIZE)
        term_key = lax.dynamic_update_slice_in_dim(term_key, key_part, anchor, 0)
        term_value = lax.dynamic_update_slice_in_dim(term_value, value_part, anchor, 0)
        return (grad_query, term_key, term_value)

    term_zero = jnp.zeros((total_len, groups * HEAD_SIZE), jnp.float32)
    grad_query, term_key, term_value = lax.fori_loop(
        0,
        blocks,
        lambda number, carried: visit(number, carried, full_step),
        (query_zero, term_zero, term_zero),
    )
    seq_count = lax.axis_size("seq")
    kv_terms = jnp.concatenate([term_key, term_value], axis=1).astype(jnp.bfloat16)
    kv_terms = lax.all_to_all(
        kv_terms.reshape(seq_count, tokens, 2 * groups * HEAD_SIZE),
        "seq",
        split_axis=0,
        concat_axis=0,
        tiled=True,
    )
    kv_total = jnp.sum(kv_terms.astype(jnp.float32), axis=0)
    key_gradient_total = kv_total[:, : groups * HEAD_SIZE]
    value_gradient_total = kv_total[:, groups * HEAD_SIZE :]
    if by_heads:
        bc_sum = lax.all_to_all(
            bc_part.reshape(seq_count, tokens, bc_part.shape[1]),
            "seq",
            split_axis=0,
            concat_axis=0,
            tiled=True,
        )
        bc_sum = jnp.sum(bc_sum, axis=0)
        grad_decay = bc_sum[:, 2 * state_width :].T
        bc_sum = bc_sum[:, : 2 * state_width]
        if lax.axis_size("head") == 2:
            bc_sum = bc_sum + lax.ppermute(bc_sum, "head", [(0, 1), (1, 0)])
        else:
            bc_sum = lax.psum(bc_sum, "head")
        grad_b, grad_c = bc_sum[:, :state_width], bc_sum[:, state_width:]
    attn_out = attention_table.reshape(tokens, groups * heads_per_group * HEAD_SIZE)
    q_grad = (
        (grad_query * logit_scale)
        .reshape(tokens, groups * heads_per_group * HEAD_SIZE)
        .astype(jnp.bfloat16)
    )
    key_gradient = (key_gradient_total * logit_scale).astype(jnp.bfloat16)
    value_gradient = value_gradient_total.astype(jnp.bfloat16)
    return (
        mixer_out,
        attn_out,
        x_grad,
        grad_b,
        grad_c,
        grad_decay,
        q_grad,
        key_gradient,
        value_gradient,
    )


def solution(mesh):
    placed = (
        P(("groups", "seq"), "head"),
        P(("groups", "seq"), None),
        P(("groups", "seq"), None),
        P(("groups", "head"), "seq"),
        P("head"),
        P("groups"),
        P(("groups", "seq"), "head"),
        P(("groups", "seq"), "head"),
        P(("groups", "seq"), "head"),
        P(("groups", "seq"), "head"),
        P(("groups", "seq"), "head"),
    )
    return jax.shard_map(
        on_device,
        mesh=mesh,
        in_specs=placed,
        out_specs=(
            P(("groups", "seq"), "head"),
            P(("groups", "seq"), "head"),
            P(("groups", "seq"), "head"),
            P(("groups", "seq"), None),
            P(("groups", "seq"), None),
            P(("groups", "head"), "seq"),
            P(("groups", "seq"), "head"),
            P(("groups", "seq"), "head"),
            P(("groups", "seq"), "head"),
        ),
        check_vma=False,
    )
```

```python
import math

import jax
import jax.numpy as jnp
from jax import lax
from jax.sharding import PartitionSpec as P

P_SIZE = 128
HEAD_SIZE = 128
TOK_SPAN = 128


precise = lax.Precision.HIGHEST
big_negative = -1e30


def entering_2(part, axis, combine, identity, reverse):
    count = lax.axis_size(axis)
    place = lax.axis_index(axis)
    ahead = count - 1 - place if reverse else place
    early = jax.tree.map(lambda a, e: jnp.zeros_like(a) + jnp.asarray(e, a.dtype), part, identity)
    span = part
    shift = 1
    while shift < count:
        if reverse:
            pairs = [(i, i - shift) for i in range(shift, count)]
        else:
            pairs = [(i, i + shift) for i in range(count - shift)]
        got = lax.ppermute(span, axis, pairs)
        have = ahead >= shift
        got = jax.tree.map(lambda g, e: jnp.where(have, g, jnp.asarray(e, g.dtype)), got, identity)
        early = combine(got, early)
        if 2 * shift < count:
            span = combine(got, span)
        shift *= 2
    return early


def doc_index(positions, lengths):
    ends = jnp.cumsum(lengths)
    return jnp.sum((positions[:, None] >= ends[None, :]).astype(jnp.int32), axis=1)


def cumulate(decay):
    return jnp.cumsum(decay, axis=1)


def local_state(inputs, b_float, cumulated, segment):
    weights = (
        jnp.exp(cumulated[:, -1:] - cumulated)
        * (segment == segment[-1]).astype(inputs.dtype)[None, :]
    )
    return jnp.einsum("hs,sn,shp->hnp", weights, b_float, inputs, precision=precise)


def carry_factor(cumulated, segment, before):
    return jnp.exp(cumulated[:, -1]) * (segment[-1] == before).astype(cumulated.dtype)


def mixer_stretch(inputs, b_float, c_float, decay, gains, segment, before, state_in):
    cumulated = cumulate(decay)
    width = inputs.shape[0]
    steps = jnp.arange(width)
    allowed = (steps[:, None] >= steps[None, :]) & (segment[:, None] == segment[None, :])
    gaps = jnp.where(allowed[None], cumulated[:, :, None] - cumulated[:, None, :], big_negative)
    kernel = jnp.exp(gaps) * jnp.dot(c_float, b_float.T, precision=precise)[None]
    inner = jnp.einsum("hts,shp->thp", kernel, inputs, precision=precise)
    keeps = (segment == before).astype(inputs.dtype)
    entering = jnp.einsum("tn,hnp->thp", c_float, state_in, precision=precise)
    reach = jnp.exp(cumulated).T * keeps[:, None]
    outputs = inner + reach[:, :, None] * entering + gains[None, :, None] * inputs
    factor = carry_factor(cumulated, segment, before)
    state_out = factor[:, None, None] * state_in + local_state(inputs, b_float, cumulated, segment)
    return (outputs, state_out)


def combine_states(earlier, later):
    return (earlier[0] * later[0], later[0][:, None, None] * earlier[1] + later[1])


def mixer_whole(inputs, b_float, c_float, decay, gains, segment):
    width = TOK_SPAN
    count = inputs.shape[0] // width
    heads = inputs.shape[1]
    inp = inputs.reshape(count, width, heads, P_SIZE)
    b_blocks = b_float.reshape(count, width, -1)
    c_blocks = c_float.reshape(count, width, -1)
    dec = decay.reshape(heads, count, width).transpose(1, 0, 2)
    seg = segment.reshape(count, width)
    befores = jnp.concatenate([jnp.full((1,), -1, seg.dtype), seg[:-1, -1]])
    cumulated = jnp.cumsum(dec, axis=2)
    factor = jax.vmap(carry_factor)(cumulated, seg, befores)
    summary = jax.vmap(local_state)(inp, b_blocks, cumulated, seg)

    columns = jnp.arange(count)[:, None]
    row = jnp.zeros((count, heads), factor.dtype)
    rows = [row]
    for k in range(1, count):
        row = jnp.where(columns < k - 1, row * factor[k - 1][None, :], (columns == k - 1).astype(factor.dtype))
        rows.append(row)
    reach = jnp.stack(rows)
    state_in = jnp.einsum("kjh,jhnp->khnp", reach, summary, precision=precise)

    def stretch(i, brow, crow, d, sg, bf, st):
        return mixer_stretch(i, brow, crow, d, gains, sg, bf, st)[0]

    outputs = jax.vmap(stretch)(inp, b_blocks, c_blocks, dec, seg, befores, state_in)
    return outputs.reshape(count * width, heads, P_SIZE)


def mamba_by_heads(x_all, cot_all, b_all, c_all, decay_log, skip_gain, doc_lengths):
    seq_count = lax.axis_size("seq")
    place = lax.axis_index("seq")
    heads_here = skip_gain.shape[0]
    own = heads_here // seq_count
    total = x_all.shape[0]
    decay = lax.all_to_all(decay_log, "seq", split_axis=0, concat_axis=1, tiled=True)
    gains = lax.dynamic_slice_in_dim(skip_gain, place * own, own)
    segment = doc_index(jnp.arange(total, dtype=jnp.int32), doc_lengths)
    inputs = x_all.astype(jnp.float32).reshape(total, own, P_SIZE)
    cot = cot_all.astype(jnp.float32).reshape(total, own, P_SIZE)

    def whole_of(i, brow, crow, d):
        return mixer_whole(i, brow, crow, d, gains, segment)

    mixed, pull = jax.vjp(
        whole_of, inputs, b_all.astype(jnp.float32), c_all.astype(jnp.float32), decay
    )
    grad_x, grad_b, grad_c, grad_decay = pull(cot)
    decay_cols = lax.dynamic_update_slice_in_dim(
        jnp.zeros((total, heads_here), jnp.float32), grad_decay.T, place * own, 1
    )
    return (
        mixed.reshape(total, own * P_SIZE).astype(jnp.bfloat16),
        grad_x.reshape(total, own * P_SIZE).astype(jnp.bfloat16),
        jnp.concatenate([grad_b, grad_c, decay_cols], axis=1),
    )


def mamba_by_stretch(
    x_input, b_rows, c_rows, decay_log, skip_gain, doc_lengths, mixer_cot, segment, offset
):
    tokens = x_input.shape[0]
    previous = doc_index(jnp.reshape(offset - 1, (1,)), doc_lengths)[0]
    before = jnp.where(offset > 0, previous, -1)
    heads_here = skip_gain.shape[0]
    inputs = x_input.astype(jnp.float32).reshape(tokens, heads_here, P_SIZE)
    b_float = b_rows.astype(jnp.float32)
    c_float = c_rows.astype(jnp.float32)
    cot_float = mixer_cot.astype(jnp.float32).reshape(tokens, heads_here, P_SIZE)

    def stretch_of(inp, brow, crow, decay, state_in):
        return mixer_stretch(inp, brow, crow, decay, skip_gain, segment, before, state_in)

    cumulated = cumulate(decay_log)
    factor = carry_factor(cumulated, segment, before)
    summary = local_state(inputs, b_float, cumulated, segment)
    zero_state = jnp.zeros_like(summary)
    identity = (jnp.ones_like(factor), zero_state)
    state_in = entering_2((factor, summary), "seq", combine_states, identity, False)[1]
    (mixed, state_out), pull = jax.vjp(stretch_of, inputs, b_float, c_float, decay_log, state_in)
    adjoint_local = pull((cot_float, zero_state))[4]
    adjoint_out = entering_2((factor, adjoint_local), "seq", combine_states, identity, True)[1]
    grad_x, grad_b, grad_c, grad_decay, unused = pull((cot_float, adjoint_out))
    head_count = lax.axis_size("head")
    if head_count == 2:
        other_b, other_c = lax.ppermute((grad_b, grad_c), "head", [(0, 1), (1, 0)])
        grad_b, grad_c = grad_b + other_b, grad_c + other_c
    else:
        grad_b, grad_c = lax.psum((grad_b, grad_c), "head")
    mixer_out = mixed.reshape(tokens, heads_here * P_SIZE).astype(jnp.bfloat16)
    x_grad = grad_x.reshape(tokens, heads_here * P_SIZE).astype(jnp.bfloat16)
    return (mixer_out, x_grad, grad_b, grad_c, grad_decay)


def on_device(
    x_input,
    b_rows,
    c_rows,
    decay_log,
    skip_gain,
    doc_lengths,
    queries,
    attention_key_rows,
    values,
    mixer_cot,
    attention_output_cotangent,
):
    tokens = x_input.shape[0]
    offset = lax.axis_index("seq") * tokens
    total_len = tokens * lax.axis_size("seq")
    positions = offset + jnp.arange(tokens, dtype=jnp.int32)
    segment = doc_index(positions, doc_lengths)
    heads_here = skip_gain.shape[0]
    by_heads = heads_here % lax.axis_size("seq") == 0
    key_width = attention_key_rows.shape[1]
    state_width = b_rows.shape[1]
    pieces = [attention_key_rows, values] + ([b_rows, c_rows] if by_heads else [])
    joined = jnp.concatenate(pieces, axis=1)
    seq_count = lax.axis_size("seq")
    if by_heads:
        own_width = heads_here // seq_count * P_SIZE

        def by_owner(a):
            return a.reshape(tokens, seq_count, own_width).transpose(1, 0, 2)

        sent = jnp.concatenate(
            [
                by_owner(x_input),
                by_owner(mixer_cot),
                jnp.broadcast_to(joined[None], (seq_count,) + joined.shape),
            ],
            axis=2,
        )
        got = lax.all_to_all(sent, "seq", split_axis=0, concat_axis=0, tiled=True)
        x_all = got[:, :, :own_width].reshape(total_len, own_width)
        cot_all = got[:, :, own_width : 2 * own_width].reshape(total_len, own_width)
        gathered = got[:, :, 2 * own_width :].reshape(total_len, joined.shape[1])
    else:
        gathered = lax.all_gather(joined, "seq", axis=0, tiled=True)
    key_all, value_all = gathered[:, :key_width], gathered[:, key_width : 2 * key_width]
    if by_heads:
        b_all = gathered[:, 2 * key_width : 2 * key_width + state_width]
        c_all = gathered[:, 2 * key_width + state_width :]
        mixed_own, x_grad_own, bc_part = mamba_by_heads(
            x_all, cot_all, b_all, c_all, decay_log, skip_gain, doc_lengths
        )
    else:
        mixer_out, x_grad, grad_b, grad_c, grad_decay = mamba_by_stretch(
            x_input, b_rows, c_rows, decay_log, skip_gain, doc_lengths, mixer_cot, segment, offset
        )
    logit_scale = 1.0 / math.sqrt(HEAD_SIZE)
    groups = attention_key_rows.shape[1] // HEAD_SIZE
    heads_per_group = queries.shape[1] // HEAD_SIZE // groups
    key_span = min(512, total_len)
    blocks = total_len // key_span
    last_pos = offset + tokens - 1
    query_grid = queries.reshape(tokens, groups, heads_per_group, HEAD_SIZE)
    cotangent_table = attention_output_cotangent.reshape(tokens, groups, heads_per_group, HEAD_SIZE)

    def block_view(number):
        anchor = number * key_span
        key_blk = lax.dynamic_slice_in_dim(key_all, anchor, key_span, 0).reshape(
            key_span, groups, HEAD_SIZE
        )
        value_blk = lax.dynamic_slice_in_dim(value_all, anchor, key_span, 0).reshape(
            key_span, groups, HEAD_SIZE
        )
        key_pos = anchor + jnp.arange(key_span, dtype=jnp.int32)
        allowed = (key_pos[None, :] <= positions[:, None]) & (
            doc_index(key_pos, doc_lengths)[None, :] == segment[:, None]
        )
        scores = (
            jnp.einsum("tgrd,kgd->grtk", query_grid, key_blk, preferred_element_type=jnp.float32)
            * logit_scale
        )
        scores = jnp.where(allowed[None, None], scores, big_negative)
        return (anchor, key_blk, value_blk, allowed, scores)

    def visit(number, carried, work):
        return lax.cond(
            number * key_span <= last_pos,
            lambda inner: work(number, inner),
            lambda inner: inner,
            carried,
        )

    def stats_step(number, carried):
        row_peak, row_total = carried
        anchor, key_blk, value_blk, allowed, scores = block_view(number)
        new_peak = jnp.maximum(row_peak, jnp.max(scores, axis=-1))
        fresh = jnp.sum(
            jnp.where(allowed[None, None], jnp.exp(scores - new_peak[..., None]), 0.0), axis=-1
        )
        return (new_peak, row_total * jnp.exp(row_peak - new_peak) + fresh)

    stat_shape = (groups, heads_per_group, tokens)
    row_peak, row_total = lax.fori_loop(
        0,
        blocks,
        lambda number, carried: visit(number, carried, stats_step),
        (jnp.full(stat_shape, big_negative, jnp.float32), jnp.zeros(stat_shape, jnp.float32)),
    )
    log_norm = row_peak + jnp.log(row_total)

    def output_step(number, totals):
        anchor, key_blk, value_blk, allowed, scores = block_view(number)
        weights = jnp.where(allowed[None, None], jnp.exp(scores - log_norm[..., None]), 0.0).astype(
            jnp.bfloat16
        )
        return totals + jnp.einsum(
            "grtk,kgd->tgrd", weights, value_blk, preferred_element_type=jnp.float32
        )

    attention_table = lax.fori_loop(
        0,
        blocks,
        lambda number, carried: visit(number, carried, output_step),
        jnp.zeros((tokens, groups, heads_per_group, HEAD_SIZE), jnp.float32),
    ).astype(jnp.bfloat16)
    row_products = jnp.einsum(
        "bkfh,bkfh->kfb", cotangent_table, attention_table, preferred_element_type=jnp.float32
    )

    def grad_terms(allowed, scores, value_blk):
        probs_full = jnp.where(allowed[None, None], jnp.exp(scores - log_norm[..., None]), 0.0)
        grad_prob = jnp.einsum(
            "tgrd,kgd->grtk", cotangent_table, value_blk, preferred_element_type=jnp.float32
        )
        grad_score = (probs_full * (grad_prob - row_products[..., None])).astype(jnp.bfloat16)
        return (probs_full.astype(jnp.bfloat16), grad_score)

    query_zero = jnp.zeros((tokens, groups, heads_per_group, HEAD_SIZE), jnp.float32)

    def full_step(number, carried):
        grad_query, term_key, term_value = carried
        anchor, key_blk, value_blk, allowed, scores = block_view(number)
        weights, grad_score = grad_terms(allowed, scores, value_blk)
        grad_query = grad_query + jnp.einsum(
            "grtk,kgd->tgrd", grad_score, key_blk, preferred_element_type=jnp.float32
        )
        key_part = jnp.einsum(
            "grtk,tgrd->kgd", grad_score, query_grid, preferred_element_type=jnp.float32
        ).reshape(key_span, groups * HEAD_SIZE)
        value_part = jnp.einsum(
            "grtk,tgrd->kgd", weights, cotangent_table, preferred_element_type=jnp.float32
        ).reshape(key_span, groups * HEAD_SIZE)
        term_key = lax.dynamic_update_slice_in_dim(term_key, key_part, anchor, 0)
        term_value = lax.dynamic_update_slice_in_dim(term_value, value_part, anchor, 0)
        return (grad_query, term_key, term_value)

    term_zero = jnp.zeros((total_len, groups * HEAD_SIZE), jnp.float32)
    grad_query, term_key, term_value = lax.fori_loop(
        0,
        blocks,
        lambda number, carried: visit(number, carried, full_step),
        (query_zero, term_zero, term_zero),
    )
    kv_terms = jnp.concatenate([term_key, term_value], axis=1).astype(jnp.bfloat16)
    kv_width = kv_terms.shape[1]
    if by_heads:
        sent = jnp.concatenate(
            [
                mixed_own.reshape(seq_count, tokens, own_width),
                x_grad_own.reshape(seq_count, tokens, own_width),
                kv_terms.reshape(seq_count, tokens, kv_width),
                bc_part.astype(jnp.bfloat16).reshape(seq_count, tokens, bc_part.shape[1]),
            ],
            axis=2,
        )
        got = lax.all_to_all(sent, "seq", split_axis=0, concat_axis=0, tiled=True)

        def from_owners(a):
            return a.transpose(1, 0, 2).reshape(tokens, seq_count * own_width)

        mixer_out = from_owners(got[:, :, :own_width])
        x_grad = from_owners(got[:, :, own_width : 2 * own_width])
        kv_total = jnp.sum(got[:, :, 2 * own_width : 2 * own_width + kv_width].astype(jnp.float32), axis=0)
        bc_sum = jnp.sum(got[:, :, 2 * own_width + kv_width :].astype(jnp.float32), axis=0)
        grad_decay = bc_sum[:, 2 * state_width :].T
        bc_sum = bc_sum[:, : 2 * state_width]
        if lax.axis_size("head") == 2:
            bc_sum = bc_sum + lax.ppermute(bc_sum, "head", [(0, 1), (1, 0)])
        else:
            bc_sum = lax.psum(bc_sum, "head")
        grad_b, grad_c = bc_sum[:, :state_width], bc_sum[:, state_width:]
    else:
        kv_terms = lax.all_to_all(
            kv_terms.reshape(seq_count, tokens, kv_width),
            "seq",
            split_axis=0,
            concat_axis=0,
            tiled=True,
        )
        kv_total = jnp.sum(kv_terms.astype(jnp.float32), axis=0)
    key_gradient_total = kv_total[:, : groups * HEAD_SIZE]
    value_gradient_total = kv_total[:, groups * HEAD_SIZE :]
    attn_out = attention_table.reshape(tokens, groups * heads_per_group * HEAD_SIZE)
    q_grad = (
        (grad_query * logit_scale)
        .reshape(tokens, groups * heads_per_group * HEAD_SIZE)
        .astype(jnp.bfloat16)
    )
    key_gradient = (key_gradient_total * logit_scale).astype(jnp.bfloat16)
    value_gradient = value_gradient_total.astype(jnp.bfloat16)
    return (
        mixer_out,
        attn_out,
        x_grad,
        grad_b,
        grad_c,
        grad_decay,
        q_grad,
        key_gradient,
        value_gradient,
    )


def solution(mesh):
    placed = (
        P(("groups", "seq"), "head"),
        P(("groups", "seq"), None),
        P(("groups", "seq"), None),
        P(("groups", "head"), "seq"),
        P("head"),
        P("groups"),
        P(("groups", "seq"), "head"),
        P(("groups", "seq"), "head"),
        P(("groups", "seq"), "head"),
        P(("groups", "seq"), "head"),
        P(("groups", "seq"), "head"),
    )
    return jax.shard_map(
        on_device,
        mesh=mesh,
        in_specs=placed,
        out_specs=(
            P(("groups", "seq"), "head"),
            P(("groups", "seq"), "head"),
            P(("groups", "seq"), "head"),
            P(("groups", "seq"), None),
            P(("groups", "seq"), None),
            P(("groups", "head"), "seq"),
            P(("groups", "seq"), "head"),
            P(("groups", "seq"), "head"),
            P(("groups", "seq"), "head"),
        ),
        check_vma=False,
    )
```

```python
import math

import jax
import jax.numpy as jnp
from jax import lax
from jax.sharding import PartitionSpec as P

P_SIZE = 128
HEAD_SIZE = 128
TOK_SPAN = 128


precise = lax.Precision.HIGHEST
big_negative = -1e30


def entering_2(part, axis, combine, identity, reverse):
    count = lax.axis_size(axis)
    place = lax.axis_index(axis)
    ahead = count - 1 - place if reverse else place
    early = jax.tree.map(lambda a, e: jnp.zeros_like(a) + jnp.asarray(e, a.dtype), part, identity)
    span = part
    shift = 1
    while shift < count:
        if reverse:
            pairs = [(i, i - shift) for i in range(shift, count)]
        else:
            pairs = [(i, i + shift) for i in range(count - shift)]
        got = lax.ppermute(span, axis, pairs)
        have = ahead >= shift
        got = jax.tree.map(lambda g, e: jnp.where(have, g, jnp.asarray(e, g.dtype)), got, identity)
        early = combine(got, early)
        if 2 * shift < count:
            span = combine(got, span)
        shift *= 2
    return early


def doc_index(positions, lengths):
    ends = jnp.cumsum(lengths)
    return jnp.sum((positions[:, None] >= ends[None, :]).astype(jnp.int32), axis=1)


def cumulate(decay):
    return jnp.cumsum(decay, axis=1)


def local_state(inputs, b_float, cumulated, segment):
    weights = (
        jnp.exp(cumulated[:, -1:] - cumulated)
        * (segment == segment[-1]).astype(inputs.dtype)[None, :]
    )
    return jnp.einsum("hs,sn,shp->hnp", weights, b_float, inputs, precision=precise)


def carry_factor(cumulated, segment, before):
    return jnp.exp(cumulated[:, -1]) * (segment[-1] == before).astype(cumulated.dtype)


def mixer_stretch(inputs, b_float, c_float, decay, gains, segment, before, state_in):
    cumulated = cumulate(decay)
    width = inputs.shape[0]
    steps = jnp.arange(width)
    allowed = (steps[:, None] >= steps[None, :]) & (segment[:, None] == segment[None, :])
    gaps = jnp.where(allowed[None], cumulated[:, :, None] - cumulated[:, None, :], big_negative)
    kernel = jnp.exp(gaps) * jnp.dot(c_float, b_float.T, precision=precise)[None]
    inner = jnp.einsum("hts,shp->thp", kernel, inputs, precision=precise)
    keeps = (segment == before).astype(inputs.dtype)
    entering = jnp.einsum("tn,hnp->thp", c_float, state_in, precision=precise)
    reach = jnp.exp(cumulated).T * keeps[:, None]
    outputs = inner + reach[:, :, None] * entering + gains[None, :, None] * inputs
    factor = carry_factor(cumulated, segment, before)
    state_out = factor[:, None, None] * state_in + local_state(inputs, b_float, cumulated, segment)
    return (outputs, state_out)


def combine_states(earlier, later):
    return (earlier[0] * later[0], later[0][:, None, None] * earlier[1] + later[1])


def mixer_whole(inputs, b_float, c_float, decay, gains, segment):
    width = TOK_SPAN
    count = inputs.shape[0] // width
    heads = inputs.shape[1]
    inp = inputs.reshape(count, width, heads, P_SIZE)
    b_blocks = b_float.reshape(count, width, -1)
    c_blocks = c_float.reshape(count, width, -1)
    dec = decay.reshape(heads, count, width).transpose(1, 0, 2)
    seg = segment.reshape(count, width)
    befores = jnp.concatenate([jnp.full((1,), -1, seg.dtype), seg[:-1, -1]])
    cumulated = jnp.cumsum(dec, axis=2)
    factor = jax.vmap(carry_factor)(cumulated, seg, befores)
    summary = jax.vmap(local_state)(inp, b_blocks, cumulated, seg)

    columns = jnp.arange(count)[:, None]
    row = jnp.zeros((count, heads), factor.dtype)
    rows = [row]
    for k in range(1, count):
        row = jnp.where(columns < k - 1, row * factor[k - 1][None, :], (columns == k - 1).astype(factor.dtype))
        rows.append(row)
    reach = jnp.stack(rows)
    state_in = jnp.einsum("kjh,jhnp->khnp", reach, summary, precision=precise)

    def stretch(i, brow, crow, d, sg, bf, st):
        return mixer_stretch(i, brow, crow, d, gains, sg, bf, st)[0]

    outputs = jax.vmap(stretch)(inp, b_blocks, c_blocks, dec, seg, befores, state_in)
    return outputs.reshape(count * width, heads, P_SIZE)


def mamba_by_heads(x_all, cot_all, b_all, c_all, decay_log, skip_gain, doc_lengths):
    seq_count = lax.axis_size("seq")
    place = lax.axis_index("seq")
    heads_here = skip_gain.shape[0]
    own = heads_here // seq_count
    total = x_all.shape[0]
    decay = lax.all_to_all(decay_log, "seq", split_axis=0, concat_axis=1, tiled=True)
    gains = lax.dynamic_slice_in_dim(skip_gain, place * own, own)
    segment = doc_index(jnp.arange(total, dtype=jnp.int32), doc_lengths)
    inputs = x_all.astype(jnp.float32).reshape(total, own, P_SIZE)
    cot = cot_all.astype(jnp.float32).reshape(total, own, P_SIZE)

    def whole_of(i, brow, crow, d):
        return mixer_whole(i, brow, crow, d, gains, segment)

    mixed, pull = jax.vjp(
        whole_of, inputs, b_all.astype(jnp.float32), c_all.astype(jnp.float32), decay
    )
    grad_x, grad_b, grad_c, grad_decay = pull(cot)
    decay_cols = lax.dynamic_update_slice_in_dim(
        jnp.zeros((total, heads_here), jnp.float32), grad_decay.T, place * own, 1
    )
    return (
        mixed.reshape(total, own * P_SIZE).astype(jnp.bfloat16),
        grad_x.reshape(total, own * P_SIZE).astype(jnp.bfloat16),
        jnp.concatenate([grad_b, grad_c, decay_cols], axis=1),
    )


def mamba_by_stretch(
    x_input, b_rows, c_rows, decay_log, skip_gain, doc_lengths, mixer_cot, segment, offset
):
    tokens = x_input.shape[0]
    previous = doc_index(jnp.reshape(offset - 1, (1,)), doc_lengths)[0]
    before = jnp.where(offset > 0, previous, -1)
    heads_here = skip_gain.shape[0]
    inputs = x_input.astype(jnp.float32).reshape(tokens, heads_here, P_SIZE)
    b_float = b_rows.astype(jnp.float32)
    c_float = c_rows.astype(jnp.float32)
    cot_float = mixer_cot.astype(jnp.float32).reshape(tokens, heads_here, P_SIZE)

    def stretch_of(inp, brow, crow, decay, state_in):
        return mixer_stretch(inp, brow, crow, decay, skip_gain, segment, before, state_in)

    cumulated = cumulate(decay_log)
    factor = carry_factor(cumulated, segment, before)
    summary = local_state(inputs, b_float, cumulated, segment)
    zero_state = jnp.zeros_like(summary)
    identity = (jnp.ones_like(factor), zero_state)
    state_in = entering_2((factor, summary), "seq", combine_states, identity, False)[1]
    (mixed, state_out), pull = jax.vjp(stretch_of, inputs, b_float, c_float, decay_log, state_in)
    adjoint_local = pull((cot_float, zero_state))[4]
    adjoint_out = entering_2((factor, adjoint_local), "seq", combine_states, identity, True)[1]
    grad_x, grad_b, grad_c, grad_decay, unused = pull((cot_float, adjoint_out))
    head_count = lax.axis_size("head")
    if head_count == 2:
        other_b, other_c = lax.ppermute((grad_b, grad_c), "head", [(0, 1), (1, 0)])
        grad_b, grad_c = grad_b + other_b, grad_c + other_c
    else:
        grad_b, grad_c = lax.psum((grad_b, grad_c), "head")
    mixer_out = mixed.reshape(tokens, heads_here * P_SIZE).astype(jnp.bfloat16)
    x_grad = grad_x.reshape(tokens, heads_here * P_SIZE).astype(jnp.bfloat16)
    return (mixer_out, x_grad, grad_b, grad_c, grad_decay)


def on_device(
    x_input,
    b_rows,
    c_rows,
    decay_log,
    skip_gain,
    doc_lengths,
    queries,
    attention_key_rows,
    values,
    mixer_cot,
    attention_output_cotangent,
):
    tokens = x_input.shape[0]
    offset = lax.axis_index("seq") * tokens
    total_len = tokens * lax.axis_size("seq")
    positions = offset + jnp.arange(tokens, dtype=jnp.int32)
    segment = doc_index(positions, doc_lengths)
    heads_here = skip_gain.shape[0]
    by_heads = heads_here % lax.axis_size("seq") == 0
    key_width = attention_key_rows.shape[1]
    state_width = b_rows.shape[1]
    seq_count = lax.axis_size("seq")
    if by_heads:
        own_width = heads_here // seq_count * P_SIZE

        def by_owner(a):
            return a.reshape(tokens, seq_count, own_width).transpose(1, 0, 2)

        def spread(a):
            return jnp.broadcast_to(a[None], (seq_count,) + a.shape)

        sent = jnp.concatenate(
            [by_owner(x_input), by_owner(mixer_cot), spread(b_rows), spread(c_rows)], axis=2
        )
        got = lax.all_to_all(sent, "seq", split_axis=0, concat_axis=0, tiled=True)
        x_all = got[:, :, :own_width].reshape(total_len, own_width)
        cot_all = got[:, :, own_width : 2 * own_width].reshape(total_len, own_width)
        b_all = got[:, :, 2 * own_width : 2 * own_width + state_width].reshape(total_len, -1)
        c_all = got[:, :, 2 * own_width + state_width :].reshape(total_len, -1)
        kv_sent = spread(jnp.concatenate([attention_key_rows, values], axis=1))
        gathered = lax.all_to_all(kv_sent, "seq", split_axis=0, concat_axis=0, tiled=True)
        gathered = gathered.reshape(total_len, 2 * key_width)
    else:
        gathered = lax.all_gather(
            jnp.concatenate([attention_key_rows, values], axis=1), "seq", axis=0, tiled=True
        )
    key_all, value_all = gathered[:, :key_width], gathered[:, key_width : 2 * key_width]
    if by_heads:
        mixed_own, x_grad_own, bc_part = mamba_by_heads(
            x_all, cot_all, b_all, c_all, decay_log, skip_gain, doc_lengths
        )
    else:
        mixer_out, x_grad, grad_b, grad_c, grad_decay = mamba_by_stretch(
            x_input, b_rows, c_rows, decay_log, skip_gain, doc_lengths, mixer_cot, segment, offset
        )
    logit_scale = 1.0 / math.sqrt(HEAD_SIZE)
    groups = attention_key_rows.shape[1] // HEAD_SIZE
    heads_per_group = queries.shape[1] // HEAD_SIZE // groups
    key_span = min(512, total_len)
    blocks = total_len // key_span
    last_pos = offset + tokens - 1
    query_grid = queries.reshape(tokens, groups, heads_per_group, HEAD_SIZE)
    cotangent_table = attention_output_cotangent.reshape(tokens, groups, heads_per_group, HEAD_SIZE)

    def block_view(number):
        anchor = number * key_span
        key_blk = lax.dynamic_slice_in_dim(key_all, anchor, key_span, 0).reshape(
            key_span, groups, HEAD_SIZE
        )
        value_blk = lax.dynamic_slice_in_dim(value_all, anchor, key_span, 0).reshape(
            key_span, groups, HEAD_SIZE
        )
        key_pos = anchor + jnp.arange(key_span, dtype=jnp.int32)
        allowed = (key_pos[None, :] <= positions[:, None]) & (
            doc_index(key_pos, doc_lengths)[None, :] == segment[:, None]
        )
        scores = (
            jnp.einsum("tgrd,kgd->grtk", query_grid, key_blk, preferred_element_type=jnp.float32)
            * logit_scale
        )
        scores = jnp.where(allowed[None, None], scores, big_negative)
        return (anchor, key_blk, value_blk, allowed, scores)

    def visit(number, carried, work):
        return lax.cond(
            number * key_span <= last_pos,
            lambda inner: work(number, inner),
            lambda inner: inner,
            carried,
        )

    def stats_step(number, carried):
        row_peak, row_total = carried
        anchor, key_blk, value_blk, allowed, scores = block_view(number)
        new_peak = jnp.maximum(row_peak, jnp.max(scores, axis=-1))
        fresh = jnp.sum(
            jnp.where(allowed[None, None], jnp.exp(scores - new_peak[..., None]), 0.0), axis=-1
        )
        return (new_peak, row_total * jnp.exp(row_peak - new_peak) + fresh)

    stat_shape = (groups, heads_per_group, tokens)
    row_peak, row_total = lax.fori_loop(
        0,
        blocks,
        lambda number, carried: visit(number, carried, stats_step),
        (jnp.full(stat_shape, big_negative, jnp.float32), jnp.zeros(stat_shape, jnp.float32)),
    )
    log_norm = row_peak + jnp.log(row_total)

    def output_step(number, totals):
        anchor, key_blk, value_blk, allowed, scores = block_view(number)
        weights = jnp.where(allowed[None, None], jnp.exp(scores - log_norm[..., None]), 0.0).astype(
            jnp.bfloat16
        )
        return totals + jnp.einsum(
            "grtk,kgd->tgrd", weights, value_blk, preferred_element_type=jnp.float32
        )

    attention_table = lax.fori_loop(
        0,
        blocks,
        lambda number, carried: visit(number, carried, output_step),
        jnp.zeros((tokens, groups, heads_per_group, HEAD_SIZE), jnp.float32),
    ).astype(jnp.bfloat16)
    row_products = jnp.einsum(
        "bkfh,bkfh->kfb", cotangent_table, attention_table, preferred_element_type=jnp.float32
    )

    def grad_terms(allowed, scores, value_blk):
        probs_full = jnp.where(allowed[None, None], jnp.exp(scores - log_norm[..., None]), 0.0)
        grad_prob = jnp.einsum(
            "tgrd,kgd->grtk", cotangent_table, value_blk, preferred_element_type=jnp.float32
        )
        grad_score = (probs_full * (grad_prob - row_products[..., None])).astype(jnp.bfloat16)
        return (probs_full.astype(jnp.bfloat16), grad_score)

    query_zero = jnp.zeros((tokens, groups, heads_per_group, HEAD_SIZE), jnp.float32)

    def full_step(number, carried):
        grad_query, term_key, term_value = carried
        anchor, key_blk, value_blk, allowed, scores = block_view(number)
        weights, grad_score = grad_terms(allowed, scores, value_blk)
        grad_query = grad_query + jnp.einsum(
            "grtk,kgd->tgrd", grad_score, key_blk, preferred_element_type=jnp.float32
        )
        key_part = jnp.einsum(
            "grtk,tgrd->kgd", grad_score, query_grid, preferred_element_type=jnp.float32
        ).reshape(key_span, groups * HEAD_SIZE)
        value_part = jnp.einsum(
            "grtk,tgrd->kgd", weights, cotangent_table, preferred_element_type=jnp.float32
        ).reshape(key_span, groups * HEAD_SIZE)
        term_key = lax.dynamic_update_slice_in_dim(term_key, key_part, anchor, 0)
        term_value = lax.dynamic_update_slice_in_dim(term_value, value_part, anchor, 0)
        return (grad_query, term_key, term_value)

    term_zero = jnp.zeros((total_len, groups * HEAD_SIZE), jnp.float32)
    grad_query, term_key, term_value = lax.fori_loop(
        0,
        blocks,
        lambda number, carried: visit(number, carried, full_step),
        (query_zero, term_zero, term_zero),
    )
    kv_terms = jnp.concatenate([term_key, term_value], axis=1).astype(jnp.bfloat16)
    kv_width = kv_terms.shape[1]
    if by_heads:
        sent = jnp.concatenate(
            [
                mixed_own.reshape(seq_count, tokens, own_width),
                x_grad_own.reshape(seq_count, tokens, own_width),
                bc_part.astype(jnp.bfloat16).reshape(seq_count, tokens, bc_part.shape[1]),
            ],
            axis=2,
        )
        got = lax.all_to_all(sent, "seq", split_axis=0, concat_axis=0, tiled=True)
        kv_got = lax.all_to_all(
            kv_terms.reshape(seq_count, tokens, kv_width),
            "seq",
            split_axis=0,
            concat_axis=0,
            tiled=True,
        )

        def from_owners(a):
            return a.transpose(1, 0, 2).reshape(tokens, seq_count * own_width)

        mixer_out = from_owners(got[:, :, :own_width])
        x_grad = from_owners(got[:, :, own_width : 2 * own_width])
        kv_total = jnp.sum(kv_got.astype(jnp.float32), axis=0)
        bc_sum = jnp.sum(got[:, :, 2 * own_width :].astype(jnp.float32), axis=0)
        grad_decay = bc_sum[:, 2 * state_width :].T
        bc_sum = bc_sum[:, : 2 * state_width]
        if lax.axis_size("head") == 2:
            bc_sum = bc_sum + lax.ppermute(bc_sum, "head", [(0, 1), (1, 0)])
        else:
            bc_sum = lax.psum(bc_sum, "head")
        grad_b, grad_c = bc_sum[:, :state_width], bc_sum[:, state_width:]
    else:
        kv_terms = lax.all_to_all(
            kv_terms.reshape(seq_count, tokens, kv_width),
            "seq",
            split_axis=0,
            concat_axis=0,
            tiled=True,
        )
        kv_total = jnp.sum(kv_terms.astype(jnp.float32), axis=0)
    key_gradient_total = kv_total[:, : groups * HEAD_SIZE]
    value_gradient_total = kv_total[:, groups * HEAD_SIZE :]
    attn_out = attention_table.reshape(tokens, groups * heads_per_group * HEAD_SIZE)
    q_grad = (
        (grad_query * logit_scale)
        .reshape(tokens, groups * heads_per_group * HEAD_SIZE)
        .astype(jnp.bfloat16)
    )
    key_gradient = (key_gradient_total * logit_scale).astype(jnp.bfloat16)
    value_gradient = value_gradient_total.astype(jnp.bfloat16)
    return (
        mixer_out,
        attn_out,
        x_grad,
        grad_b,
        grad_c,
        grad_decay,
        q_grad,
        key_gradient,
        value_gradient,
    )


def solution(mesh):
    placed = (
        P(("groups", "seq"), "head"),
        P(("groups", "seq"), None),
        P(("groups", "seq"), None),
        P(("groups", "head"), "seq"),
        P("head"),
        P("groups"),
        P(("groups", "seq"), "head"),
        P(("groups", "seq"), "head"),
        P(("groups", "seq"), "head"),
        P(("groups", "seq"), "head"),
        P(("groups", "seq"), "head"),
    )
    return jax.shard_map(
        on_device,
        mesh=mesh,
        in_specs=placed,
        out_specs=(
            P(("groups", "seq"), "head"),
            P(("groups", "seq"), "head"),
            P(("groups", "seq"), "head"),
            P(("groups", "seq"), None),
            P(("groups", "seq"), None),
            P(("groups", "head"), "seq"),
            P(("groups", "seq"), "head"),
            P(("groups", "seq"), "head"),
            P(("groups", "seq"), "head"),
        ),
        check_vma=False,
    )
```

```python
import math

import jax
import jax.numpy as jnp
from jax import lax
from jax.sharding import PartitionSpec as P

P_SIZE = 128
HEAD_SIZE = 128
TOK_SPAN = 128


precise = lax.Precision.HIGH
big_negative = -1e30


def entering_2(part, axis, combine, identity, reverse):
    count = lax.axis_size(axis)
    place = lax.axis_index(axis)
    ahead = count - 1 - place if reverse else place
    early = jax.tree.map(lambda a, e: jnp.zeros_like(a) + jnp.asarray(e, a.dtype), part, identity)
    span = part
    shift = 1
    while shift < count:
        if reverse:
            pairs = [(i, i - shift) for i in range(shift, count)]
        else:
            pairs = [(i, i + shift) for i in range(count - shift)]
        got = lax.ppermute(span, axis, pairs)
        have = ahead >= shift
        got = jax.tree.map(lambda g, e: jnp.where(have, g, jnp.asarray(e, g.dtype)), got, identity)
        early = combine(got, early)
        if 2 * shift < count:
            span = combine(got, span)
        shift *= 2
    return early


def doc_index(positions, lengths):
    ends = jnp.cumsum(lengths)
    return jnp.sum((positions[:, None] >= ends[None, :]).astype(jnp.int32), axis=1)


def cumulate(decay):
    return jnp.cumsum(decay, axis=1)


def local_state(inputs, b_float, cumulated, segment):
    weights = (
        jnp.exp(cumulated[:, -1:] - cumulated)
        * (segment == segment[-1]).astype(inputs.dtype)[None, :]
    )
    return jnp.einsum("hs,sn,shp->hnp", weights, b_float, inputs, precision=precise)


def carry_factor(cumulated, segment, before):
    return jnp.exp(cumulated[:, -1]) * (segment[-1] == before).astype(cumulated.dtype)


def mixer_stretch(inputs, b_float, c_float, decay, gains, segment, before, state_in):
    cumulated = cumulate(decay)
    width = inputs.shape[0]
    steps = jnp.arange(width)
    allowed = (steps[:, None] >= steps[None, :]) & (segment[:, None] == segment[None, :])
    gaps = jnp.where(allowed[None], cumulated[:, :, None] - cumulated[:, None, :], big_negative)
    kernel = jnp.exp(gaps) * jnp.dot(c_float, b_float.T, precision=precise)[None]
    inner = jnp.einsum("hts,shp->thp", kernel, inputs, precision=precise)
    keeps = (segment == before).astype(inputs.dtype)
    entering = jnp.einsum("tn,hnp->thp", c_float, state_in, precision=precise)
    reach = jnp.exp(cumulated).T * keeps[:, None]
    outputs = inner + reach[:, :, None] * entering + gains[None, :, None] * inputs
    factor = carry_factor(cumulated, segment, before)
    state_out = factor[:, None, None] * state_in + local_state(inputs, b_float, cumulated, segment)
    return (outputs, state_out)


def combine_states(earlier, later):
    return (earlier[0] * later[0], later[0][:, None, None] * earlier[1] + later[1])


def mixer_whole(inputs, b_float, c_float, decay, gains, segment):
    width = TOK_SPAN
    count = inputs.shape[0] // width
    heads = inputs.shape[1]
    inp = inputs.reshape(count, width, heads, P_SIZE)
    b_blocks = b_float.reshape(count, width, -1)
    c_blocks = c_float.reshape(count, width, -1)
    dec = decay.reshape(heads, count, width).transpose(1, 0, 2)
    seg = segment.reshape(count, width)
    befores = jnp.concatenate([jnp.full((1,), -1, seg.dtype), seg[:-1, -1]])
    cumulated = jnp.cumsum(dec, axis=2)
    factor = jax.vmap(carry_factor)(cumulated, seg, befores)
    summary = jax.vmap(local_state)(inp, b_blocks, cumulated, seg)

    columns = jnp.arange(count)[:, None]
    row = jnp.zeros((count, heads), factor.dtype)
    rows = [row]
    for k in range(1, count):
        row = jnp.where(columns < k - 1, row * factor[k - 1][None, :], (columns == k - 1).astype(factor.dtype))
        rows.append(row)
    reach = jnp.stack(rows)
    state_in = jnp.einsum("kjh,jhnp->khnp", reach, summary, precision=precise)

    def stretch(i, brow, crow, d, sg, bf, st):
        return mixer_stretch(i, brow, crow, d, gains, sg, bf, st)[0]

    outputs = jax.vmap(stretch)(inp, b_blocks, c_blocks, dec, seg, befores, state_in)
    return outputs.reshape(count * width, heads, P_SIZE)


def mamba_by_heads(x_all, cot_all, b_all, c_all, decay_log, skip_gain, doc_lengths):
    seq_count = lax.axis_size("seq")
    place = lax.axis_index("seq")
    heads_here = skip_gain.shape[0]
    own = heads_here // seq_count
    total = x_all.shape[0]
    decay = lax.all_to_all(decay_log, "seq", split_axis=0, concat_axis=1, tiled=True)
    gains = lax.dynamic_slice_in_dim(skip_gain, place * own, own)
    segment = doc_index(jnp.arange(total, dtype=jnp.int32), doc_lengths)
    inputs = x_all.astype(jnp.float32).reshape(total, own, P_SIZE)
    cot = cot_all.astype(jnp.float32).reshape(total, own, P_SIZE)

    def whole_of(i, brow, crow, d):
        return mixer_whole(i, brow, crow, d, gains, segment)

    mixed, pull = jax.vjp(
        whole_of, inputs, b_all.astype(jnp.float32), c_all.astype(jnp.float32), decay
    )
    grad_x, grad_b, grad_c, grad_decay = pull(cot)
    decay_cols = lax.dynamic_update_slice_in_dim(
        jnp.zeros((total, heads_here), jnp.float32), grad_decay.T, place * own, 1
    )
    return (
        mixed.reshape(total, own * P_SIZE).astype(jnp.bfloat16),
        grad_x.reshape(total, own * P_SIZE).astype(jnp.bfloat16),
        jnp.concatenate([grad_b, grad_c, decay_cols], axis=1),
    )


def mamba_by_stretch(
    x_input, b_rows, c_rows, decay_log, skip_gain, doc_lengths, mixer_cot, segment, offset
):
    tokens = x_input.shape[0]
    previous = doc_index(jnp.reshape(offset - 1, (1,)), doc_lengths)[0]
    before = jnp.where(offset > 0, previous, -1)
    heads_here = skip_gain.shape[0]
    inputs = x_input.astype(jnp.float32).reshape(tokens, heads_here, P_SIZE)
    b_float = b_rows.astype(jnp.float32)
    c_float = c_rows.astype(jnp.float32)
    cot_float = mixer_cot.astype(jnp.float32).reshape(tokens, heads_here, P_SIZE)

    def stretch_of(inp, brow, crow, decay, state_in):
        return mixer_stretch(inp, brow, crow, decay, skip_gain, segment, before, state_in)

    cumulated = cumulate(decay_log)
    factor = carry_factor(cumulated, segment, before)
    summary = local_state(inputs, b_float, cumulated, segment)
    zero_state = jnp.zeros_like(summary)
    identity = (jnp.ones_like(factor), zero_state)
    state_in = entering_2((factor, summary), "seq", combine_states, identity, False)[1]
    (mixed, state_out), pull = jax.vjp(stretch_of, inputs, b_float, c_float, decay_log, state_in)
    adjoint_local = pull((cot_float, zero_state))[4]
    adjoint_out = entering_2((factor, adjoint_local), "seq", combine_states, identity, True)[1]
    grad_x, grad_b, grad_c, grad_decay, unused = pull((cot_float, adjoint_out))
    head_count = lax.axis_size("head")
    if head_count == 2:
        other_b, other_c = lax.ppermute((grad_b, grad_c), "head", [(0, 1), (1, 0)])
        grad_b, grad_c = grad_b + other_b, grad_c + other_c
    else:
        grad_b, grad_c = lax.psum((grad_b, grad_c), "head")
    mixer_out = mixed.reshape(tokens, heads_here * P_SIZE).astype(jnp.bfloat16)
    x_grad = grad_x.reshape(tokens, heads_here * P_SIZE).astype(jnp.bfloat16)
    return (mixer_out, x_grad, grad_b, grad_c, grad_decay)


def on_device(
    x_input,
    b_rows,
    c_rows,
    decay_log,
    skip_gain,
    doc_lengths,
    queries,
    attention_key_rows,
    values,
    mixer_cot,
    attention_output_cotangent,
):
    tokens = x_input.shape[0]
    offset = lax.axis_index("seq") * tokens
    total_len = tokens * lax.axis_size("seq")
    positions = offset + jnp.arange(tokens, dtype=jnp.int32)
    segment = doc_index(positions, doc_lengths)
    heads_here = skip_gain.shape[0]
    by_heads = heads_here % lax.axis_size("seq") == 0
    key_width = attention_key_rows.shape[1]
    state_width = b_rows.shape[1]
    seq_count = lax.axis_size("seq")
    if by_heads:
        own_width = heads_here // seq_count * P_SIZE

        def by_owner(a):
            return a.reshape(tokens, seq_count, own_width).transpose(1, 0, 2)

        def spread(a):
            return jnp.broadcast_to(a[None], (seq_count,) + a.shape)

        sent = jnp.concatenate(
            [by_owner(x_input), by_owner(mixer_cot), spread(b_rows), spread(c_rows)], axis=2
        )
        got = lax.all_to_all(sent, "seq", split_axis=0, concat_axis=0, tiled=True)
        x_all = got[:, :, :own_width].reshape(total_len, own_width)
        cot_all = got[:, :, own_width : 2 * own_width].reshape(total_len, own_width)
        b_all = got[:, :, 2 * own_width : 2 * own_width + state_width].reshape(total_len, -1)
        c_all = got[:, :, 2 * own_width + state_width :].reshape(total_len, -1)
        kv_sent = spread(jnp.concatenate([attention_key_rows, values], axis=1))
        gathered = lax.all_to_all(kv_sent, "seq", split_axis=0, concat_axis=0, tiled=True)
        gathered = gathered.reshape(total_len, 2 * key_width)
    else:
        gathered = lax.all_gather(
            jnp.concatenate([attention_key_rows, values], axis=1), "seq", axis=0, tiled=True
        )
    key_all, value_all = gathered[:, :key_width], gathered[:, key_width : 2 * key_width]
    if by_heads:
        mixed_own, x_grad_own, bc_part = mamba_by_heads(
            x_all, cot_all, b_all, c_all, decay_log, skip_gain, doc_lengths
        )
    else:
        mixer_out, x_grad, grad_b, grad_c, grad_decay = mamba_by_stretch(
            x_input, b_rows, c_rows, decay_log, skip_gain, doc_lengths, mixer_cot, segment, offset
        )
    logit_scale = 1.0 / math.sqrt(HEAD_SIZE)
    groups = attention_key_rows.shape[1] // HEAD_SIZE
    heads_per_group = queries.shape[1] // HEAD_SIZE // groups
    key_span = min(512, total_len)
    blocks = total_len // key_span
    last_pos = offset + tokens - 1
    query_grid = queries.reshape(tokens, groups, heads_per_group, HEAD_SIZE)
    cotangent_table = attention_output_cotangent.reshape(tokens, groups, heads_per_group, HEAD_SIZE)

    def block_view(number):
        anchor = number * key_span
        key_blk = lax.dynamic_slice_in_dim(key_all, anchor, key_span, 0).reshape(
            key_span, groups, HEAD_SIZE
        )
        value_blk = lax.dynamic_slice_in_dim(value_all, anchor, key_span, 0).reshape(
            key_span, groups, HEAD_SIZE
        )
        key_pos = anchor + jnp.arange(key_span, dtype=jnp.int32)
        allowed = (key_pos[None, :] <= positions[:, None]) & (
            doc_index(key_pos, doc_lengths)[None, :] == segment[:, None]
        )
        scores = (
            jnp.einsum("tgrd,kgd->grtk", query_grid, key_blk, preferred_element_type=jnp.float32)
            * logit_scale
        )
        scores = jnp.where(allowed[None, None], scores, big_negative)
        return (anchor, key_blk, value_blk, allowed, scores)

    def visit(number, carried, work):
        return lax.cond(
            number * key_span <= last_pos,
            lambda inner: work(number, inner),
            lambda inner: inner,
            carried,
        )

    def stats_step(number, carried):
        row_peak, row_total = carried
        anchor, key_blk, value_blk, allowed, scores = block_view(number)
        new_peak = jnp.maximum(row_peak, jnp.max(scores, axis=-1))
        fresh = jnp.sum(
            jnp.where(allowed[None, None], jnp.exp(scores - new_peak[..., None]), 0.0), axis=-1
        )
        return (new_peak, row_total * jnp.exp(row_peak - new_peak) + fresh)

    stat_shape = (groups, heads_per_group, tokens)
    row_peak, row_total = lax.fori_loop(
        0,
        blocks,
        lambda number, carried: visit(number, carried, stats_step),
        (jnp.full(stat_shape, big_negative, jnp.float32), jnp.zeros(stat_shape, jnp.float32)),
    )
    log_norm = row_peak + jnp.log(row_total)

    def output_step(number, totals):
        anchor, key_blk, value_blk, allowed, scores = block_view(number)
        weights = jnp.where(allowed[None, None], jnp.exp(scores - log_norm[..., None]), 0.0).astype(
            jnp.bfloat16
        )
        return totals + jnp.einsum(
            "grtk,kgd->tgrd", weights, value_blk, preferred_element_type=jnp.float32
        )

    attention_table = lax.fori_loop(
        0,
        blocks,
        lambda number, carried: visit(number, carried, output_step),
        jnp.zeros((tokens, groups, heads_per_group, HEAD_SIZE), jnp.float32),
    ).astype(jnp.bfloat16)
    row_products = jnp.einsum(
        "bkfh,bkfh->kfb", cotangent_table, attention_table, preferred_element_type=jnp.float32
    )

    def grad_terms(allowed, scores, value_blk):
        probs_full = jnp.where(allowed[None, None], jnp.exp(scores - log_norm[..., None]), 0.0)
        grad_prob = jnp.einsum(
            "tgrd,kgd->grtk", cotangent_table, value_blk, preferred_element_type=jnp.float32
        )
        grad_score = (probs_full * (grad_prob - row_products[..., None])).astype(jnp.bfloat16)
        return (probs_full.astype(jnp.bfloat16), grad_score)

    query_zero = jnp.zeros((tokens, groups, heads_per_group, HEAD_SIZE), jnp.float32)

    def full_step(number, carried):
        grad_query, term_key, term_value = carried
        anchor, key_blk, value_blk, allowed, scores = block_view(number)
        weights, grad_score = grad_terms(allowed, scores, value_blk)
        grad_query = grad_query + jnp.einsum(
            "grtk,kgd->tgrd", grad_score, key_blk, preferred_element_type=jnp.float32
        )
        key_part = jnp.einsum(
            "grtk,tgrd->kgd", grad_score, query_grid, preferred_element_type=jnp.float32
        ).reshape(key_span, groups * HEAD_SIZE)
        value_part = jnp.einsum(
            "grtk,tgrd->kgd", weights, cotangent_table, preferred_element_type=jnp.float32
        ).reshape(key_span, groups * HEAD_SIZE)
        term_key = lax.dynamic_update_slice_in_dim(term_key, key_part, anchor, 0)
        term_value = lax.dynamic_update_slice_in_dim(term_value, value_part, anchor, 0)
        return (grad_query, term_key, term_value)

    term_zero = jnp.zeros((total_len, groups * HEAD_SIZE), jnp.float32)
    grad_query, term_key, term_value = lax.fori_loop(
        0,
        blocks,
        lambda number, carried: visit(number, carried, full_step),
        (query_zero, term_zero, term_zero),
    )
    kv_terms = jnp.concatenate([term_key, term_value], axis=1).astype(jnp.bfloat16)
    kv_width = kv_terms.shape[1]
    if by_heads:
        sent = jnp.concatenate(
            [
                mixed_own.reshape(seq_count, tokens, own_width),
                x_grad_own.reshape(seq_count, tokens, own_width),
                bc_part.astype(jnp.bfloat16).reshape(seq_count, tokens, bc_part.shape[1]),
            ],
            axis=2,
        )
        got = lax.all_to_all(sent, "seq", split_axis=0, concat_axis=0, tiled=True)
        kv_got = lax.all_to_all(
            kv_terms.reshape(seq_count, tokens, kv_width),
            "seq",
            split_axis=0,
            concat_axis=0,
            tiled=True,
        )

        def from_owners(a):
            return a.transpose(1, 0, 2).reshape(tokens, seq_count * own_width)

        mixer_out = from_owners(got[:, :, :own_width])
        x_grad = from_owners(got[:, :, own_width : 2 * own_width])
        kv_total = jnp.sum(kv_got.astype(jnp.float32), axis=0)
        bc_sum = jnp.sum(got[:, :, 2 * own_width :].astype(jnp.float32), axis=0)
        grad_decay = bc_sum[:, 2 * state_width :].T
        bc_sum = bc_sum[:, : 2 * state_width]
        if lax.axis_size("head") == 2:
            bc_sum = bc_sum + lax.ppermute(bc_sum, "head", [(0, 1), (1, 0)])
        else:
            bc_sum = lax.psum(bc_sum, "head")
        grad_b, grad_c = bc_sum[:, :state_width], bc_sum[:, state_width:]
    else:
        kv_terms = lax.all_to_all(
            kv_terms.reshape(seq_count, tokens, kv_width),
            "seq",
            split_axis=0,
            concat_axis=0,
            tiled=True,
        )
        kv_total = jnp.sum(kv_terms.astype(jnp.float32), axis=0)
    key_gradient_total = kv_total[:, : groups * HEAD_SIZE]
    value_gradient_total = kv_total[:, groups * HEAD_SIZE :]
    attn_out = attention_table.reshape(tokens, groups * heads_per_group * HEAD_SIZE)
    q_grad = (
        (grad_query * logit_scale)
        .reshape(tokens, groups * heads_per_group * HEAD_SIZE)
        .astype(jnp.bfloat16)
    )
    key_gradient = (key_gradient_total * logit_scale).astype(jnp.bfloat16)
    value_gradient = value_gradient_total.astype(jnp.bfloat16)
    return (
        mixer_out,
        attn_out,
        x_grad,
        grad_b,
        grad_c,
        grad_decay,
        q_grad,
        key_gradient,
        value_gradient,
    )


def solution(mesh):
    placed = (
        P(("groups", "seq"), "head"),
        P(("groups", "seq"), None),
        P(("groups", "seq"), None),
        P(("groups", "head"), "seq"),
        P("head"),
        P("groups"),
        P(("groups", "seq"), "head"),
        P(("groups", "seq"), "head"),
        P(("groups", "seq"), "head"),
        P(("groups", "seq"), "head"),
        P(("groups", "seq"), "head"),
    )
    return jax.shard_map(
        on_device,
        mesh=mesh,
        in_specs=placed,
        out_specs=(
            P(("groups", "seq"), "head"),
            P(("groups", "seq"), "head"),
            P(("groups", "seq"), "head"),
            P(("groups", "seq"), None),
            P(("groups", "seq"), None),
            P(("groups", "head"), "seq"),
            P(("groups", "seq"), "head"),
            P(("groups", "seq"), "head"),
            P(("groups", "seq"), "head"),
        ),
        check_vma=False,
    )
```

```python
import math

import jax
import jax.numpy as jnp
from jax import lax
from jax.sharding import PartitionSpec as P

P_SIZE = 128
HEAD_SIZE = 128
TOK_SPAN = 128


precise = lax.Precision.HIGH
big_negative = -1e30


def entering_2(part, axis, combine, identity, reverse):
    count = lax.axis_size(axis)
    place = lax.axis_index(axis)
    ahead = count - 1 - place if reverse else place
    early = jax.tree.map(lambda a, e: jnp.zeros_like(a) + jnp.asarray(e, a.dtype), part, identity)
    span = part
    shift = 1
    while shift < count:
        if reverse:
            pairs = [(i, i - shift) for i in range(shift, count)]
        else:
            pairs = [(i, i + shift) for i in range(count - shift)]
        got = lax.ppermute(span, axis, pairs)
        have = ahead >= shift
        got = jax.tree.map(lambda g, e: jnp.where(have, g, jnp.asarray(e, g.dtype)), got, identity)
        early = combine(got, early)
        if 2 * shift < count:
            span = combine(got, span)
        shift *= 2
    return early


def doc_index(positions, lengths):
    ends = jnp.cumsum(lengths)
    return jnp.sum((positions[:, None] >= ends[None, :]).astype(jnp.int32), axis=1)


def cumulate(decay):
    return jnp.cumsum(decay, axis=1)


def local_state(inputs, b_float, cumulated, segment):
    weights = (
        jnp.exp(cumulated[:, -1:] - cumulated)
        * (segment == segment[-1]).astype(inputs.dtype)[None, :]
    )
    return jnp.einsum("hs,sn,shp->hnp", weights, b_float, inputs, precision=precise)


def carry_factor(cumulated, segment, before):
    return jnp.exp(cumulated[:, -1]) * (segment[-1] == before).astype(cumulated.dtype)


def mixer_stretch(inputs, b_float, c_float, decay, gains, segment, before, state_in):
    cumulated = cumulate(decay)
    width = inputs.shape[0]
    steps = jnp.arange(width)
    allowed = (steps[:, None] >= steps[None, :]) & (segment[:, None] == segment[None, :])
    gaps = jnp.where(allowed[None], cumulated[:, :, None] - cumulated[:, None, :], big_negative)
    kernel = jnp.exp(gaps) * jnp.dot(c_float, b_float.T, precision=precise)[None]
    inner = jnp.einsum("hts,shp->thp", kernel, inputs, precision=precise)
    keeps = (segment == before).astype(inputs.dtype)
    entering = jnp.einsum("tn,hnp->thp", c_float, state_in, precision=precise)
    reach = jnp.exp(cumulated).T * keeps[:, None]
    outputs = inner + reach[:, :, None] * entering + gains[None, :, None] * inputs
    factor = carry_factor(cumulated, segment, before)
    state_out = factor[:, None, None] * state_in + local_state(inputs, b_float, cumulated, segment)
    return (outputs, state_out)


def combine_states(earlier, later):
    return (earlier[0] * later[0], later[0][:, None, None] * earlier[1] + later[1])


def mixer_whole(inputs, b_float, c_float, decay, gains, segment):
    width = TOK_SPAN
    count = inputs.shape[0] // width
    heads = inputs.shape[1]
    inp = inputs.reshape(count, width, heads, P_SIZE)
    b_blocks = b_float.reshape(count, width, -1)
    c_blocks = c_float.reshape(count, width, -1)
    dec = decay.reshape(heads, count, width).transpose(1, 0, 2)
    seg = segment.reshape(count, width)
    befores = jnp.concatenate([jnp.full((1,), -1, seg.dtype), seg[:-1, -1]])
    cumulated = jnp.cumsum(dec, axis=2)
    factor = jax.vmap(carry_factor)(cumulated, seg, befores)
    summary = jax.vmap(local_state)(inp, b_blocks, cumulated, seg)

    columns = jnp.arange(count)[:, None]
    row = jnp.zeros((count, heads), factor.dtype)
    rows = [row]
    for k in range(1, count):
        row = jnp.where(columns < k - 1, row * factor[k - 1][None, :], (columns == k - 1).astype(factor.dtype))
        rows.append(row)
    reach = jnp.stack(rows)
    state_in = jnp.einsum("kjh,jhnp->khnp", reach, summary, precision=precise)

    def stretch(i, brow, crow, d, sg, bf, st):
        return mixer_stretch(i, brow, crow, d, gains, sg, bf, st)[0]

    outputs = jax.vmap(stretch)(inp, b_blocks, c_blocks, dec, seg, befores, state_in)
    return outputs.reshape(count * width, heads, P_SIZE)


def mamba_by_heads(x_all, cot_all, b_all, c_all, decay, skip_gain, doc_lengths):
    seq_count = lax.axis_size("seq")
    place = lax.axis_index("seq")
    heads_here = skip_gain.shape[0]
    own = heads_here // seq_count
    total = x_all.shape[0]
    gains = lax.dynamic_slice_in_dim(skip_gain, place * own, own)
    segment = doc_index(jnp.arange(total, dtype=jnp.int32), doc_lengths)
    inputs = x_all.astype(jnp.float32).reshape(total, own, P_SIZE)
    cot = cot_all.astype(jnp.float32).reshape(total, own, P_SIZE)

    def whole_of(i, brow, crow, d):
        return mixer_whole(i, brow, crow, d, gains, segment)

    mixed, pull = jax.vjp(
        whole_of, inputs, b_all.astype(jnp.float32), c_all.astype(jnp.float32), decay
    )
    grad_x, grad_b, grad_c, grad_decay = pull(cot)
    decay_cols = lax.dynamic_update_slice_in_dim(
        jnp.zeros((total, heads_here), jnp.float32), grad_decay.T, place * own, 1
    )
    return (
        mixed.reshape(total, own * P_SIZE).astype(jnp.bfloat16),
        grad_x.reshape(total, own * P_SIZE).astype(jnp.bfloat16),
        jnp.concatenate([grad_b, grad_c, decay_cols], axis=1),
    )


def mamba_by_stretch(
    x_input, b_rows, c_rows, decay_log, skip_gain, doc_lengths, mixer_cot, segment, offset
):
    tokens = x_input.shape[0]
    previous = doc_index(jnp.reshape(offset - 1, (1,)), doc_lengths)[0]
    before = jnp.where(offset > 0, previous, -1)
    heads_here = skip_gain.shape[0]
    inputs = x_input.astype(jnp.float32).reshape(tokens, heads_here, P_SIZE)
    b_float = b_rows.astype(jnp.float32)
    c_float = c_rows.astype(jnp.float32)
    cot_float = mixer_cot.astype(jnp.float32).reshape(tokens, heads_here, P_SIZE)

    def stretch_of(inp, brow, crow, decay, state_in):
        return mixer_stretch(inp, brow, crow, decay, skip_gain, segment, before, state_in)

    cumulated = cumulate(decay_log)
    factor = carry_factor(cumulated, segment, before)
    summary = local_state(inputs, b_float, cumulated, segment)
    zero_state = jnp.zeros_like(summary)
    identity = (jnp.ones_like(factor), zero_state)
    state_in = entering_2((factor, summary), "seq", combine_states, identity, False)[1]
    (mixed, state_out), pull = jax.vjp(stretch_of, inputs, b_float, c_float, decay_log, state_in)
    adjoint_local = pull((cot_float, zero_state))[4]
    adjoint_out = entering_2((factor, adjoint_local), "seq", combine_states, identity, True)[1]
    grad_x, grad_b, grad_c, grad_decay, unused = pull((cot_float, adjoint_out))
    head_count = lax.axis_size("head")
    if head_count == 2:
        other_b, other_c = lax.ppermute((grad_b, grad_c), "head", [(0, 1), (1, 0)])
        grad_b, grad_c = grad_b + other_b, grad_c + other_c
    else:
        grad_b, grad_c = lax.psum((grad_b, grad_c), "head")
    mixer_out = mixed.reshape(tokens, heads_here * P_SIZE).astype(jnp.bfloat16)
    x_grad = grad_x.reshape(tokens, heads_here * P_SIZE).astype(jnp.bfloat16)
    return (mixer_out, x_grad, grad_b, grad_c, grad_decay)


def on_device(
    x_input,
    b_rows,
    c_rows,
    decay_log,
    skip_gain,
    doc_lengths,
    queries,
    attention_key_rows,
    values,
    mixer_cot,
    attention_output_cotangent,
):
    tokens = x_input.shape[0]
    offset = lax.axis_index("seq") * tokens
    total_len = tokens * lax.axis_size("seq")
    positions = offset + jnp.arange(tokens, dtype=jnp.int32)
    segment = doc_index(positions, doc_lengths)
    heads_here = skip_gain.shape[0]
    by_heads = heads_here % lax.axis_size("seq") == 0
    key_width = attention_key_rows.shape[1]
    state_width = b_rows.shape[1]
    seq_count = lax.axis_size("seq")
    if by_heads:
        own_width = heads_here // seq_count * P_SIZE

        def by_owner(a):
            return a.reshape(tokens, seq_count, own_width).transpose(1, 0, 2)

        def spread(a):
            return jnp.broadcast_to(a[None], (seq_count,) + a.shape)

        decay_parts = []
        rest = decay_log
        for scale in (2.0**8, 2.0**16, 2.0**24, 2.0**32):
            part = jnp.round(rest * scale) / scale
            rest = rest - part
            decay_parts.append(part)
        decay_sent = jnp.concatenate(decay_parts, axis=0).astype(jnp.bfloat16)
        decay_sent = decay_sent.reshape(len(decay_parts), seq_count, heads_here // seq_count, tokens)
        decay_sent = decay_sent.transpose(1, 3, 0, 2).reshape(seq_count, tokens, -1)
        sent = jnp.concatenate(
            [
                by_owner(x_input),
                by_owner(mixer_cot),
                spread(b_rows),
                spread(c_rows),
                decay_sent,
            ],
            axis=2,
        )
        got = lax.all_to_all(sent, "seq", split_axis=0, concat_axis=0, tiled=True)
        x_all = got[:, :, :own_width].reshape(total_len, own_width)
        cot_all = got[:, :, own_width : 2 * own_width].reshape(total_len, own_width)
        b_all = got[:, :, 2 * own_width : 2 * own_width + state_width].reshape(total_len, -1)
        c_all = got[:, :, 2 * own_width + state_width : 2 * own_width + 2 * state_width]
        c_all = c_all.reshape(total_len, -1)
        decay_got = got[:, :, 2 * own_width + 2 * state_width :].astype(jnp.float32)
        decay_got = decay_got.reshape(total_len, 4, heads_here // seq_count)
        decay_own = ((decay_got[:, 0] + decay_got[:, 1]) + decay_got[:, 2]) + decay_got[:, 3]
        decay_own = decay_own.T
        kv_sent = spread(jnp.concatenate([attention_key_rows, values], axis=1))
        gathered = lax.all_to_all(kv_sent, "seq", split_axis=0, concat_axis=0, tiled=True)
        gathered = gathered.reshape(total_len, 2 * key_width)
    else:
        gathered = lax.all_gather(
            jnp.concatenate([attention_key_rows, values], axis=1), "seq", axis=0, tiled=True
        )
    key_all, value_all = gathered[:, :key_width], gathered[:, key_width : 2 * key_width]
    if by_heads:
        mixed_own, x_grad_own, bc_part = mamba_by_heads(
            x_all, cot_all, b_all, c_all, decay_own, skip_gain, doc_lengths
        )
    else:
        mixer_out, x_grad, grad_b, grad_c, grad_decay = mamba_by_stretch(
            x_input, b_rows, c_rows, decay_log, skip_gain, doc_lengths, mixer_cot, segment, offset
        )
    logit_scale = 1.0 / math.sqrt(HEAD_SIZE)
    groups = attention_key_rows.shape[1] // HEAD_SIZE
    heads_per_group = queries.shape[1] // HEAD_SIZE // groups
    key_span = min(512, total_len)
    blocks = total_len // key_span
    last_pos = offset + tokens - 1
    query_grid = queries.reshape(tokens, groups, heads_per_group, HEAD_SIZE)
    cotangent_table = attention_output_cotangent.reshape(tokens, groups, heads_per_group, HEAD_SIZE)

    def block_view(number):
        anchor = number * key_span
        key_blk = lax.dynamic_slice_in_dim(key_all, anchor, key_span, 0).reshape(
            key_span, groups, HEAD_SIZE
        )
        value_blk = lax.dynamic_slice_in_dim(value_all, anchor, key_span, 0).reshape(
            key_span, groups, HEAD_SIZE
        )
        key_pos = anchor + jnp.arange(key_span, dtype=jnp.int32)
        allowed = (key_pos[None, :] <= positions[:, None]) & (
            doc_index(key_pos, doc_lengths)[None, :] == segment[:, None]
        )
        scores = (
            jnp.einsum("tgrd,kgd->grtk", query_grid, key_blk, preferred_element_type=jnp.float32)
            * logit_scale
        )
        scores = jnp.where(allowed[None, None], scores, big_negative)
        return (anchor, key_blk, value_blk, allowed, scores)

    def visit(number, carried, work):
        return lax.cond(
            number * key_span <= last_pos,
            lambda inner: work(number, inner),
            lambda inner: inner,
            carried,
        )

    def stats_step(number, carried):
        row_peak, row_total = carried
        anchor, key_blk, value_blk, allowed, scores = block_view(number)
        new_peak = jnp.maximum(row_peak, jnp.max(scores, axis=-1))
        fresh = jnp.sum(
            jnp.where(allowed[None, None], jnp.exp(scores - new_peak[..., None]), 0.0), axis=-1
        )
        return (new_peak, row_total * jnp.exp(row_peak - new_peak) + fresh)

    stat_shape = (groups, heads_per_group, tokens)
    row_peak, row_total = lax.fori_loop(
        0,
        blocks,
        lambda number, carried: visit(number, carried, stats_step),
        (jnp.full(stat_shape, big_negative, jnp.float32), jnp.zeros(stat_shape, jnp.float32)),
    )
    log_norm = row_peak + jnp.log(row_total)

    def output_step(number, totals):
        anchor, key_blk, value_blk, allowed, scores = block_view(number)
        weights = jnp.where(allowed[None, None], jnp.exp(scores - log_norm[..., None]), 0.0).astype(
            jnp.bfloat16
        )
        return totals + jnp.einsum(
            "grtk,kgd->tgrd", weights, value_blk, preferred_element_type=jnp.float32
        )

    attention_table = lax.fori_loop(
        0,
        blocks,
        lambda number, carried: visit(number, carried, output_step),
        jnp.zeros((tokens, groups, heads_per_group, HEAD_SIZE), jnp.float32),
    ).astype(jnp.bfloat16)
    row_products = jnp.einsum(
        "bkfh,bkfh->kfb", cotangent_table, attention_table, preferred_element_type=jnp.float32
    )

    def grad_terms(allowed, scores, value_blk):
        probs_full = jnp.where(allowed[None, None], jnp.exp(scores - log_norm[..., None]), 0.0)
        grad_prob = jnp.einsum(
            "tgrd,kgd->grtk", cotangent_table, value_blk, preferred_element_type=jnp.float32
        )
        grad_score = (probs_full * (grad_prob - row_products[..., None])).astype(jnp.bfloat16)
        return (probs_full.astype(jnp.bfloat16), grad_score)

    query_zero = jnp.zeros((tokens, groups, heads_per_group, HEAD_SIZE), jnp.float32)

    def full_step(number, carried):
        grad_query, term_key, term_value = carried
        anchor, key_blk, value_blk, allowed, scores = block_view(number)
        weights, grad_score = grad_terms(allowed, scores, value_blk)
        grad_query = grad_query + jnp.einsum(
            "grtk,kgd->tgrd", grad_score, key_blk, preferred_element_type=jnp.float32
        )
        key_part = jnp.einsum(
            "grtk,tgrd->kgd", grad_score, query_grid, preferred_element_type=jnp.float32
        ).reshape(key_span, groups * HEAD_SIZE)
        value_part = jnp.einsum(
            "grtk,tgrd->kgd", weights, cotangent_table, preferred_element_type=jnp.float32
        ).reshape(key_span, groups * HEAD_SIZE)
        term_key = lax.dynamic_update_slice_in_dim(term_key, key_part, anchor, 0)
        term_value = lax.dynamic_update_slice_in_dim(term_value, value_part, anchor, 0)
        return (grad_query, term_key, term_value)

    term_zero = jnp.zeros((total_len, groups * HEAD_SIZE), jnp.float32)
    grad_query, term_key, term_value = lax.fori_loop(
        0,
        blocks,
        lambda number, carried: visit(number, carried, full_step),
        (query_zero, term_zero, term_zero),
    )
    kv_terms = jnp.concatenate([term_key, term_value], axis=1).astype(jnp.bfloat16)
    kv_width = kv_terms.shape[1]
    if by_heads:
        sent = jnp.concatenate(
            [
                mixed_own.reshape(seq_count, tokens, own_width),
                x_grad_own.reshape(seq_count, tokens, own_width),
                bc_part.astype(jnp.bfloat16).reshape(seq_count, tokens, bc_part.shape[1]),
            ],
            axis=2,
        )
        got = lax.all_to_all(sent, "seq", split_axis=0, concat_axis=0, tiled=True)
        kv_got = lax.all_to_all(
            kv_terms.reshape(seq_count, tokens, kv_width),
            "seq",
            split_axis=0,
            concat_axis=0,
            tiled=True,
        )

        def from_owners(a):
            return a.transpose(1, 0, 2).reshape(tokens, seq_count * own_width)

        mixer_out = from_owners(got[:, :, :own_width])
        x_grad = from_owners(got[:, :, own_width : 2 * own_width])
        kv_total = jnp.sum(kv_got.astype(jnp.float32), axis=0)
        bc_sum = jnp.sum(got[:, :, 2 * own_width :].astype(jnp.float32), axis=0)
        grad_decay = bc_sum[:, 2 * state_width :].T
        bc_sum = bc_sum[:, : 2 * state_width]
        if lax.axis_size("head") == 2:
            bc_sum = bc_sum + lax.ppermute(bc_sum, "head", [(0, 1), (1, 0)])
        else:
            bc_sum = lax.psum(bc_sum, "head")
        grad_b, grad_c = bc_sum[:, :state_width], bc_sum[:, state_width:]
    else:
        kv_terms = lax.all_to_all(
            kv_terms.reshape(seq_count, tokens, kv_width),
            "seq",
            split_axis=0,
            concat_axis=0,
            tiled=True,
        )
        kv_total = jnp.sum(kv_terms.astype(jnp.float32), axis=0)
    key_gradient_total = kv_total[:, : groups * HEAD_SIZE]
    value_gradient_total = kv_total[:, groups * HEAD_SIZE :]
    attn_out = attention_table.reshape(tokens, groups * heads_per_group * HEAD_SIZE)
    q_grad = (
        (grad_query * logit_scale)
        .reshape(tokens, groups * heads_per_group * HEAD_SIZE)
        .astype(jnp.bfloat16)
    )
    key_gradient = (key_gradient_total * logit_scale).astype(jnp.bfloat16)
    value_gradient = value_gradient_total.astype(jnp.bfloat16)
    return (
        mixer_out,
        attn_out,
        x_grad,
        grad_b,
        grad_c,
        grad_decay,
        q_grad,
        key_gradient,
        value_gradient,
    )


def solution(mesh):
    placed = (
        P(("groups", "seq"), "head"),
        P(("groups", "seq"), None),
        P(("groups", "seq"), None),
        P(("groups", "head"), "seq"),
        P("head"),
        P("groups"),
        P(("groups", "seq"), "head"),
        P(("groups", "seq"), "head"),
        P(("groups", "seq"), "head"),
        P(("groups", "seq"), "head"),
        P(("groups", "seq"), "head"),
    )
    return jax.shard_map(
        on_device,
        mesh=mesh,
        in_specs=placed,
        out_specs=(
            P(("groups", "seq"), "head"),
            P(("groups", "seq"), "head"),
            P(("groups", "seq"), "head"),
            P(("groups", "seq"), None),
            P(("groups", "seq"), None),
            P(("groups", "head"), "seq"),
            P(("groups", "seq"), "head"),
            P(("groups", "seq"), "head"),
            P(("groups", "seq"), "head"),
        ),
        check_vma=False,
    )
```

```python
import math

import jax
import jax.numpy as jnp
from jax import lax
from jax.sharding import PartitionSpec as P

P_SIZE = 128
HEAD_SIZE = 128
TOK_SPAN = 128


precise = lax.Precision.HIGH
big_negative = -1e30


def entering_2(part, axis, combine, identity, reverse):
    count = lax.axis_size(axis)
    place = lax.axis_index(axis)
    ahead = count - 1 - place if reverse else place
    early = jax.tree.map(lambda a, e: jnp.zeros_like(a) + jnp.asarray(e, a.dtype), part, identity)
    span = part
    shift = 1
    while shift < count:
        if reverse:
            pairs = [(i, i - shift) for i in range(shift, count)]
        else:
            pairs = [(i, i + shift) for i in range(count - shift)]
        got = lax.ppermute(span, axis, pairs)
        have = ahead >= shift
        got = jax.tree.map(lambda g, e: jnp.where(have, g, jnp.asarray(e, g.dtype)), got, identity)
        early = combine(got, early)
        if 2 * shift < count:
            span = combine(got, span)
        shift *= 2
    return early


def doc_index(positions, lengths):
    ends = jnp.cumsum(lengths)
    return jnp.sum((positions[:, None] >= ends[None, :]).astype(jnp.int32), axis=1)


def cumulate(decay):
    return jnp.cumsum(decay, axis=1)


def local_state(inputs, b_float, cumulated, segment):
    weights = (
        jnp.exp(cumulated[:, -1:] - cumulated)
        * (segment == segment[-1]).astype(inputs.dtype)[None, :]
    )
    return jnp.einsum("hs,sn,shp->hnp", weights, b_float, inputs, precision=precise)


def carry_factor(cumulated, segment, before):
    return jnp.exp(cumulated[:, -1]) * (segment[-1] == before).astype(cumulated.dtype)


def mixer_stretch(inputs, b_float, c_float, decay, gains, segment, before, state_in):
    cumulated = cumulate(decay)
    width = inputs.shape[0]
    steps = jnp.arange(width)
    allowed = (steps[:, None] >= steps[None, :]) & (segment[:, None] == segment[None, :])
    gaps = jnp.where(allowed[None], cumulated[:, :, None] - cumulated[:, None, :], big_negative)
    kernel = jnp.exp(gaps) * jnp.dot(c_float, b_float.T, precision=precise)[None]
    inner = jnp.einsum("hts,shp->thp", kernel, inputs, precision=precise)
    keeps = (segment == before).astype(inputs.dtype)
    entering = jnp.einsum("tn,hnp->thp", c_float, state_in, precision=precise)
    reach = jnp.exp(cumulated).T * keeps[:, None]
    outputs = inner + reach[:, :, None] * entering + gains[None, :, None] * inputs
    factor = carry_factor(cumulated, segment, before)
    state_out = factor[:, None, None] * state_in + local_state(inputs, b_float, cumulated, segment)
    return (outputs, state_out)


def combine_states(earlier, later):
    return (earlier[0] * later[0], later[0][:, None, None] * earlier[1] + later[1])


def mixer_whole(inputs, b_float, c_float, decay, gains, segment):
    width = TOK_SPAN
    count = inputs.shape[0] // width
    heads = inputs.shape[1]
    inp = inputs.reshape(count, width, heads, P_SIZE)
    b_blocks = b_float.reshape(count, width, -1)
    c_blocks = c_float.reshape(count, width, -1)
    dec = decay.reshape(heads, count, width).transpose(1, 0, 2)
    seg = segment.reshape(count, width)
    befores = jnp.concatenate([jnp.full((1,), -1, seg.dtype), seg[:-1, -1]])
    cumulated = jnp.cumsum(dec, axis=2)
    factor = jax.vmap(carry_factor)(cumulated, seg, befores)
    summary = jax.vmap(local_state)(inp, b_blocks, cumulated, seg)

    columns = jnp.arange(count)[:, None]
    row = jnp.zeros((count, heads), factor.dtype)
    rows = [row]
    for k in range(1, count):
        row = jnp.where(columns < k - 1, row * factor[k - 1][None, :], (columns == k - 1).astype(factor.dtype))
        rows.append(row)
    reach = jnp.stack(rows)
    state_in = jnp.einsum("kjh,jhnp->khnp", reach, summary, precision=precise)

    def stretch(i, brow, crow, d, sg, bf, st):
        return mixer_stretch(i, brow, crow, d, gains, sg, bf, st)[0]

    outputs = jax.vmap(stretch)(inp, b_blocks, c_blocks, dec, seg, befores, state_in)
    return outputs.reshape(count * width, heads, P_SIZE)


def mamba_by_heads(x_all, cot_all, b_all, c_all, decay_log, skip_gain, doc_lengths):
    seq_count = lax.axis_size("seq")
    place = lax.axis_index("seq")
    heads_here = skip_gain.shape[0]
    own = heads_here // seq_count
    total = x_all.shape[0]
    decay = lax.all_to_all(decay_log, "seq", split_axis=0, concat_axis=1, tiled=True)
    gains = lax.dynamic_slice_in_dim(skip_gain, place * own, own)
    segment = doc_index(jnp.arange(total, dtype=jnp.int32), doc_lengths)
    inputs = x_all.astype(jnp.float32).reshape(total, own, P_SIZE)
    cot = cot_all.astype(jnp.float32).reshape(total, own, P_SIZE)

    def whole_of(i, brow, crow, d):
        return mixer_whole(i, brow, crow, d, gains, segment)

    mixed, pull = jax.vjp(
        whole_of, inputs, b_all.astype(jnp.float32), c_all.astype(jnp.float32), decay
    )
    grad_x, grad_b, grad_c, grad_decay = pull(cot)
    decay_cols = lax.dynamic_update_slice_in_dim(
        jnp.zeros((total, heads_here), jnp.float32), grad_decay.T, place * own, 1
    )
    return (
        mixed.reshape(total, own * P_SIZE).astype(jnp.bfloat16),
        grad_x.reshape(total, own * P_SIZE).astype(jnp.bfloat16),
        jnp.concatenate([grad_b, grad_c, decay_cols], axis=1),
    )


def mamba_by_stretch(
    x_input, b_rows, c_rows, decay_log, skip_gain, doc_lengths, mixer_cot, segment, offset
):
    tokens = x_input.shape[0]
    previous = doc_index(jnp.reshape(offset - 1, (1,)), doc_lengths)[0]
    before = jnp.where(offset > 0, previous, -1)
    heads_here = skip_gain.shape[0]
    inputs = x_input.astype(jnp.float32).reshape(tokens, heads_here, P_SIZE)
    b_float = b_rows.astype(jnp.float32)
    c_float = c_rows.astype(jnp.float32)
    cot_float = mixer_cot.astype(jnp.float32).reshape(tokens, heads_here, P_SIZE)

    def stretch_of(inp, brow, crow, decay, state_in):
        return mixer_stretch(inp, brow, crow, decay, skip_gain, segment, before, state_in)

    cumulated = cumulate(decay_log)
    factor = carry_factor(cumulated, segment, before)
    summary = local_state(inputs, b_float, cumulated, segment)
    zero_state = jnp.zeros_like(summary)
    identity = (jnp.ones_like(factor), zero_state)
    state_in = entering_2((factor, summary), "seq", combine_states, identity, False)[1]
    (mixed, state_out), pull = jax.vjp(stretch_of, inputs, b_float, c_float, decay_log, state_in)
    adjoint_local = pull((cot_float, zero_state))[4]
    adjoint_out = entering_2((factor, adjoint_local), "seq", combine_states, identity, True)[1]
    grad_x, grad_b, grad_c, grad_decay, unused = pull((cot_float, adjoint_out))
    head_count = lax.axis_size("head")
    if head_count == 2:
        other_b, other_c = lax.ppermute((grad_b, grad_c), "head", [(0, 1), (1, 0)])
        grad_b, grad_c = grad_b + other_b, grad_c + other_c
    else:
        grad_b, grad_c = lax.psum((grad_b, grad_c), "head")
    mixer_out = mixed.reshape(tokens, heads_here * P_SIZE).astype(jnp.bfloat16)
    x_grad = grad_x.reshape(tokens, heads_here * P_SIZE).astype(jnp.bfloat16)
    return (mixer_out, x_grad, grad_b, grad_c, grad_decay)


def on_device(
    x_input,
    b_rows,
    c_rows,
    decay_log,
    skip_gain,
    doc_lengths,
    queries,
    attention_key_rows,
    values,
    mixer_cot,
    attention_output_cotangent,
):
    tokens = x_input.shape[0]
    offset = lax.axis_index("seq") * tokens
    total_len = tokens * lax.axis_size("seq")
    positions = offset + jnp.arange(tokens, dtype=jnp.int32)
    segment = doc_index(positions, doc_lengths)
    heads_here = skip_gain.shape[0]
    by_heads = heads_here % lax.axis_size("seq") == 0
    key_width = attention_key_rows.shape[1]
    state_width = b_rows.shape[1]
    seq_count = lax.axis_size("seq")
    if by_heads:
        own_width = heads_here // seq_count * P_SIZE

        def by_owner(a):
            return a.reshape(tokens, seq_count, own_width).transpose(1, 0, 2)

        def spread(a):
            return jnp.broadcast_to(a[None], (seq_count,) + a.shape)

        sent = jnp.concatenate(
            [by_owner(x_input), by_owner(mixer_cot), spread(b_rows), spread(c_rows)], axis=2
        )
        got = lax.all_to_all(sent, "seq", split_axis=0, concat_axis=0, tiled=True)
        x_all = got[:, :, :own_width].reshape(total_len, own_width)
        cot_all = got[:, :, own_width : 2 * own_width].reshape(total_len, own_width)
        b_all = got[:, :, 2 * own_width : 2 * own_width + state_width].reshape(total_len, -1)
        c_all = got[:, :, 2 * own_width + state_width :].reshape(total_len, -1)
        kv_sent = spread(jnp.concatenate([attention_key_rows, values], axis=1))
        gathered = lax.all_to_all(kv_sent, "seq", split_axis=0, concat_axis=0, tiled=True)
        gathered = gathered.reshape(total_len, 2 * key_width)
    else:
        gathered = lax.all_gather(
            jnp.concatenate([attention_key_rows, values], axis=1), "seq", axis=0, tiled=True
        )
    key_all, value_all = gathered[:, :key_width], gathered[:, key_width : 2 * key_width]
    if by_heads:
        mixed_own, x_grad_own, bc_part = mamba_by_heads(
            x_all, cot_all, b_all, c_all, decay_log, skip_gain, doc_lengths
        )
    else:
        mixer_out, x_grad, grad_b, grad_c, grad_decay = mamba_by_stretch(
            x_input, b_rows, c_rows, decay_log, skip_gain, doc_lengths, mixer_cot, segment, offset
        )
    logit_scale = 1.0 / math.sqrt(HEAD_SIZE)
    groups = attention_key_rows.shape[1] // HEAD_SIZE
    heads_per_group = queries.shape[1] // HEAD_SIZE // groups
    key_span = min(512, total_len)
    blocks = total_len // key_span
    last_pos = offset + tokens - 1
    query_grid = queries.reshape(tokens, groups, heads_per_group, HEAD_SIZE)
    cotangent_table = attention_output_cotangent.reshape(tokens, groups, heads_per_group, HEAD_SIZE)

    def block_view(number):
        anchor = number * key_span
        key_blk = lax.dynamic_slice_in_dim(key_all, anchor, key_span, 0).reshape(
            key_span, groups, HEAD_SIZE
        )
        value_blk = lax.dynamic_slice_in_dim(value_all, anchor, key_span, 0).reshape(
            key_span, groups, HEAD_SIZE
        )
        key_pos = anchor + jnp.arange(key_span, dtype=jnp.int32)
        allowed = (key_pos[None, :] <= positions[:, None]) & (
            doc_index(key_pos, doc_lengths)[None, :] == segment[:, None]
        )
        scores = (
            jnp.einsum("tgrd,kgd->grtk", query_grid, key_blk, preferred_element_type=jnp.float32)
            * logit_scale
        )
        scores = jnp.where(allowed[None, None], scores, big_negative)
        return (anchor, key_blk, value_blk, allowed, scores)

    def visit(number, carried, work):
        return lax.cond(
            number * key_span <= last_pos,
            lambda inner: work(number, inner),
            lambda inner: inner,
            carried,
        )

    def stats_step(number, carried):
        row_peak, row_total = carried
        anchor, key_blk, value_blk, allowed, scores = block_view(number)
        new_peak = jnp.maximum(row_peak, jnp.max(scores, axis=-1))
        fresh = jnp.sum(
            jnp.where(allowed[None, None], jnp.exp(scores - new_peak[..., None]), 0.0), axis=-1
        )
        return (new_peak, row_total * jnp.exp(row_peak - new_peak) + fresh)

    stat_shape = (groups, heads_per_group, tokens)
    row_peak, row_total = lax.fori_loop(
        0,
        blocks,
        lambda number, carried: visit(number, carried, stats_step),
        (jnp.full(stat_shape, big_negative, jnp.float32), jnp.zeros(stat_shape, jnp.float32)),
    )
    log_norm = row_peak + jnp.log(row_total)

    def output_step(number, totals):
        anchor, key_blk, value_blk, allowed, scores = block_view(number)
        weights = jnp.where(allowed[None, None], jnp.exp(scores - log_norm[..., None]), 0.0).astype(
            jnp.bfloat16
        )
        return totals + jnp.einsum(
            "grtk,kgd->tgrd", weights, value_blk, preferred_element_type=jnp.float32
        )

    attention_table = lax.fori_loop(
        0,
        blocks,
        lambda number, carried: visit(number, carried, output_step),
        jnp.zeros((tokens, groups, heads_per_group, HEAD_SIZE), jnp.float32),
    ).astype(jnp.bfloat16)
    row_products = jnp.einsum(
        "bkfh,bkfh->kfb", cotangent_table, attention_table, preferred_element_type=jnp.float32
    )

    def grad_terms(allowed, scores, value_blk):
        probs_full = jnp.where(allowed[None, None], jnp.exp(scores - log_norm[..., None]), 0.0)
        grad_prob = jnp.einsum(
            "tgrd,kgd->grtk", cotangent_table, value_blk, preferred_element_type=jnp.float32
        )
        grad_score = (probs_full * (grad_prob - row_products[..., None])).astype(jnp.bfloat16)
        return (probs_full.astype(jnp.bfloat16), grad_score)

    query_zero = jnp.zeros((tokens, groups, heads_per_group, HEAD_SIZE), jnp.float32)

    def full_step(number, carried):
        grad_query, term_key, term_value = carried
        anchor, key_blk, value_blk, allowed, scores = block_view(number)
        weights, grad_score = grad_terms(allowed, scores, value_blk)
        grad_query = grad_query + jnp.einsum(
            "grtk,kgd->tgrd", grad_score, key_blk, preferred_element_type=jnp.float32
        )
        key_part = jnp.einsum(
            "grtk,tgrd->kgd", grad_score, query_grid, preferred_element_type=jnp.float32
        ).reshape(key_span, groups * HEAD_SIZE)
        value_part = jnp.einsum(
            "grtk,tgrd->kgd", weights, cotangent_table, preferred_element_type=jnp.float32
        ).reshape(key_span, groups * HEAD_SIZE)
        term_key = lax.dynamic_update_slice_in_dim(term_key, key_part, anchor, 0)
        term_value = lax.dynamic_update_slice_in_dim(term_value, value_part, anchor, 0)
        return (grad_query, term_key, term_value)

    term_zero = jnp.zeros((total_len, groups * HEAD_SIZE), jnp.float32)
    grad_query, term_key, term_value = lax.fori_loop(
        0,
        blocks,
        lambda number, carried: visit(number, carried, full_step),
        (query_zero, term_zero, term_zero),
    )
    kv_terms = jnp.concatenate([term_key, term_value], axis=1).astype(jnp.bfloat16)
    kv_width = kv_terms.shape[1]
    if by_heads:
        kv_got = lax.all_to_all(
            jnp.concatenate(
                [
                    kv_terms.reshape(seq_count, tokens, kv_width),
                    mixed_own.reshape(seq_count, tokens, own_width),
                ],
                axis=2,
            ),
            "seq",
            split_axis=0,
            concat_axis=0,
            tiled=True,
        )
        sent = jnp.concatenate(
            [
                x_grad_own.reshape(seq_count, tokens, own_width),
                bc_part.astype(jnp.bfloat16).reshape(seq_count, tokens, bc_part.shape[1]),
            ],
            axis=2,
        )
        got = lax.all_to_all(sent, "seq", split_axis=0, concat_axis=0, tiled=True)

        def from_owners(a):
            return a.transpose(1, 0, 2).reshape(tokens, seq_count * own_width)

        mixer_out = from_owners(kv_got[:, :, kv_width:])
        x_grad = from_owners(got[:, :, :own_width])
        kv_total = jnp.sum(kv_got[:, :, :kv_width].astype(jnp.float32), axis=0)
        bc_sum = jnp.sum(got[:, :, own_width:].astype(jnp.float32), axis=0)
        grad_decay = bc_sum[:, 2 * state_width :].T
        bc_sum = bc_sum[:, : 2 * state_width]
        if lax.axis_size("head") == 2:
            bc_sum = bc_sum + lax.ppermute(bc_sum, "head", [(0, 1), (1, 0)])
        else:
            bc_sum = lax.psum(bc_sum, "head")
        grad_b, grad_c = bc_sum[:, :state_width], bc_sum[:, state_width:]
    else:
        kv_terms = lax.all_to_all(
            kv_terms.reshape(seq_count, tokens, kv_width),
            "seq",
            split_axis=0,
            concat_axis=0,
            tiled=True,
        )
        kv_total = jnp.sum(kv_terms.astype(jnp.float32), axis=0)
    key_gradient_total = kv_total[:, : groups * HEAD_SIZE]
    value_gradient_total = kv_total[:, groups * HEAD_SIZE :]
    attn_out = attention_table.reshape(tokens, groups * heads_per_group * HEAD_SIZE)
    q_grad = (
        (grad_query * logit_scale)
        .reshape(tokens, groups * heads_per_group * HEAD_SIZE)
        .astype(jnp.bfloat16)
    )
    key_gradient = (key_gradient_total * logit_scale).astype(jnp.bfloat16)
    value_gradient = value_gradient_total.astype(jnp.bfloat16)
    return (
        mixer_out,
        attn_out,
        x_grad,
        grad_b,
        grad_c,
        grad_decay,
        q_grad,
        key_gradient,
        value_gradient,
    )


def solution(mesh):
    placed = (
        P(("groups", "seq"), "head"),
        P(("groups", "seq"), None),
        P(("groups", "seq"), None),
        P(("groups", "head"), "seq"),
        P("head"),
        P("groups"),
        P(("groups", "seq"), "head"),
        P(("groups", "seq"), "head"),
        P(("groups", "seq"), "head"),
        P(("groups", "seq"), "head"),
        P(("groups", "seq"), "head"),
    )
    return jax.shard_map(
        on_device,
        mesh=mesh,
        in_specs=placed,
        out_specs=(
            P(("groups", "seq"), "head"),
            P(("groups", "seq"), "head"),
            P(("groups", "seq"), "head"),
            P(("groups", "seq"), None),
            P(("groups", "seq"), None),
            P(("groups", "head"), "seq"),
            P(("groups", "seq"), "head"),
            P(("groups", "seq"), "head"),
            P(("groups", "seq"), "head"),
        ),
        check_vma=False,
    )
```

```python
import math

import jax
import jax.numpy as jnp
from jax import lax
from jax.sharding import PartitionSpec as P

P_SIZE = 128
HEAD_SIZE = 128
TOK_SPAN = 128


precise = lax.Precision.HIGH
big_negative = -1e30


def entering_2(part, axis, combine, identity, reverse):
    count = lax.axis_size(axis)
    place = lax.axis_index(axis)
    ahead = count - 1 - place if reverse else place
    early = jax.tree.map(lambda a, e: jnp.zeros_like(a) + jnp.asarray(e, a.dtype), part, identity)
    span = part
    shift = 1
    while shift < count:
        if reverse:
            pairs = [(i, i - shift) for i in range(shift, count)]
        else:
            pairs = [(i, i + shift) for i in range(count - shift)]
        got = lax.ppermute(span, axis, pairs)
        have = ahead >= shift
        got = jax.tree.map(lambda g, e: jnp.where(have, g, jnp.asarray(e, g.dtype)), got, identity)
        early = combine(got, early)
        if 2 * shift < count:
            span = combine(got, span)
        shift *= 2
    return early


def doc_index(positions, lengths):
    ends = jnp.cumsum(lengths)
    return jnp.sum((positions[:, None] >= ends[None, :]).astype(jnp.int32), axis=1)


def cumulate(decay):
    return jnp.cumsum(decay, axis=1)


def local_state(inputs, b_float, cumulated, segment):
    weights = (
        jnp.exp(cumulated[:, -1:] - cumulated)
        * (segment == segment[-1]).astype(inputs.dtype)[None, :]
    )
    return jnp.einsum("hs,sn,shp->hnp", weights, b_float, inputs, precision=precise)


def carry_factor(cumulated, segment, before):
    return jnp.exp(cumulated[:, -1]) * (segment[-1] == before).astype(cumulated.dtype)


def mixer_stretch(inputs, b_float, c_float, decay, gains, segment, before, state_in):
    cumulated = cumulate(decay)
    width = inputs.shape[0]
    steps = jnp.arange(width)
    allowed = (steps[:, None] >= steps[None, :]) & (segment[:, None] == segment[None, :])
    gaps = jnp.where(allowed[None], cumulated[:, :, None] - cumulated[:, None, :], big_negative)
    kernel = jnp.exp(gaps) * jnp.dot(c_float, b_float.T, precision=precise)[None]
    inner = jnp.einsum("hts,shp->thp", kernel, inputs, precision=precise)
    keeps = (segment == before).astype(inputs.dtype)
    entering = jnp.einsum("tn,hnp->thp", c_float, state_in, precision=precise)
    reach = jnp.exp(cumulated).T * keeps[:, None]
    outputs = inner + reach[:, :, None] * entering + gains[None, :, None] * inputs
    factor = carry_factor(cumulated, segment, before)
    state_out = factor[:, None, None] * state_in + local_state(inputs, b_float, cumulated, segment)
    return (outputs, state_out)


def combine_states(earlier, later):
    return (earlier[0] * later[0], later[0][:, None, None] * earlier[1] + later[1])


def mixer_whole(inputs, b_float, c_float, decay, gains, segment):
    width = TOK_SPAN
    count = inputs.shape[0] // width
    heads = inputs.shape[1]
    inp = inputs.reshape(count, width, heads, P_SIZE)
    b_blocks = b_float.reshape(count, width, -1)
    c_blocks = c_float.reshape(count, width, -1)
    dec = decay.reshape(heads, count, width).transpose(1, 0, 2)
    seg = segment.reshape(count, width)
    befores = jnp.concatenate([jnp.full((1,), -1, seg.dtype), seg[:-1, -1]])
    cumulated = jnp.cumsum(dec, axis=2)
    factor = jax.vmap(carry_factor)(cumulated, seg, befores)
    summary = jax.vmap(local_state)(inp, b_blocks, cumulated, seg)

    columns = jnp.arange(count)[:, None]
    row = jnp.zeros((count, heads), factor.dtype)
    rows = [row]
    for k in range(1, count):
        row = jnp.where(columns < k - 1, row * factor[k - 1][None, :], (columns == k - 1).astype(factor.dtype))
        rows.append(row)
    reach = jnp.stack(rows)
    state_in = jnp.einsum("kjh,jhnp->khnp", reach, summary, precision=precise)

    def stretch(i, brow, crow, d, sg, bf, st):
        return mixer_stretch(i, brow, crow, d, gains, sg, bf, st)[0]

    outputs = jax.vmap(stretch)(inp, b_blocks, c_blocks, dec, seg, befores, state_in)
    return outputs.reshape(count * width, heads, P_SIZE)


def mamba_by_heads(x_all, cot_all, b_all, c_all, decay_log, skip_gain, doc_lengths):
    seq_count = lax.axis_size("seq")
    place = lax.axis_index("seq")
    heads_here = skip_gain.shape[0]
    own = heads_here // seq_count
    total = x_all.shape[0]
    decay = lax.all_to_all(decay_log, "seq", split_axis=0, concat_axis=1, tiled=True)
    gains = lax.dynamic_slice_in_dim(skip_gain, place * own, own)
    segment = doc_index(jnp.arange(total, dtype=jnp.int32), doc_lengths)
    inputs = x_all.astype(jnp.float32).reshape(total, own, P_SIZE)
    cot = cot_all.astype(jnp.float32).reshape(total, own, P_SIZE)

    def whole_of(i, brow, crow, d):
        return mixer_whole(i, brow, crow, d, gains, segment)

    mixed, pull = jax.vjp(
        whole_of, inputs, b_all.astype(jnp.float32), c_all.astype(jnp.float32), decay
    )
    grad_x, grad_b, grad_c, grad_decay = pull(cot)
    decay_cols = lax.dynamic_update_slice_in_dim(
        jnp.zeros((total, heads_here), jnp.float32), grad_decay.T, place * own, 1
    )
    return (
        mixed.reshape(total, own * P_SIZE).astype(jnp.bfloat16),
        grad_x.reshape(total, own * P_SIZE).astype(jnp.bfloat16),
        jnp.concatenate([grad_b, grad_c, decay_cols], axis=1),
    )


def mamba_by_stretch(
    x_input, b_rows, c_rows, decay_log, skip_gain, doc_lengths, mixer_cot, segment, offset
):
    tokens = x_input.shape[0]
    previous = doc_index(jnp.reshape(offset - 1, (1,)), doc_lengths)[0]
    before = jnp.where(offset > 0, previous, -1)
    heads_here = skip_gain.shape[0]
    inputs = x_input.astype(jnp.float32).reshape(tokens, heads_here, P_SIZE)
    b_float = b_rows.astype(jnp.float32)
    c_float = c_rows.astype(jnp.float32)
    cot_float = mixer_cot.astype(jnp.float32).reshape(tokens, heads_here, P_SIZE)

    def stretch_of(inp, brow, crow, decay, state_in):
        return mixer_stretch(inp, brow, crow, decay, skip_gain, segment, before, state_in)

    cumulated = cumulate(decay_log)
    factor = carry_factor(cumulated, segment, before)
    summary = local_state(inputs, b_float, cumulated, segment)
    zero_state = jnp.zeros_like(summary)
    identity = (jnp.ones_like(factor), zero_state)
    state_in = entering_2((factor, summary), "seq", combine_states, identity, False)[1]
    (mixed, state_out), pull = jax.vjp(stretch_of, inputs, b_float, c_float, decay_log, state_in)
    adjoint_local = pull((cot_float, zero_state))[4]
    adjoint_out = entering_2((factor, adjoint_local), "seq", combine_states, identity, True)[1]
    grad_x, grad_b, grad_c, grad_decay, unused = pull((cot_float, adjoint_out))
    head_count = lax.axis_size("head")
    if head_count == 2:
        other_b, other_c = lax.ppermute((grad_b, grad_c), "head", [(0, 1), (1, 0)])
        grad_b, grad_c = grad_b + other_b, grad_c + other_c
    else:
        grad_b, grad_c = lax.psum((grad_b, grad_c), "head")
    mixer_out = mixed.reshape(tokens, heads_here * P_SIZE).astype(jnp.bfloat16)
    x_grad = grad_x.reshape(tokens, heads_here * P_SIZE).astype(jnp.bfloat16)
    return (mixer_out, x_grad, grad_b, grad_c, grad_decay)


def on_device(
    x_input,
    b_rows,
    c_rows,
    decay_log,
    skip_gain,
    doc_lengths,
    queries,
    attention_key_rows,
    values,
    mixer_cot,
    attention_output_cotangent,
):
    tokens = x_input.shape[0]
    offset = lax.axis_index("seq") * tokens
    total_len = tokens * lax.axis_size("seq")
    positions = offset + jnp.arange(tokens, dtype=jnp.int32)
    segment = doc_index(positions, doc_lengths)
    heads_here = skip_gain.shape[0]
    by_heads = heads_here % lax.axis_size("seq") == 0
    key_width = attention_key_rows.shape[1]
    state_width = b_rows.shape[1]
    seq_count = lax.axis_size("seq")
    if by_heads:
        own_width = heads_here // seq_count * P_SIZE

        def by_owner(a):
            return a.reshape(tokens, seq_count, own_width).transpose(1, 0, 2)

        def spread(a):
            return jnp.broadcast_to(a[None], (seq_count,) + a.shape)

        sent = jnp.concatenate(
            [by_owner(x_input), by_owner(mixer_cot), spread(b_rows), spread(c_rows)], axis=2
        )
        got = lax.all_to_all(sent, "seq", split_axis=0, concat_axis=0, tiled=True)
        x_all = got[:, :, :own_width].reshape(total_len, own_width)
        cot_all = got[:, :, own_width : 2 * own_width].reshape(total_len, own_width)
        b_all = got[:, :, 2 * own_width : 2 * own_width + state_width].reshape(total_len, -1)
        c_all = got[:, :, 2 * own_width + state_width :].reshape(total_len, -1)
        kv_sent = spread(jnp.concatenate([attention_key_rows, values], axis=1))
        gathered = lax.all_to_all(kv_sent, "seq", split_axis=0, concat_axis=0, tiled=True)
        gathered = gathered.reshape(total_len, 2 * key_width)
    else:
        gathered = lax.all_gather(
            jnp.concatenate([attention_key_rows, values], axis=1), "seq", axis=0, tiled=True
        )
    key_all, value_all = gathered[:, :key_width], gathered[:, key_width : 2 * key_width]
    if by_heads:
        mixed_own, x_grad_own, bc_part = mamba_by_heads(
            x_all, cot_all, b_all, c_all, decay_log, skip_gain, doc_lengths
        )
    else:
        mixer_out, x_grad, grad_b, grad_c, grad_decay = mamba_by_stretch(
            x_input, b_rows, c_rows, decay_log, skip_gain, doc_lengths, mixer_cot, segment, offset
        )
    logit_scale = 1.0 / math.sqrt(HEAD_SIZE)
    groups = attention_key_rows.shape[1] // HEAD_SIZE
    heads_per_group = queries.shape[1] // HEAD_SIZE // groups
    key_span = total_len
    blocks = total_len // key_span
    last_pos = offset + tokens - 1
    query_grid = queries.reshape(tokens, groups, heads_per_group, HEAD_SIZE)
    cotangent_table = attention_output_cotangent.reshape(tokens, groups, heads_per_group, HEAD_SIZE)

    def block_view(number):
        anchor = number * key_span
        key_blk = lax.dynamic_slice_in_dim(key_all, anchor, key_span, 0).reshape(
            key_span, groups, HEAD_SIZE
        )
        value_blk = lax.dynamic_slice_in_dim(value_all, anchor, key_span, 0).reshape(
            key_span, groups, HEAD_SIZE
        )
        key_pos = anchor + jnp.arange(key_span, dtype=jnp.int32)
        allowed = (key_pos[None, :] <= positions[:, None]) & (
            doc_index(key_pos, doc_lengths)[None, :] == segment[:, None]
        )
        scores = (
            jnp.einsum("tgrd,kgd->grtk", query_grid, key_blk, preferred_element_type=jnp.float32)
            * logit_scale
        )
        scores = jnp.where(allowed[None, None], scores, big_negative)
        return (anchor, key_blk, value_blk, allowed, scores)

    def visit(number, carried, work):
        return lax.cond(
            number * key_span <= last_pos,
            lambda inner: work(number, inner),
            lambda inner: inner,
            carried,
        )

    def stats_step(number, carried):
        row_peak, row_total = carried
        anchor, key_blk, value_blk, allowed, scores = block_view(number)
        new_peak = jnp.maximum(row_peak, jnp.max(scores, axis=-1))
        fresh = jnp.sum(
            jnp.where(allowed[None, None], jnp.exp(scores - new_peak[..., None]), 0.0), axis=-1
        )
        return (new_peak, row_total * jnp.exp(row_peak - new_peak) + fresh)

    stat_shape = (groups, heads_per_group, tokens)
    row_peak, row_total = lax.fori_loop(
        0,
        blocks,
        lambda number, carried: visit(number, carried, stats_step),
        (jnp.full(stat_shape, big_negative, jnp.float32), jnp.zeros(stat_shape, jnp.float32)),
    )
    log_norm = row_peak + jnp.log(row_total)

    def output_step(number, totals):
        anchor, key_blk, value_blk, allowed, scores = block_view(number)
        weights = jnp.where(allowed[None, None], jnp.exp(scores - log_norm[..., None]), 0.0).astype(
            jnp.bfloat16
        )
        return totals + jnp.einsum(
            "grtk,kgd->tgrd", weights, value_blk, preferred_element_type=jnp.float32
        )

    attention_table = lax.fori_loop(
        0,
        blocks,
        lambda number, carried: visit(number, carried, output_step),
        jnp.zeros((tokens, groups, heads_per_group, HEAD_SIZE), jnp.float32),
    ).astype(jnp.bfloat16)
    row_products = jnp.einsum(
        "bkfh,bkfh->kfb", cotangent_table, attention_table, preferred_element_type=jnp.float32
    )

    def grad_terms(allowed, scores, value_blk):
        probs_full = jnp.where(allowed[None, None], jnp.exp(scores - log_norm[..., None]), 0.0)
        grad_prob = jnp.einsum(
            "tgrd,kgd->grtk", cotangent_table, value_blk, preferred_element_type=jnp.float32
        )
        grad_score = (probs_full * (grad_prob - row_products[..., None])).astype(jnp.bfloat16)
        return (probs_full.astype(jnp.bfloat16), grad_score)

    query_zero = jnp.zeros((tokens, groups, heads_per_group, HEAD_SIZE), jnp.float32)

    def full_step(number, carried):
        grad_query, term_key, term_value = carried
        anchor, key_blk, value_blk, allowed, scores = block_view(number)
        weights, grad_score = grad_terms(allowed, scores, value_blk)
        grad_query = grad_query + jnp.einsum(
            "grtk,kgd->tgrd", grad_score, key_blk, preferred_element_type=jnp.float32
        )
        key_part = jnp.einsum(
            "grtk,tgrd->kgd", grad_score, query_grid, preferred_element_type=jnp.float32
        ).reshape(key_span, groups * HEAD_SIZE)
        value_part = jnp.einsum(
            "grtk,tgrd->kgd", weights, cotangent_table, preferred_element_type=jnp.float32
        ).reshape(key_span, groups * HEAD_SIZE)
        term_key = lax.dynamic_update_slice_in_dim(term_key, key_part, anchor, 0)
        term_value = lax.dynamic_update_slice_in_dim(term_value, value_part, anchor, 0)
        return (grad_query, term_key, term_value)

    term_zero = jnp.zeros((total_len, groups * HEAD_SIZE), jnp.float32)
    grad_query, term_key, term_value = lax.fori_loop(
        0,
        blocks,
        lambda number, carried: visit(number, carried, full_step),
        (query_zero, term_zero, term_zero),
    )
    kv_terms = jnp.concatenate([term_key, term_value], axis=1).astype(jnp.bfloat16)
    kv_width = kv_terms.shape[1]
    if by_heads:
        kv_got = lax.all_to_all(
            jnp.concatenate(
                [
                    kv_terms.reshape(seq_count, tokens, kv_width),
                    mixed_own.reshape(seq_count, tokens, own_width),
                ],
                axis=2,
            ),
            "seq",
            split_axis=0,
            concat_axis=0,
            tiled=True,
        )
        sent = jnp.concatenate(
            [
                x_grad_own.reshape(seq_count, tokens, own_width),
                bc_part.astype(jnp.bfloat16).reshape(seq_count, tokens, bc_part.shape[1]),
            ],
            axis=2,
        )
        got = lax.all_to_all(sent, "seq", split_axis=0, concat_axis=0, tiled=True)

        def from_owners(a):
            return a.transpose(1, 0, 2).reshape(tokens, seq_count * own_width)

        mixer_out = from_owners(kv_got[:, :, kv_width:])
        x_grad = from_owners(got[:, :, :own_width])
        kv_total = jnp.sum(kv_got[:, :, :kv_width].astype(jnp.float32), axis=0)
        bc_sum = jnp.sum(got[:, :, own_width:].astype(jnp.float32), axis=0)
        grad_decay = bc_sum[:, 2 * state_width :].T
        bc_sum = bc_sum[:, : 2 * state_width]
        if lax.axis_size("head") == 2:
            bc_sum = bc_sum + lax.ppermute(bc_sum, "head", [(0, 1), (1, 0)])
        else:
            bc_sum = lax.psum(bc_sum, "head")
        grad_b, grad_c = bc_sum[:, :state_width], bc_sum[:, state_width:]
    else:
        kv_terms = lax.all_to_all(
            kv_terms.reshape(seq_count, tokens, kv_width),
            "seq",
            split_axis=0,
            concat_axis=0,
            tiled=True,
        )
        kv_total = jnp.sum(kv_terms.astype(jnp.float32), axis=0)
    key_gradient_total = kv_total[:, : groups * HEAD_SIZE]
    value_gradient_total = kv_total[:, groups * HEAD_SIZE :]
    attn_out = attention_table.reshape(tokens, groups * heads_per_group * HEAD_SIZE)
    q_grad = (
        (grad_query * logit_scale)
        .reshape(tokens, groups * heads_per_group * HEAD_SIZE)
        .astype(jnp.bfloat16)
    )
    key_gradient = (key_gradient_total * logit_scale).astype(jnp.bfloat16)
    value_gradient = value_gradient_total.astype(jnp.bfloat16)
    return (
        mixer_out,
        attn_out,
        x_grad,
        grad_b,
        grad_c,
        grad_decay,
        q_grad,
        key_gradient,
        value_gradient,
    )


def solution(mesh):
    placed = (
        P(("groups", "seq"), "head"),
        P(("groups", "seq"), None),
        P(("groups", "seq"), None),
        P(("groups", "head"), "seq"),
        P("head"),
        P("groups"),
        P(("groups", "seq"), "head"),
        P(("groups", "seq"), "head"),
        P(("groups", "seq"), "head"),
        P(("groups", "seq"), "head"),
        P(("groups", "seq"), "head"),
    )
    return jax.shard_map(
        on_device,
        mesh=mesh,
        in_specs=placed,
        out_specs=(
            P(("groups", "seq"), "head"),
            P(("groups", "seq"), "head"),
            P(("groups", "seq"), "head"),
            P(("groups", "seq"), None),
            P(("groups", "seq"), None),
            P(("groups", "head"), "seq"),
            P(("groups", "seq"), "head"),
            P(("groups", "seq"), "head"),
            P(("groups", "seq"), "head"),
        ),
        check_vma=False,
    )
```

```python
import math

import jax
import jax.numpy as jnp
from jax import lax
from jax.sharding import PartitionSpec as P

P_SIZE = 128
HEAD_SIZE = 128
TOK_SPAN = 128


precise = lax.Precision.HIGH
big_negative = -1e30


def entering_2(part, axis, combine, identity, reverse):
    count = lax.axis_size(axis)
    place = lax.axis_index(axis)
    ahead = count - 1 - place if reverse else place
    early = jax.tree.map(lambda a, e: jnp.zeros_like(a) + jnp.asarray(e, a.dtype), part, identity)
    span = part
    shift = 1
    while shift < count:
        if reverse:
            pairs = [(i, i - shift) for i in range(shift, count)]
        else:
            pairs = [(i, i + shift) for i in range(count - shift)]
        got = lax.ppermute(span, axis, pairs)
        have = ahead >= shift
        got = jax.tree.map(lambda g, e: jnp.where(have, g, jnp.asarray(e, g.dtype)), got, identity)
        early = combine(got, early)
        if 2 * shift < count:
            span = combine(got, span)
        shift *= 2
    return early


def doc_index(positions, lengths):
    ends = jnp.cumsum(lengths)
    return jnp.sum((positions[:, None] >= ends[None, :]).astype(jnp.int32), axis=1)


def cumulate(decay):
    return jnp.cumsum(decay, axis=1)


def local_state(inputs, b_float, cumulated, segment):
    weights = (
        jnp.exp(cumulated[:, -1:] - cumulated)
        * (segment == segment[-1]).astype(inputs.dtype)[None, :]
    )
    return jnp.einsum("hs,sn,shp->hnp", weights, b_float, inputs, precision=precise)


def carry_factor(cumulated, segment, before):
    return jnp.exp(cumulated[:, -1]) * (segment[-1] == before).astype(cumulated.dtype)


def mixer_stretch(inputs, b_float, c_float, decay, gains, segment, before, state_in):
    cumulated = cumulate(decay)
    width = inputs.shape[0]
    steps = jnp.arange(width)
    allowed = (steps[:, None] >= steps[None, :]) & (segment[:, None] == segment[None, :])
    gaps = jnp.where(allowed[None], cumulated[:, :, None] - cumulated[:, None, :], big_negative)
    kernel = jnp.exp(gaps) * jnp.dot(c_float, b_float.T, precision=precise)[None]
    inner = jnp.einsum("hts,shp->thp", kernel, inputs, precision=precise)
    keeps = (segment == before).astype(inputs.dtype)
    entering = jnp.einsum("tn,hnp->thp", c_float, state_in, precision=precise)
    reach = jnp.exp(cumulated).T * keeps[:, None]
    outputs = inner + reach[:, :, None] * entering + gains[None, :, None] * inputs
    factor = carry_factor(cumulated, segment, before)
    state_out = factor[:, None, None] * state_in + local_state(inputs, b_float, cumulated, segment)
    return (outputs, state_out)


def combine_states(earlier, later):
    return (earlier[0] * later[0], later[0][:, None, None] * earlier[1] + later[1])


def mixer_whole(inputs, b_float, c_float, decay, gains, segment):
    width = TOK_SPAN
    count = inputs.shape[0] // width
    heads = inputs.shape[1]
    inp = inputs.reshape(count, width, heads, P_SIZE)
    b_blocks = b_float.reshape(count, width, -1)
    c_blocks = c_float.reshape(count, width, -1)
    dec = decay.reshape(heads, count, width).transpose(1, 0, 2)
    seg = segment.reshape(count, width)
    befores = jnp.concatenate([jnp.full((1,), -1, seg.dtype), seg[:-1, -1]])
    cumulated = jnp.cumsum(dec, axis=2)
    factor = jax.vmap(carry_factor)(cumulated, seg, befores)
    summary = jax.vmap(local_state)(inp, b_blocks, cumulated, seg)

    columns = jnp.arange(count)[:, None]
    row = jnp.zeros((count, heads), factor.dtype)
    rows = [row]
    for k in range(1, count):
        row = jnp.where(columns < k - 1, row * factor[k - 1][None, :], (columns == k - 1).astype(factor.dtype))
        rows.append(row)
    reach = jnp.stack(rows)
    state_in = jnp.einsum("kjh,jhnp->khnp", reach, summary, precision=precise)

    def stretch(i, brow, crow, d, sg, bf, st):
        return mixer_stretch(i, brow, crow, d, gains, sg, bf, st)[0]

    outputs = jax.vmap(stretch)(inp, b_blocks, c_blocks, dec, seg, befores, state_in)
    return outputs.reshape(count * width, heads, P_SIZE)


def mamba_by_heads(x_all, cot_all, b_all, c_all, decay_log, skip_gain, doc_lengths):
    seq_count = lax.axis_size("seq")
    place = lax.axis_index("seq")
    heads_here = skip_gain.shape[0]
    own = heads_here // seq_count
    total = x_all.shape[0]
    decay = lax.all_to_all(decay_log, "seq", split_axis=0, concat_axis=1, tiled=True)
    gains = lax.dynamic_slice_in_dim(skip_gain, place * own, own)
    segment = doc_index(jnp.arange(total, dtype=jnp.int32), doc_lengths)
    inputs = x_all.astype(jnp.float32).reshape(total, own, P_SIZE)
    cot = cot_all.astype(jnp.float32).reshape(total, own, P_SIZE)

    def whole_of(i, brow, crow, d):
        return mixer_whole(i, brow, crow, d, gains, segment)

    mixed, pull = jax.vjp(
        whole_of, inputs, b_all.astype(jnp.float32), c_all.astype(jnp.float32), decay
    )
    grad_x, grad_b, grad_c, grad_decay = pull(cot)
    decay_cols = lax.dynamic_update_slice_in_dim(
        jnp.zeros((total, heads_here), jnp.float32), grad_decay.T, place * own, 1
    )
    return (
        mixed.reshape(total, own * P_SIZE).astype(jnp.bfloat16),
        grad_x.reshape(total, own * P_SIZE).astype(jnp.bfloat16),
        jnp.concatenate([grad_b, grad_c, decay_cols], axis=1),
    )


def mamba_by_stretch(
    x_input, b_rows, c_rows, decay_log, skip_gain, doc_lengths, mixer_cot, segment, offset
):
    tokens = x_input.shape[0]
    previous = doc_index(jnp.reshape(offset - 1, (1,)), doc_lengths)[0]
    before = jnp.where(offset > 0, previous, -1)
    heads_here = skip_gain.shape[0]
    inputs = x_input.astype(jnp.float32).reshape(tokens, heads_here, P_SIZE)
    b_float = b_rows.astype(jnp.float32)
    c_float = c_rows.astype(jnp.float32)
    cot_float = mixer_cot.astype(jnp.float32).reshape(tokens, heads_here, P_SIZE)

    def stretch_of(inp, brow, crow, decay, state_in):
        return mixer_stretch(inp, brow, crow, decay, skip_gain, segment, before, state_in)

    cumulated = cumulate(decay_log)
    factor = carry_factor(cumulated, segment, before)
    summary = local_state(inputs, b_float, cumulated, segment)
    zero_state = jnp.zeros_like(summary)
    identity = (jnp.ones_like(factor), zero_state)
    state_in = entering_2((factor, summary), "seq", combine_states, identity, False)[1]
    (mixed, state_out), pull = jax.vjp(stretch_of, inputs, b_float, c_float, decay_log, state_in)
    adjoint_local = pull((cot_float, zero_state))[4]
    adjoint_out = entering_2((factor, adjoint_local), "seq", combine_states, identity, True)[1]
    grad_x, grad_b, grad_c, grad_decay, unused = pull((cot_float, adjoint_out))
    head_count = lax.axis_size("head")
    if head_count == 2:
        other_b, other_c = lax.ppermute((grad_b, grad_c), "head", [(0, 1), (1, 0)])
        grad_b, grad_c = grad_b + other_b, grad_c + other_c
    else:
        grad_b, grad_c = lax.psum((grad_b, grad_c), "head")
    mixer_out = mixed.reshape(tokens, heads_here * P_SIZE).astype(jnp.bfloat16)
    x_grad = grad_x.reshape(tokens, heads_here * P_SIZE).astype(jnp.bfloat16)
    return (mixer_out, x_grad, grad_b, grad_c, grad_decay)


def on_device(
    x_input,
    b_rows,
    c_rows,
    decay_log,
    skip_gain,
    doc_lengths,
    queries,
    attention_key_rows,
    values,
    mixer_cot,
    attention_output_cotangent,
):
    tokens = x_input.shape[0]
    offset = lax.axis_index("seq") * tokens
    total_len = tokens * lax.axis_size("seq")
    positions = offset + jnp.arange(tokens, dtype=jnp.int32)
    segment = doc_index(positions, doc_lengths)
    heads_here = skip_gain.shape[0]
    by_heads = heads_here % lax.axis_size("seq") == 0
    key_width = attention_key_rows.shape[1]
    state_width = b_rows.shape[1]
    seq_count = lax.axis_size("seq")
    if by_heads:
        own_width = heads_here // seq_count * P_SIZE

        def by_owner(a):
            return a.reshape(tokens, seq_count, own_width).transpose(1, 0, 2)

        def spread(a):
            return jnp.broadcast_to(a[None], (seq_count,) + a.shape)

        sent = jnp.concatenate(
            [by_owner(x_input), by_owner(mixer_cot), spread(b_rows), spread(c_rows)], axis=2
        )
        got = lax.all_to_all(sent, "seq", split_axis=0, concat_axis=0, tiled=True)
        x_all = got[:, :, :own_width].reshape(total_len, own_width)
        cot_all = got[:, :, own_width : 2 * own_width].reshape(total_len, own_width)
        b_all = got[:, :, 2 * own_width : 2 * own_width + state_width].reshape(total_len, -1)
        c_all = got[:, :, 2 * own_width + state_width :].reshape(total_len, -1)
        kv_sent = spread(jnp.concatenate([attention_key_rows, values], axis=1))
        gathered = lax.all_to_all(kv_sent, "seq", split_axis=0, concat_axis=0, tiled=True)
        gathered = gathered.reshape(total_len, 2 * key_width)
    else:
        gathered = lax.all_gather(
            jnp.concatenate([attention_key_rows, values], axis=1), "seq", axis=0, tiled=True
        )
    key_all, value_all = gathered[:, :key_width], gathered[:, key_width : 2 * key_width]
    if by_heads:
        mixed_own, x_grad_own, bc_part = mamba_by_heads(
            x_all, cot_all, b_all, c_all, decay_log, skip_gain, doc_lengths
        )
    else:
        mixer_out, x_grad, grad_b, grad_c, grad_decay = mamba_by_stretch(
            x_input, b_rows, c_rows, decay_log, skip_gain, doc_lengths, mixer_cot, segment, offset
        )
    logit_scale = 1.0 / math.sqrt(HEAD_SIZE)
    groups = attention_key_rows.shape[1] // HEAD_SIZE
    heads_per_group = queries.shape[1] // HEAD_SIZE // groups
    key_span = min(256, total_len)
    blocks = total_len // key_span
    last_pos = offset + tokens - 1
    query_grid = queries.reshape(tokens, groups, heads_per_group, HEAD_SIZE)
    cotangent_table = attention_output_cotangent.reshape(tokens, groups, heads_per_group, HEAD_SIZE)

    def block_view(number):
        anchor = number * key_span
        key_blk = lax.dynamic_slice_in_dim(key_all, anchor, key_span, 0).reshape(
            key_span, groups, HEAD_SIZE
        )
        value_blk = lax.dynamic_slice_in_dim(value_all, anchor, key_span, 0).reshape(
            key_span, groups, HEAD_SIZE
        )
        key_pos = anchor + jnp.arange(key_span, dtype=jnp.int32)
        allowed = (key_pos[None, :] <= positions[:, None]) & (
            doc_index(key_pos, doc_lengths)[None, :] == segment[:, None]
        )
        scores = (
            jnp.einsum("tgrd,kgd->grtk", query_grid, key_blk, preferred_element_type=jnp.float32)
            * logit_scale
        )
        scores = jnp.where(allowed[None, None], scores, big_negative)
        return (anchor, key_blk, value_blk, allowed, scores)

    def visit(number, carried, work):
        return lax.cond(
            number * key_span <= last_pos,
            lambda inner: work(number, inner),
            lambda inner: inner,
            carried,
        )

    def stats_step(number, carried):
        row_peak, row_total = carried
        anchor, key_blk, value_blk, allowed, scores = block_view(number)
        new_peak = jnp.maximum(row_peak, jnp.max(scores, axis=-1))
        fresh = jnp.sum(
            jnp.where(allowed[None, None], jnp.exp(scores - new_peak[..., None]), 0.0), axis=-1
        )
        return (new_peak, row_total * jnp.exp(row_peak - new_peak) + fresh)

    stat_shape = (groups, heads_per_group, tokens)
    row_peak, row_total = lax.fori_loop(
        0,
        blocks,
        lambda number, carried: visit(number, carried, stats_step),
        (jnp.full(stat_shape, big_negative, jnp.float32), jnp.zeros(stat_shape, jnp.float32)),
    )
    log_norm = row_peak + jnp.log(row_total)

    def output_step(number, totals):
        anchor, key_blk, value_blk, allowed, scores = block_view(number)
        weights = jnp.where(allowed[None, None], jnp.exp(scores - log_norm[..., None]), 0.0).astype(
            jnp.bfloat16
        )
        return totals + jnp.einsum(
            "grtk,kgd->tgrd", weights, value_blk, preferred_element_type=jnp.float32
        )

    attention_table = lax.fori_loop(
        0,
        blocks,
        lambda number, carried: visit(number, carried, output_step),
        jnp.zeros((tokens, groups, heads_per_group, HEAD_SIZE), jnp.float32),
    ).astype(jnp.bfloat16)
    row_products = jnp.einsum(
        "bkfh,bkfh->kfb", cotangent_table, attention_table, preferred_element_type=jnp.float32
    )

    def grad_terms(allowed, scores, value_blk):
        probs_full = jnp.where(allowed[None, None], jnp.exp(scores - log_norm[..., None]), 0.0)
        grad_prob = jnp.einsum(
            "tgrd,kgd->grtk", cotangent_table, value_blk, preferred_element_type=jnp.float32
        )
        grad_score = (probs_full * (grad_prob - row_products[..., None])).astype(jnp.bfloat16)
        return (probs_full.astype(jnp.bfloat16), grad_score)

    query_zero = jnp.zeros((tokens, groups, heads_per_group, HEAD_SIZE), jnp.float32)

    def full_step(number, carried):
        grad_query, term_key, term_value = carried
        anchor, key_blk, value_blk, allowed, scores = block_view(number)
        weights, grad_score = grad_terms(allowed, scores, value_blk)
        grad_query = grad_query + jnp.einsum(
            "grtk,kgd->tgrd", grad_score, key_blk, preferred_element_type=jnp.float32
        )
        key_part = jnp.einsum(
            "grtk,tgrd->kgd", grad_score, query_grid, preferred_element_type=jnp.float32
        ).reshape(key_span, groups * HEAD_SIZE)
        value_part = jnp.einsum(
            "grtk,tgrd->kgd", weights, cotangent_table, preferred_element_type=jnp.float32
        ).reshape(key_span, groups * HEAD_SIZE)
        term_key = lax.dynamic_update_slice_in_dim(term_key, key_part, anchor, 0)
        term_value = lax.dynamic_update_slice_in_dim(term_value, value_part, anchor, 0)
        return (grad_query, term_key, term_value)

    term_zero = jnp.zeros((total_len, groups * HEAD_SIZE), jnp.float32)
    grad_query, term_key, term_value = lax.fori_loop(
        0,
        blocks,
        lambda number, carried: visit(number, carried, full_step),
        (query_zero, term_zero, term_zero),
    )
    kv_terms = jnp.concatenate([term_key, term_value], axis=1).astype(jnp.bfloat16)
    kv_width = kv_terms.shape[1]
    if by_heads:
        kv_got = lax.all_to_all(
            jnp.concatenate(
                [
                    kv_terms.reshape(seq_count, tokens, kv_width),
                    mixed_own.reshape(seq_count, tokens, own_width),
                ],
                axis=2,
            ),
            "seq",
            split_axis=0,
            concat_axis=0,
            tiled=True,
        )
        sent = jnp.concatenate(
            [
                x_grad_own.reshape(seq_count, tokens, own_width),
                bc_part.astype(jnp.bfloat16).reshape(seq_count, tokens, bc_part.shape[1]),
            ],
            axis=2,
        )
        got = lax.all_to_all(sent, "seq", split_axis=0, concat_axis=0, tiled=True)

        def from_owners(a):
            return a.transpose(1, 0, 2).reshape(tokens, seq_count * own_width)

        mixer_out = from_owners(kv_got[:, :, kv_width:])
        x_grad = from_owners(got[:, :, :own_width])
        kv_total = jnp.sum(kv_got[:, :, :kv_width].astype(jnp.float32), axis=0)
        bc_sum = jnp.sum(got[:, :, own_width:].astype(jnp.float32), axis=0)
        grad_decay = bc_sum[:, 2 * state_width :].T
        bc_sum = bc_sum[:, : 2 * state_width]
        if lax.axis_size("head") == 2:
            bc_sum = bc_sum + lax.ppermute(bc_sum, "head", [(0, 1), (1, 0)])
        else:
            bc_sum = lax.psum(bc_sum, "head")
        grad_b, grad_c = bc_sum[:, :state_width], bc_sum[:, state_width:]
    else:
        kv_terms = lax.all_to_all(
            kv_terms.reshape(seq_count, tokens, kv_width),
            "seq",
            split_axis=0,
            concat_axis=0,
            tiled=True,
        )
        kv_total = jnp.sum(kv_terms.astype(jnp.float32), axis=0)
    key_gradient_total = kv_total[:, : groups * HEAD_SIZE]
    value_gradient_total = kv_total[:, groups * HEAD_SIZE :]
    attn_out = attention_table.reshape(tokens, groups * heads_per_group * HEAD_SIZE)
    q_grad = (
        (grad_query * logit_scale)
        .reshape(tokens, groups * heads_per_group * HEAD_SIZE)
        .astype(jnp.bfloat16)
    )
    key_gradient = (key_gradient_total * logit_scale).astype(jnp.bfloat16)
    value_gradient = value_gradient_total.astype(jnp.bfloat16)
    return (
        mixer_out,
        attn_out,
        x_grad,
        grad_b,
        grad_c,
        grad_decay,
        q_grad,
        key_gradient,
        value_gradient,
    )


def solution(mesh):
    placed = (
        P(("groups", "seq"), "head"),
        P(("groups", "seq"), None),
        P(("groups", "seq"), None),
        P(("groups", "head"), "seq"),
        P("head"),
        P("groups"),
        P(("groups", "seq"), "head"),
        P(("groups", "seq"), "head"),
        P(("groups", "seq"), "head"),
        P(("groups", "seq"), "head"),
        P(("groups", "seq"), "head"),
    )
    return jax.shard_map(
        on_device,
        mesh=mesh,
        in_specs=placed,
        out_specs=(
            P(("groups", "seq"), "head"),
            P(("groups", "seq"), "head"),
            P(("groups", "seq"), "head"),
            P(("groups", "seq"), None),
            P(("groups", "seq"), None),
            P(("groups", "head"), "seq"),
            P(("groups", "seq"), "head"),
            P(("groups", "seq"), "head"),
            P(("groups", "seq"), "head"),
        ),
        check_vma=False,
    )
```

```python
import math

import jax
import jax.numpy as jnp
from jax import lax
from jax.sharding import PartitionSpec as P

P_SIZE = 128
HEAD_SIZE = 128
TOK_SPAN = 128


precise = lax.Precision.HIGH
big_negative = -1e30


def entering_2(part, axis, combine, identity, reverse):
    count = lax.axis_size(axis)
    place = lax.axis_index(axis)
    ahead = count - 1 - place if reverse else place
    early = jax.tree.map(lambda a, e: jnp.zeros_like(a) + jnp.asarray(e, a.dtype), part, identity)
    span = part
    shift = 1
    while shift < count:
        if reverse:
            pairs = [(i, i - shift) for i in range(shift, count)]
        else:
            pairs = [(i, i + shift) for i in range(count - shift)]
        got = lax.ppermute(span, axis, pairs)
        have = ahead >= shift
        got = jax.tree.map(lambda g, e: jnp.where(have, g, jnp.asarray(e, g.dtype)), got, identity)
        early = combine(got, early)
        if 2 * shift < count:
            span = combine(got, span)
        shift *= 2
    return early


def doc_index(positions, lengths):
    ends = jnp.cumsum(lengths)
    return jnp.sum((positions[:, None] >= ends[None, :]).astype(jnp.int32), axis=1)


def cumulate(decay):
    return jnp.cumsum(decay, axis=1)


def local_state(inputs, b_float, cumulated, segment):
    weights = (
        jnp.exp(cumulated[:, -1:] - cumulated)
        * (segment == segment[-1]).astype(inputs.dtype)[None, :]
    )
    return jnp.einsum("hs,sn,shp->hnp", weights, b_float, inputs, precision=precise)


def carry_factor(cumulated, segment, before):
    return jnp.exp(cumulated[:, -1]) * (segment[-1] == before).astype(cumulated.dtype)


def mixer_stretch(inputs, b_float, c_float, decay, gains, segment, before, state_in):
    cumulated = cumulate(decay)
    width = inputs.shape[0]
    steps = jnp.arange(width)
    allowed = (steps[:, None] >= steps[None, :]) & (segment[:, None] == segment[None, :])
    gaps = jnp.where(allowed[None], cumulated[:, :, None] - cumulated[:, None, :], big_negative)
    kernel = jnp.exp(gaps) * jnp.dot(c_float, b_float.T, precision=precise)[None]
    inner = jnp.einsum("hts,shp->thp", kernel, inputs, precision=precise)
    keeps = (segment == before).astype(inputs.dtype)
    entering = jnp.einsum("tn,hnp->thp", c_float, state_in, precision=precise)
    reach = jnp.exp(cumulated).T * keeps[:, None]
    outputs = inner + reach[:, :, None] * entering + gains[None, :, None] * inputs
    factor = carry_factor(cumulated, segment, before)
    state_out = factor[:, None, None] * state_in + local_state(inputs, b_float, cumulated, segment)
    return (outputs, state_out)


def combine_states(earlier, later):
    return (earlier[0] * later[0], later[0][:, None, None] * earlier[1] + later[1])


def mixer_whole(inputs, b_float, c_float, decay, gains, segment):
    width = TOK_SPAN
    count = inputs.shape[0] // width
    heads = inputs.shape[1]
    inp = inputs.reshape(count, width, heads, P_SIZE)
    b_blocks = b_float.reshape(count, width, -1)
    c_blocks = c_float.reshape(count, width, -1)
    dec = decay.reshape(heads, count, width).transpose(1, 0, 2)
    seg = segment.reshape(count, width)
    befores = jnp.concatenate([jnp.full((1,), -1, seg.dtype), seg[:-1, -1]])
    cumulated = jnp.cumsum(dec, axis=2)
    factor = jax.vmap(carry_factor)(cumulated, seg, befores)
    summary = jax.vmap(local_state)(inp, b_blocks, cumulated, seg)

    columns = jnp.arange(count)[:, None]
    row = jnp.zeros((count, heads), factor.dtype)
    rows = [row]
    for k in range(1, count):
        row = jnp.where(columns < k - 1, row * factor[k - 1][None, :], (columns == k - 1).astype(factor.dtype))
        rows.append(row)
    reach = jnp.stack(rows)
    state_in = jnp.einsum("kjh,jhnp->khnp", reach, summary, precision=precise)

    def stretch(i, brow, crow, d, sg, bf, st):
        return mixer_stretch(i, brow, crow, d, gains, sg, bf, st)[0]

    outputs = jax.vmap(stretch)(inp, b_blocks, c_blocks, dec, seg, befores, state_in)
    return outputs.reshape(count * width, heads, P_SIZE)


def mamba_by_heads(x_all, cot_all, b_all, c_all, decay_log, skip_gain, doc_lengths):
    seq_count = lax.axis_size("seq")
    place = lax.axis_index("seq")
    heads_here = skip_gain.shape[0]
    own = heads_here // seq_count
    total = x_all.shape[0]
    decay = lax.all_to_all(decay_log, "seq", split_axis=0, concat_axis=1, tiled=True)
    gains = lax.dynamic_slice_in_dim(skip_gain, place * own, own)
    segment = doc_index(jnp.arange(total, dtype=jnp.int32), doc_lengths)
    inputs = x_all.astype(jnp.float32).reshape(total, own, P_SIZE)
    cot = cot_all.astype(jnp.float32).reshape(total, own, P_SIZE)

    def whole_of(i, brow, crow, d):
        return mixer_whole(i, brow, crow, d, gains, segment)

    mixed, pull = jax.vjp(
        whole_of, inputs, b_all.astype(jnp.float32), c_all.astype(jnp.float32), decay
    )
    grad_x, grad_b, grad_c, grad_decay = pull(cot)
    decay_cols = lax.dynamic_update_slice_in_dim(
        jnp.zeros((total, heads_here), jnp.float32), grad_decay.T, place * own, 1
    )
    return (
        mixed.reshape(total, own * P_SIZE).astype(jnp.bfloat16),
        grad_x.reshape(total, own * P_SIZE).astype(jnp.bfloat16),
        jnp.concatenate([grad_b, grad_c, decay_cols], axis=1),
    )


def mamba_by_stretch(
    x_input, b_rows, c_rows, decay_log, skip_gain, doc_lengths, mixer_cot, segment, offset
):
    tokens = x_input.shape[0]
    previous = doc_index(jnp.reshape(offset - 1, (1,)), doc_lengths)[0]
    before = jnp.where(offset > 0, previous, -1)
    heads_here = skip_gain.shape[0]
    inputs = x_input.astype(jnp.float32).reshape(tokens, heads_here, P_SIZE)
    b_float = b_rows.astype(jnp.float32)
    c_float = c_rows.astype(jnp.float32)
    cot_float = mixer_cot.astype(jnp.float32).reshape(tokens, heads_here, P_SIZE)

    def stretch_of(inp, brow, crow, decay, state_in):
        return mixer_stretch(inp, brow, crow, decay, skip_gain, segment, before, state_in)

    cumulated = cumulate(decay_log)
    factor = carry_factor(cumulated, segment, before)
    summary = local_state(inputs, b_float, cumulated, segment)
    zero_state = jnp.zeros_like(summary)
    identity = (jnp.ones_like(factor), zero_state)
    state_in = entering_2((factor, summary), "seq", combine_states, identity, False)[1]
    (mixed, state_out), pull = jax.vjp(stretch_of, inputs, b_float, c_float, decay_log, state_in)
    adjoint_local = pull((cot_float, zero_state))[4]
    adjoint_out = entering_2((factor, adjoint_local), "seq", combine_states, identity, True)[1]
    grad_x, grad_b, grad_c, grad_decay, unused = pull((cot_float, adjoint_out))
    head_count = lax.axis_size("head")
    if head_count == 2:
        other_b, other_c = lax.ppermute((grad_b, grad_c), "head", [(0, 1), (1, 0)])
        grad_b, grad_c = grad_b + other_b, grad_c + other_c
    else:
        grad_b, grad_c = lax.psum((grad_b, grad_c), "head")
    mixer_out = mixed.reshape(tokens, heads_here * P_SIZE).astype(jnp.bfloat16)
    x_grad = grad_x.reshape(tokens, heads_here * P_SIZE).astype(jnp.bfloat16)
    return (mixer_out, x_grad, grad_b, grad_c, grad_decay)


def unrolled(count, step, carried):
    for number in range(count):
        carried = step(number, carried)
    return carried


def on_device(
    x_input,
    b_rows,
    c_rows,
    decay_log,
    skip_gain,
    doc_lengths,
    queries,
    attention_key_rows,
    values,
    mixer_cot,
    attention_output_cotangent,
):
    tokens = x_input.shape[0]
    offset = lax.axis_index("seq") * tokens
    total_len = tokens * lax.axis_size("seq")
    positions = offset + jnp.arange(tokens, dtype=jnp.int32)
    segment = doc_index(positions, doc_lengths)
    heads_here = skip_gain.shape[0]
    by_heads = heads_here % lax.axis_size("seq") == 0
    key_width = attention_key_rows.shape[1]
    state_width = b_rows.shape[1]
    seq_count = lax.axis_size("seq")
    if by_heads:
        own_width = heads_here // seq_count * P_SIZE

        def by_owner(a):
            return a.reshape(tokens, seq_count, own_width).transpose(1, 0, 2)

        def spread(a):
            return jnp.broadcast_to(a[None], (seq_count,) + a.shape)

        sent = jnp.concatenate(
            [by_owner(x_input), by_owner(mixer_cot), spread(b_rows), spread(c_rows)], axis=2
        )
        got = lax.all_to_all(sent, "seq", split_axis=0, concat_axis=0, tiled=True)
        x_all = got[:, :, :own_width].reshape(total_len, own_width)
        cot_all = got[:, :, own_width : 2 * own_width].reshape(total_len, own_width)
        b_all = got[:, :, 2 * own_width : 2 * own_width + state_width].reshape(total_len, -1)
        c_all = got[:, :, 2 * own_width + state_width :].reshape(total_len, -1)
        kv_sent = spread(jnp.concatenate([attention_key_rows, values], axis=1))
        gathered = lax.all_to_all(kv_sent, "seq", split_axis=0, concat_axis=0, tiled=True)
        gathered = gathered.reshape(total_len, 2 * key_width)
    else:
        gathered = lax.all_gather(
            jnp.concatenate([attention_key_rows, values], axis=1), "seq", axis=0, tiled=True
        )
    key_all, value_all = gathered[:, :key_width], gathered[:, key_width : 2 * key_width]
    if by_heads:
        mixed_own, x_grad_own, bc_part = mamba_by_heads(
            x_all, cot_all, b_all, c_all, decay_log, skip_gain, doc_lengths
        )
    else:
        mixer_out, x_grad, grad_b, grad_c, grad_decay = mamba_by_stretch(
            x_input, b_rows, c_rows, decay_log, skip_gain, doc_lengths, mixer_cot, segment, offset
        )
    logit_scale = 1.0 / math.sqrt(HEAD_SIZE)
    groups = attention_key_rows.shape[1] // HEAD_SIZE
    heads_per_group = queries.shape[1] // HEAD_SIZE // groups
    key_span = min(512, total_len)
    blocks = total_len // key_span
    last_pos = offset + tokens - 1
    query_grid = queries.reshape(tokens, groups, heads_per_group, HEAD_SIZE)
    cotangent_table = attention_output_cotangent.reshape(tokens, groups, heads_per_group, HEAD_SIZE)

    def block_view(number):
        anchor = number * key_span
        key_blk = lax.dynamic_slice_in_dim(key_all, anchor, key_span, 0).reshape(
            key_span, groups, HEAD_SIZE
        )
        value_blk = lax.dynamic_slice_in_dim(value_all, anchor, key_span, 0).reshape(
            key_span, groups, HEAD_SIZE
        )
        key_pos = anchor + jnp.arange(key_span, dtype=jnp.int32)
        allowed = (key_pos[None, :] <= positions[:, None]) & (
            doc_index(key_pos, doc_lengths)[None, :] == segment[:, None]
        )
        scores = (
            jnp.einsum("tgrd,kgd->grtk", query_grid, key_blk, preferred_element_type=jnp.float32)
            * logit_scale
        )
        scores = jnp.where(allowed[None, None], scores, big_negative)
        return (anchor, key_blk, value_blk, allowed, scores)

    def visit(number, carried, work):
        return lax.cond(
            number * key_span <= last_pos,
            lambda inner: work(number, inner),
            lambda inner: inner,
            carried,
        )

    def stats_step(number, carried):
        row_peak, row_total = carried
        anchor, key_blk, value_blk, allowed, scores = block_view(number)
        new_peak = jnp.maximum(row_peak, jnp.max(scores, axis=-1))
        fresh = jnp.sum(
            jnp.where(allowed[None, None], jnp.exp(scores - new_peak[..., None]), 0.0), axis=-1
        )
        return (new_peak, row_total * jnp.exp(row_peak - new_peak) + fresh)

    stat_shape = (groups, heads_per_group, tokens)
    row_peak, row_total = unrolled(
        blocks,
        lambda number, carried: visit(number, carried, stats_step),
        (jnp.full(stat_shape, big_negative, jnp.float32), jnp.zeros(stat_shape, jnp.float32)),
    )
    log_norm = row_peak + jnp.log(row_total)

    def output_step(number, totals):
        anchor, key_blk, value_blk, allowed, scores = block_view(number)
        weights = jnp.where(allowed[None, None], jnp.exp(scores - log_norm[..., None]), 0.0).astype(
            jnp.bfloat16
        )
        return totals + jnp.einsum(
            "grtk,kgd->tgrd", weights, value_blk, preferred_element_type=jnp.float32
        )

    attention_table = unrolled(
        blocks,
        lambda number, carried: visit(number, carried, output_step),
        jnp.zeros((tokens, groups, heads_per_group, HEAD_SIZE), jnp.float32),
    ).astype(jnp.bfloat16)
    row_products = jnp.einsum(
        "bkfh,bkfh->kfb", cotangent_table, attention_table, preferred_element_type=jnp.float32
    )

    def grad_terms(allowed, scores, value_blk):
        probs_full = jnp.where(allowed[None, None], jnp.exp(scores - log_norm[..., None]), 0.0)
        grad_prob = jnp.einsum(
            "tgrd,kgd->grtk", cotangent_table, value_blk, preferred_element_type=jnp.float32
        )
        grad_score = (probs_full * (grad_prob - row_products[..., None])).astype(jnp.bfloat16)
        return (probs_full.astype(jnp.bfloat16), grad_score)

    query_zero = jnp.zeros((tokens, groups, heads_per_group, HEAD_SIZE), jnp.float32)

    def full_step(number, carried):
        grad_query, term_key, term_value = carried
        anchor, key_blk, value_blk, allowed, scores = block_view(number)
        weights, grad_score = grad_terms(allowed, scores, value_blk)
        grad_query = grad_query + jnp.einsum(
            "grtk,kgd->tgrd", grad_score, key_blk, preferred_element_type=jnp.float32
        )
        key_part = jnp.einsum(
            "grtk,tgrd->kgd", grad_score, query_grid, preferred_element_type=jnp.float32
        ).reshape(key_span, groups * HEAD_SIZE)
        value_part = jnp.einsum(
            "grtk,tgrd->kgd", weights, cotangent_table, preferred_element_type=jnp.float32
        ).reshape(key_span, groups * HEAD_SIZE)
        term_key = lax.dynamic_update_slice_in_dim(term_key, key_part, anchor, 0)
        term_value = lax.dynamic_update_slice_in_dim(term_value, value_part, anchor, 0)
        return (grad_query, term_key, term_value)

    term_zero = jnp.zeros((total_len, groups * HEAD_SIZE), jnp.float32)
    grad_query, term_key, term_value = unrolled(
        blocks,
        lambda number, carried: visit(number, carried, full_step),
        (query_zero, term_zero, term_zero),
    )
    kv_terms = jnp.concatenate([term_key, term_value], axis=1).astype(jnp.bfloat16)
    kv_width = kv_terms.shape[1]
    if by_heads:
        kv_got = lax.all_to_all(
            jnp.concatenate(
                [
                    kv_terms.reshape(seq_count, tokens, kv_width),
                    mixed_own.reshape(seq_count, tokens, own_width),
                ],
                axis=2,
            ),
            "seq",
            split_axis=0,
            concat_axis=0,
            tiled=True,
        )
        sent = jnp.concatenate(
            [
                x_grad_own.reshape(seq_count, tokens, own_width),
                bc_part.astype(jnp.bfloat16).reshape(seq_count, tokens, bc_part.shape[1]),
            ],
            axis=2,
        )
        got = lax.all_to_all(sent, "seq", split_axis=0, concat_axis=0, tiled=True)

        def from_owners(a):
            return a.transpose(1, 0, 2).reshape(tokens, seq_count * own_width)

        mixer_out = from_owners(kv_got[:, :, kv_width:])
        x_grad = from_owners(got[:, :, :own_width])
        kv_total = jnp.sum(kv_got[:, :, :kv_width].astype(jnp.float32), axis=0)
        bc_sum = jnp.sum(got[:, :, own_width:].astype(jnp.float32), axis=0)
        grad_decay = bc_sum[:, 2 * state_width :].T
        bc_sum = bc_sum[:, : 2 * state_width]
        if lax.axis_size("head") == 2:
            bc_sum = bc_sum + lax.ppermute(bc_sum, "head", [(0, 1), (1, 0)])
        else:
            bc_sum = lax.psum(bc_sum, "head")
        grad_b, grad_c = bc_sum[:, :state_width], bc_sum[:, state_width:]
    else:
        kv_terms = lax.all_to_all(
            kv_terms.reshape(seq_count, tokens, kv_width),
            "seq",
            split_axis=0,
            concat_axis=0,
            tiled=True,
        )
        kv_total = jnp.sum(kv_terms.astype(jnp.float32), axis=0)
    key_gradient_total = kv_total[:, : groups * HEAD_SIZE]
    value_gradient_total = kv_total[:, groups * HEAD_SIZE :]
    attn_out = attention_table.reshape(tokens, groups * heads_per_group * HEAD_SIZE)
    q_grad = (
        (grad_query * logit_scale)
        .reshape(tokens, groups * heads_per_group * HEAD_SIZE)
        .astype(jnp.bfloat16)
    )
    key_gradient = (key_gradient_total * logit_scale).astype(jnp.bfloat16)
    value_gradient = value_gradient_total.astype(jnp.bfloat16)
    return (
        mixer_out,
        attn_out,
        x_grad,
        grad_b,
        grad_c,
        grad_decay,
        q_grad,
        key_gradient,
        value_gradient,
    )


def solution(mesh):
    placed = (
        P(("groups", "seq"), "head"),
        P(("groups", "seq"), None),
        P(("groups", "seq"), None),
        P(("groups", "head"), "seq"),
        P("head"),
        P("groups"),
        P(("groups", "seq"), "head"),
        P(("groups", "seq"), "head"),
        P(("groups", "seq"), "head"),
        P(("groups", "seq"), "head"),
        P(("groups", "seq"), "head"),
    )
    return jax.shard_map(
        on_device,
        mesh=mesh,
        in_specs=placed,
        out_specs=(
            P(("groups", "seq"), "head"),
            P(("groups", "seq"), "head"),
            P(("groups", "seq"), "head"),
            P(("groups", "seq"), None),
            P(("groups", "seq"), None),
            P(("groups", "head"), "seq"),
            P(("groups", "seq"), "head"),
            P(("groups", "seq"), "head"),
            P(("groups", "seq"), "head"),
        ),
        check_vma=False,
    )
```

```python
import math

import jax
import jax.numpy as jnp
from jax import lax
from jax.sharding import PartitionSpec as P

P_SIZE = 128
HEAD_SIZE = 128
TOK_SPAN = 128


precise = lax.Precision.HIGH
big_negative = -1e30


def entering_2(part, axis, combine, identity, reverse):
    count = lax.axis_size(axis)
    place = lax.axis_index(axis)
    ahead = count - 1 - place if reverse else place
    early = jax.tree.map(lambda a, e: jnp.zeros_like(a) + jnp.asarray(e, a.dtype), part, identity)
    span = part
    shift = 1
    while shift < count:
        if reverse:
            pairs = [(i, i - shift) for i in range(shift, count)]
        else:
            pairs = [(i, i + shift) for i in range(count - shift)]
        got = lax.ppermute(span, axis, pairs)
        have = ahead >= shift
        got = jax.tree.map(lambda g, e: jnp.where(have, g, jnp.asarray(e, g.dtype)), got, identity)
        early = combine(got, early)
        if 2 * shift < count:
            span = combine(got, span)
        shift *= 2
    return early


def doc_index(positions, lengths):
    ends = jnp.cumsum(lengths)
    return jnp.sum((positions[:, None] >= ends[None, :]).astype(jnp.int32), axis=1)


def cumulate(decay):
    return jnp.cumsum(decay, axis=1)


def local_state(inputs, b_float, cumulated, segment):
    weights = (
        jnp.exp(cumulated[:, -1:] - cumulated)
        * (segment == segment[-1]).astype(inputs.dtype)[None, :]
    )
    return jnp.einsum("hs,sn,shp->hnp", weights, b_float, inputs, precision=precise)


def carry_factor(cumulated, segment, before):
    return jnp.exp(cumulated[:, -1]) * (segment[-1] == before).astype(cumulated.dtype)


def mixer_stretch(inputs, b_float, c_float, decay, gains, segment, before, state_in):
    cumulated = cumulate(decay)
    width = inputs.shape[0]
    steps = jnp.arange(width)
    allowed = (steps[:, None] >= steps[None, :]) & (segment[:, None] == segment[None, :])
    gaps = jnp.where(allowed[None], cumulated[:, :, None] - cumulated[:, None, :], big_negative)
    kernel = jnp.exp(gaps) * jnp.dot(c_float, b_float.T, precision=precise)[None]
    inner = jnp.einsum("hts,shp->thp", kernel, inputs, precision=precise)
    keeps = (segment == before).astype(inputs.dtype)
    entering = jnp.einsum("tn,hnp->thp", c_float, state_in, precision=precise)
    reach = jnp.exp(cumulated).T * keeps[:, None]
    outputs = inner + reach[:, :, None] * entering + gains[None, :, None] * inputs
    factor = carry_factor(cumulated, segment, before)
    state_out = factor[:, None, None] * state_in + local_state(inputs, b_float, cumulated, segment)
    return (outputs, state_out)


def combine_states(earlier, later):
    return (earlier[0] * later[0], later[0][:, None, None] * earlier[1] + later[1])


def mixer_whole(inputs, b_float, c_float, decay, gains, segment):
    width = TOK_SPAN
    count = inputs.shape[0] // width
    heads = inputs.shape[1]
    inp = inputs.reshape(count, width, heads, P_SIZE)
    b_blocks = b_float.reshape(count, width, -1)
    c_blocks = c_float.reshape(count, width, -1)
    dec = decay.reshape(heads, count, width).transpose(1, 0, 2)
    seg = segment.reshape(count, width)
    befores = jnp.concatenate([jnp.full((1,), -1, seg.dtype), seg[:-1, -1]])
    cumulated = jnp.cumsum(dec, axis=2)
    factor = jax.vmap(carry_factor)(cumulated, seg, befores)
    summary = jax.vmap(local_state)(inp, b_blocks, cumulated, seg)

    columns = jnp.arange(count)[:, None]
    row = jnp.zeros((count, heads), factor.dtype)
    rows = [row]
    for k in range(1, count):
        row = jnp.where(columns < k - 1, row * factor[k - 1][None, :], (columns == k - 1).astype(factor.dtype))
        rows.append(row)
    reach = jnp.stack(rows)
    state_in = jnp.einsum("kjh,jhnp->khnp", reach, summary, precision=precise)

    def stretch(i, brow, crow, d, sg, bf, st):
        return mixer_stretch(i, brow, crow, d, gains, sg, bf, st)[0]

    outputs = jax.vmap(stretch)(inp, b_blocks, c_blocks, dec, seg, befores, state_in)
    return outputs.reshape(count * width, heads, P_SIZE)


def mamba_by_heads(x_all, cot_all, b_all, c_all, decay_log, skip_gain, doc_lengths):
    seq_count = lax.axis_size("seq")
    place = lax.axis_index("seq")
    heads_here = skip_gain.shape[0]
    own = heads_here // seq_count
    total = x_all.shape[0]
    decay = lax.all_to_all(decay_log, "seq", split_axis=0, concat_axis=1, tiled=True)
    gains = lax.dynamic_slice_in_dim(skip_gain, place * own, own)
    segment = doc_index(jnp.arange(total, dtype=jnp.int32), doc_lengths)
    inputs = x_all.astype(jnp.float32).reshape(total, own, P_SIZE)
    cot = cot_all.astype(jnp.float32).reshape(total, own, P_SIZE)

    def whole_of(i, brow, crow, d):
        return mixer_whole(i, brow, crow, d, gains, segment)

    mixed, pull = jax.vjp(
        whole_of, inputs, b_all.astype(jnp.float32), c_all.astype(jnp.float32), decay
    )
    grad_x, grad_b, grad_c, grad_decay = pull(cot)
    decay_cols = lax.dynamic_update_slice_in_dim(
        jnp.zeros((total, heads_here), jnp.float32), grad_decay.T, place * own, 1
    )
    return (
        mixed.reshape(total, own * P_SIZE).astype(jnp.bfloat16),
        grad_x.reshape(total, own * P_SIZE).astype(jnp.bfloat16),
        jnp.concatenate([grad_b, grad_c, decay_cols], axis=1),
    )


def mamba_by_stretch(
    x_input, b_rows, c_rows, decay_log, skip_gain, doc_lengths, mixer_cot, segment, offset
):
    tokens = x_input.shape[0]
    previous = doc_index(jnp.reshape(offset - 1, (1,)), doc_lengths)[0]
    before = jnp.where(offset > 0, previous, -1)
    heads_here = skip_gain.shape[0]
    inputs = x_input.astype(jnp.float32).reshape(tokens, heads_here, P_SIZE)
    b_float = b_rows.astype(jnp.float32)
    c_float = c_rows.astype(jnp.float32)
    cot_float = mixer_cot.astype(jnp.float32).reshape(tokens, heads_here, P_SIZE)

    def stretch_of(inp, brow, crow, decay, state_in):
        return mixer_stretch(inp, brow, crow, decay, skip_gain, segment, before, state_in)

    cumulated = cumulate(decay_log)
    factor = carry_factor(cumulated, segment, before)
    summary = local_state(inputs, b_float, cumulated, segment)
    zero_state = jnp.zeros_like(summary)
    identity = (jnp.ones_like(factor), zero_state)
    state_in = entering_2((factor, summary), "seq", combine_states, identity, False)[1]
    (mixed, state_out), pull = jax.vjp(stretch_of, inputs, b_float, c_float, decay_log, state_in)
    adjoint_local = pull((cot_float, zero_state))[4]
    adjoint_out = entering_2((factor, adjoint_local), "seq", combine_states, identity, True)[1]
    grad_x, grad_b, grad_c, grad_decay, unused = pull((cot_float, adjoint_out))
    head_count = lax.axis_size("head")
    if head_count == 2:
        other_b, other_c = lax.ppermute((grad_b, grad_c), "head", [(0, 1), (1, 0)])
        grad_b, grad_c = grad_b + other_b, grad_c + other_c
    else:
        grad_b, grad_c = lax.psum((grad_b, grad_c), "head")
    mixer_out = mixed.reshape(tokens, heads_here * P_SIZE).astype(jnp.bfloat16)
    x_grad = grad_x.reshape(tokens, heads_here * P_SIZE).astype(jnp.bfloat16)
    return (mixer_out, x_grad, grad_b, grad_c, grad_decay)


def on_device(
    x_input,
    b_rows,
    c_rows,
    decay_log,
    skip_gain,
    doc_lengths,
    queries,
    attention_key_rows,
    values,
    mixer_cot,
    attention_output_cotangent,
):
    tokens = x_input.shape[0]
    offset = lax.axis_index("seq") * tokens
    total_len = tokens * lax.axis_size("seq")
    positions = offset + jnp.arange(tokens, dtype=jnp.int32)
    segment = doc_index(positions, doc_lengths)
    heads_here = skip_gain.shape[0]
    by_heads = heads_here % lax.axis_size("seq") == 0
    key_width = attention_key_rows.shape[1]
    state_width = b_rows.shape[1]
    seq_count = lax.axis_size("seq")
    if by_heads:
        own_width = heads_here // seq_count * P_SIZE

        def by_owner(a):
            return a.reshape(tokens, seq_count, own_width).transpose(1, 0, 2)

        def spread(a):
            return jnp.broadcast_to(a[None], (seq_count,) + a.shape)

        shared = lax.axis_size("head") == 2
        if shared:
            first = lax.axis_index("head") == 0
            rows_sent = [spread(jnp.where(first, b_rows, c_rows))]
        else:
            rows_sent = [spread(b_rows), spread(c_rows)]
        sent = jnp.concatenate([by_owner(x_input), by_owner(mixer_cot)] + rows_sent, axis=2)
        got = lax.all_to_all(sent, "seq", split_axis=0, concat_axis=0, tiled=True)
        x_all = got[:, :, :own_width].reshape(total_len, own_width)
        cot_all = got[:, :, own_width : 2 * own_width].reshape(total_len, own_width)
        if shared:
            mine = got[:, :, 2 * own_width :].reshape(total_len, -1)
            theirs = lax.ppermute(mine, "head", [(0, 1), (1, 0)])
            b_all = jnp.where(first, mine, theirs)
            c_all = jnp.where(first, theirs, mine)
        else:
            b_all = got[:, :, 2 * own_width : 2 * own_width + state_width].reshape(total_len, -1)
            c_all = got[:, :, 2 * own_width + state_width :].reshape(total_len, -1)
        kv_sent = spread(jnp.concatenate([attention_key_rows, values], axis=1))
        gathered = lax.all_to_all(kv_sent, "seq", split_axis=0, concat_axis=0, tiled=True)
        gathered = gathered.reshape(total_len, 2 * key_width)
    else:
        gathered = lax.all_gather(
            jnp.concatenate([attention_key_rows, values], axis=1), "seq", axis=0, tiled=True
        )
    key_all, value_all = gathered[:, :key_width], gathered[:, key_width : 2 * key_width]
    if by_heads:
        mixed_own, x_grad_own, bc_part = mamba_by_heads(
            x_all, cot_all, b_all, c_all, decay_log, skip_gain, doc_lengths
        )
    else:
        mixer_out, x_grad, grad_b, grad_c, grad_decay = mamba_by_stretch(
            x_input, b_rows, c_rows, decay_log, skip_gain, doc_lengths, mixer_cot, segment, offset
        )
    logit_scale = 1.0 / math.sqrt(HEAD_SIZE)
    groups = attention_key_rows.shape[1] // HEAD_SIZE
    heads_per_group = queries.shape[1] // HEAD_SIZE // groups
    key_span = min(512, total_len)
    blocks = total_len // key_span
    last_pos = offset + tokens - 1
    query_grid = queries.reshape(tokens, groups, heads_per_group, HEAD_SIZE)
    cotangent_table = attention_output_cotangent.reshape(tokens, groups, heads_per_group, HEAD_SIZE)

    def block_view(number):
        anchor = number * key_span
        key_blk = lax.dynamic_slice_in_dim(key_all, anchor, key_span, 0).reshape(
            key_span, groups, HEAD_SIZE
        )
        value_blk = lax.dynamic_slice_in_dim(value_all, anchor, key_span, 0).reshape(
            key_span, groups, HEAD_SIZE
        )
        key_pos = anchor + jnp.arange(key_span, dtype=jnp.int32)
        allowed = (key_pos[None, :] <= positions[:, None]) & (
            doc_index(key_pos, doc_lengths)[None, :] == segment[:, None]
        )
        scores = (
            jnp.einsum("tgrd,kgd->grtk", query_grid, key_blk, preferred_element_type=jnp.float32)
            * logit_scale
        )
        scores = jnp.where(allowed[None, None], scores, big_negative)
        return (anchor, key_blk, value_blk, allowed, scores)

    def visit(number, carried, work):
        return lax.cond(
            number * key_span <= last_pos,
            lambda inner: work(number, inner),
            lambda inner: inner,
            carried,
        )

    def stats_step(number, carried):
        row_peak, row_total = carried
        anchor, key_blk, value_blk, allowed, scores = block_view(number)
        new_peak = jnp.maximum(row_peak, jnp.max(scores, axis=-1))
        fresh = jnp.sum(
            jnp.where(allowed[None, None], jnp.exp(scores - new_peak[..., None]), 0.0), axis=-1
        )
        return (new_peak, row_total * jnp.exp(row_peak - new_peak) + fresh)

    stat_shape = (groups, heads_per_group, tokens)
    row_peak, row_total = lax.fori_loop(
        0,
        blocks,
        lambda number, carried: visit(number, carried, stats_step),
        (jnp.full(stat_shape, big_negative, jnp.float32), jnp.zeros(stat_shape, jnp.float32)),
    )
    log_norm = row_peak + jnp.log(row_total)

    def output_step(number, totals):
        anchor, key_blk, value_blk, allowed, scores = block_view(number)
        weights = jnp.where(allowed[None, None], jnp.exp(scores - log_norm[..., None]), 0.0).astype(
            jnp.bfloat16
        )
        return totals + jnp.einsum(
            "grtk,kgd->tgrd", weights, value_blk, preferred_element_type=jnp.float32
        )

    attention_table = lax.fori_loop(
        0,
        blocks,
        lambda number, carried: visit(number, carried, output_step),
        jnp.zeros((tokens, groups, heads_per_group, HEAD_SIZE), jnp.float32),
    ).astype(jnp.bfloat16)
    row_products = jnp.einsum(
        "bkfh,bkfh->kfb", cotangent_table, attention_table, preferred_element_type=jnp.float32
    )

    def grad_terms(allowed, scores, value_blk):
        probs_full = jnp.where(allowed[None, None], jnp.exp(scores - log_norm[..., None]), 0.0)
        grad_prob = jnp.einsum(
            "tgrd,kgd->grtk", cotangent_table, value_blk, preferred_element_type=jnp.float32
        )
        grad_score = (probs_full * (grad_prob - row_products[..., None])).astype(jnp.bfloat16)
        return (probs_full.astype(jnp.bfloat16), grad_score)

    query_zero = jnp.zeros((tokens, groups, heads_per_group, HEAD_SIZE), jnp.float32)

    def full_step(number, carried):
        grad_query, term_key, term_value = carried
        anchor, key_blk, value_blk, allowed, scores = block_view(number)
        weights, grad_score = grad_terms(allowed, scores, value_blk)
        grad_query = grad_query + jnp.einsum(
            "grtk,kgd->tgrd", grad_score, key_blk, preferred_element_type=jnp.float32
        )
        key_part = jnp.einsum(
            "grtk,tgrd->kgd", grad_score, query_grid, preferred_element_type=jnp.float32
        ).reshape(key_span, groups * HEAD_SIZE)
        value_part = jnp.einsum(
            "grtk,tgrd->kgd", weights, cotangent_table, preferred_element_type=jnp.float32
        ).reshape(key_span, groups * HEAD_SIZE)
        term_key = lax.dynamic_update_slice_in_dim(term_key, key_part, anchor, 0)
        term_value = lax.dynamic_update_slice_in_dim(term_value, value_part, anchor, 0)
        return (grad_query, term_key, term_value)

    term_zero = jnp.zeros((total_len, groups * HEAD_SIZE), jnp.float32)
    grad_query, term_key, term_value = lax.fori_loop(
        0,
        blocks,
        lambda number, carried: visit(number, carried, full_step),
        (query_zero, term_zero, term_zero),
    )
    kv_terms = jnp.concatenate([term_key, term_value], axis=1).astype(jnp.bfloat16)
    kv_width = kv_terms.shape[1]
    if by_heads:
        kv_got = lax.all_to_all(
            jnp.concatenate(
                [
                    kv_terms.reshape(seq_count, tokens, kv_width),
                    mixed_own.reshape(seq_count, tokens, own_width),
                ],
                axis=2,
            ),
            "seq",
            split_axis=0,
            concat_axis=0,
            tiled=True,
        )
        sent = jnp.concatenate(
            [
                x_grad_own.reshape(seq_count, tokens, own_width),
                bc_part.astype(jnp.bfloat16).reshape(seq_count, tokens, bc_part.shape[1]),
            ],
            axis=2,
        )
        got = lax.all_to_all(sent, "seq", split_axis=0, concat_axis=0, tiled=True)

        def from_owners(a):
            return a.transpose(1, 0, 2).reshape(tokens, seq_count * own_width)

        mixer_out = from_owners(kv_got[:, :, kv_width:])
        x_grad = from_owners(got[:, :, :own_width])
        kv_total = jnp.sum(kv_got[:, :, :kv_width].astype(jnp.float32), axis=0)
        bc_sum = jnp.sum(got[:, :, own_width:].astype(jnp.float32), axis=0)
        grad_decay = bc_sum[:, 2 * state_width :].T
        bc_sum = bc_sum[:, : 2 * state_width]
        if lax.axis_size("head") == 2:
            bc_sum = bc_sum + lax.ppermute(bc_sum, "head", [(0, 1), (1, 0)])
        else:
            bc_sum = lax.psum(bc_sum, "head")
        grad_b, grad_c = bc_sum[:, :state_width], bc_sum[:, state_width:]
    else:
        kv_terms = lax.all_to_all(
            kv_terms.reshape(seq_count, tokens, kv_width),
            "seq",
            split_axis=0,
            concat_axis=0,
            tiled=True,
        )
        kv_total = jnp.sum(kv_terms.astype(jnp.float32), axis=0)
    key_gradient_total = kv_total[:, : groups * HEAD_SIZE]
    value_gradient_total = kv_total[:, groups * HEAD_SIZE :]
    attn_out = attention_table.reshape(tokens, groups * heads_per_group * HEAD_SIZE)
    q_grad = (
        (grad_query * logit_scale)
        .reshape(tokens, groups * heads_per_group * HEAD_SIZE)
        .astype(jnp.bfloat16)
    )
    key_gradient = (key_gradient_total * logit_scale).astype(jnp.bfloat16)
    value_gradient = value_gradient_total.astype(jnp.bfloat16)
    return (
        mixer_out,
        attn_out,
        x_grad,
        grad_b,
        grad_c,
        grad_decay,
        q_grad,
        key_gradient,
        value_gradient,
    )


def solution(mesh):
    placed = (
        P(("groups", "seq"), "head"),
        P(("groups", "seq"), None),
        P(("groups", "seq"), None),
        P(("groups", "head"), "seq"),
        P("head"),
        P("groups"),
        P(("groups", "seq"), "head"),
        P(("groups", "seq"), "head"),
        P(("groups", "seq"), "head"),
        P(("groups", "seq"), "head"),
        P(("groups", "seq"), "head"),
    )
    return jax.shard_map(
        on_device,
        mesh=mesh,
        in_specs=placed,
        out_specs=(
            P(("groups", "seq"), "head"),
            P(("groups", "seq"), "head"),
            P(("groups", "seq"), "head"),
            P(("groups", "seq"), None),
            P(("groups", "seq"), None),
            P(("groups", "head"), "seq"),
            P(("groups", "seq"), "head"),
            P(("groups", "seq"), "head"),
            P(("groups", "seq"), "head"),
        ),
        check_vma=False,
    )
```

```python
import math

import jax
import jax.numpy as jnp
from jax import lax
from jax.sharding import PartitionSpec as P

P_SIZE = 128
HEAD_SIZE = 128
TOK_SPAN = 128


precise = lax.Precision.DEFAULT
big_negative = -1e30


def entering_2(part, axis, combine, identity, reverse):
    count = lax.axis_size(axis)
    place = lax.axis_index(axis)
    ahead = count - 1 - place if reverse else place
    early = jax.tree.map(lambda a, e: jnp.zeros_like(a) + jnp.asarray(e, a.dtype), part, identity)
    span = part
    shift = 1
    while shift < count:
        if reverse:
            pairs = [(i, i - shift) for i in range(shift, count)]
        else:
            pairs = [(i, i + shift) for i in range(count - shift)]
        got = lax.ppermute(span, axis, pairs)
        have = ahead >= shift
        got = jax.tree.map(lambda g, e: jnp.where(have, g, jnp.asarray(e, g.dtype)), got, identity)
        early = combine(got, early)
        if 2 * shift < count:
            span = combine(got, span)
        shift *= 2
    return early


def doc_index(positions, lengths):
    ends = jnp.cumsum(lengths)
    return jnp.sum((positions[:, None] >= ends[None, :]).astype(jnp.int32), axis=1)


def cumulate(decay):
    return jnp.cumsum(decay, axis=1)


def local_state(inputs, b_float, cumulated, segment):
    weights = (
        jnp.exp(cumulated[:, -1:] - cumulated)
        * (segment == segment[-1]).astype(inputs.dtype)[None, :]
    )
    return jnp.einsum("hs,sn,shp->hnp", weights, b_float, inputs, precision=precise)


def carry_factor(cumulated, segment, before):
    return jnp.exp(cumulated[:, -1]) * (segment[-1] == before).astype(cumulated.dtype)


def mixer_stretch(inputs, b_float, c_float, decay, gains, segment, before, state_in):
    cumulated = cumulate(decay)
    width = inputs.shape[0]
    steps = jnp.arange(width)
    allowed = (steps[:, None] >= steps[None, :]) & (segment[:, None] == segment[None, :])
    gaps = jnp.where(allowed[None], cumulated[:, :, None] - cumulated[:, None, :], big_negative)
    kernel = jnp.exp(gaps) * jnp.dot(c_float, b_float.T, precision=precise)[None]
    inner = jnp.einsum("hts,shp->thp", kernel, inputs, precision=precise)
    keeps = (segment == before).astype(inputs.dtype)
    entering = jnp.einsum("tn,hnp->thp", c_float, state_in, precision=precise)
    reach = jnp.exp(cumulated).T * keeps[:, None]
    outputs = inner + reach[:, :, None] * entering + gains[None, :, None] * inputs
    factor = carry_factor(cumulated, segment, before)
    state_out = factor[:, None, None] * state_in + local_state(inputs, b_float, cumulated, segment)
    return (outputs, state_out)


def combine_states(earlier, later):
    return (earlier[0] * later[0], later[0][:, None, None] * earlier[1] + later[1])


def mixer_whole(inputs, b_float, c_float, decay, gains, segment):
    width = TOK_SPAN
    count = inputs.shape[0] // width
    heads = inputs.shape[1]
    inp = inputs.reshape(count, width, heads, P_SIZE)
    b_blocks = b_float.reshape(count, width, -1)
    c_blocks = c_float.reshape(count, width, -1)
    dec = decay.reshape(heads, count, width).transpose(1, 0, 2)
    seg = segment.reshape(count, width)
    befores = jnp.concatenate([jnp.full((1,), -1, seg.dtype), seg[:-1, -1]])
    cumulated = jnp.cumsum(dec, axis=2)
    factor = jax.vmap(carry_factor)(cumulated, seg, befores)
    summary = jax.vmap(local_state)(inp, b_blocks, cumulated, seg)

    columns = jnp.arange(count)[:, None]
    row = jnp.zeros((count, heads), factor.dtype)
    rows = [row]
    for k in range(1, count):
        row = jnp.where(columns < k - 1, row * factor[k - 1][None, :], (columns == k - 1).astype(factor.dtype))
        rows.append(row)
    reach = jnp.stack(rows)
    state_in = jnp.einsum("kjh,jhnp->khnp", reach, summary, precision=precise)

    def stretch(i, brow, crow, d, sg, bf, st):
        return mixer_stretch(i, brow, crow, d, gains, sg, bf, st)[0]

    outputs = jax.vmap(stretch)(inp, b_blocks, c_blocks, dec, seg, befores, state_in)
    return outputs.reshape(count * width, heads, P_SIZE)


def mamba_by_heads(x_all, cot_all, b_all, c_all, decay_log, skip_gain, doc_lengths):
    seq_count = lax.axis_size("seq")
    place = lax.axis_index("seq")
    heads_here = skip_gain.shape[0]
    own = heads_here // seq_count
    total = x_all.shape[0]
    decay = lax.all_to_all(decay_log, "seq", split_axis=0, concat_axis=1, tiled=True)
    gains = lax.dynamic_slice_in_dim(skip_gain, place * own, own)
    segment = doc_index(jnp.arange(total, dtype=jnp.int32), doc_lengths)
    inputs = x_all.astype(jnp.float32).reshape(total, own, P_SIZE)
    cot = cot_all.astype(jnp.float32).reshape(total, own, P_SIZE)

    def whole_of(i, brow, crow, d):
        return mixer_whole(i, brow, crow, d, gains, segment)

    mixed, pull = jax.vjp(
        whole_of, inputs, b_all.astype(jnp.float32), c_all.astype(jnp.float32), decay
    )
    grad_x, grad_b, grad_c, grad_decay = pull(cot)
    decay_cols = lax.dynamic_update_slice_in_dim(
        jnp.zeros((total, heads_here), jnp.float32), grad_decay.T, place * own, 1
    )
    return (
        mixed.reshape(total, own * P_SIZE).astype(jnp.bfloat16),
        grad_x.reshape(total, own * P_SIZE).astype(jnp.bfloat16),
        jnp.concatenate([grad_b, grad_c, decay_cols], axis=1),
    )


def mamba_by_stretch(
    x_input, b_rows, c_rows, decay_log, skip_gain, doc_lengths, mixer_cot, segment, offset
):
    tokens = x_input.shape[0]
    previous = doc_index(jnp.reshape(offset - 1, (1,)), doc_lengths)[0]
    before = jnp.where(offset > 0, previous, -1)
    heads_here = skip_gain.shape[0]
    inputs = x_input.astype(jnp.float32).reshape(tokens, heads_here, P_SIZE)
    b_float = b_rows.astype(jnp.float32)
    c_float = c_rows.astype(jnp.float32)
    cot_float = mixer_cot.astype(jnp.float32).reshape(tokens, heads_here, P_SIZE)

    def stretch_of(inp, brow, crow, decay, state_in):
        return mixer_stretch(inp, brow, crow, decay, skip_gain, segment, before, state_in)

    cumulated = cumulate(decay_log)
    factor = carry_factor(cumulated, segment, before)
    summary = local_state(inputs, b_float, cumulated, segment)
    zero_state = jnp.zeros_like(summary)
    identity = (jnp.ones_like(factor), zero_state)
    state_in = entering_2((factor, summary), "seq", combine_states, identity, False)[1]
    (mixed, state_out), pull = jax.vjp(stretch_of, inputs, b_float, c_float, decay_log, state_in)
    adjoint_local = pull((cot_float, zero_state))[4]
    adjoint_out = entering_2((factor, adjoint_local), "seq", combine_states, identity, True)[1]
    grad_x, grad_b, grad_c, grad_decay, unused = pull((cot_float, adjoint_out))
    head_count = lax.axis_size("head")
    if head_count == 2:
        other_b, other_c = lax.ppermute((grad_b, grad_c), "head", [(0, 1), (1, 0)])
        grad_b, grad_c = grad_b + other_b, grad_c + other_c
    else:
        grad_b, grad_c = lax.psum((grad_b, grad_c), "head")
    mixer_out = mixed.reshape(tokens, heads_here * P_SIZE).astype(jnp.bfloat16)
    x_grad = grad_x.reshape(tokens, heads_here * P_SIZE).astype(jnp.bfloat16)
    return (mixer_out, x_grad, grad_b, grad_c, grad_decay)


def on_device(
    x_input,
    b_rows,
    c_rows,
    decay_log,
    skip_gain,
    doc_lengths,
    queries,
    attention_key_rows,
    values,
    mixer_cot,
    attention_output_cotangent,
):
    tokens = x_input.shape[0]
    offset = lax.axis_index("seq") * tokens
    total_len = tokens * lax.axis_size("seq")
    positions = offset + jnp.arange(tokens, dtype=jnp.int32)
    segment = doc_index(positions, doc_lengths)
    heads_here = skip_gain.shape[0]
    by_heads = heads_here % lax.axis_size("seq") == 0
    key_width = attention_key_rows.shape[1]
    state_width = b_rows.shape[1]
    seq_count = lax.axis_size("seq")
    if by_heads:
        own_width = heads_here // seq_count * P_SIZE

        def by_owner(a):
            return a.reshape(tokens, seq_count, own_width).transpose(1, 0, 2)

        def spread(a):
            return jnp.broadcast_to(a[None], (seq_count,) + a.shape)

        sent = jnp.concatenate(
            [by_owner(x_input), by_owner(mixer_cot), spread(b_rows), spread(c_rows)], axis=2
        )
        got = lax.all_to_all(sent, "seq", split_axis=0, concat_axis=0, tiled=True)
        x_all = got[:, :, :own_width].reshape(total_len, own_width)
        cot_all = got[:, :, own_width : 2 * own_width].reshape(total_len, own_width)
        b_all = got[:, :, 2 * own_width : 2 * own_width + state_width].reshape(total_len, -1)
        c_all = got[:, :, 2 * own_width + state_width :].reshape(total_len, -1)
        kv_sent = spread(jnp.concatenate([attention_key_rows, values], axis=1))
        gathered = lax.all_to_all(kv_sent, "seq", split_axis=0, concat_axis=0, tiled=True)
        gathered = gathered.reshape(total_len, 2 * key_width)
    else:
        gathered = lax.all_gather(
            jnp.concatenate([attention_key_rows, values], axis=1), "seq", axis=0, tiled=True
        )
    key_all, value_all = gathered[:, :key_width], gathered[:, key_width : 2 * key_width]
    if by_heads:
        mixed_own, x_grad_own, bc_part = mamba_by_heads(
            x_all, cot_all, b_all, c_all, decay_log, skip_gain, doc_lengths
        )
    else:
        mixer_out, x_grad, grad_b, grad_c, grad_decay = mamba_by_stretch(
            x_input, b_rows, c_rows, decay_log, skip_gain, doc_lengths, mixer_cot, segment, offset
        )
    logit_scale = 1.0 / math.sqrt(HEAD_SIZE)
    groups = attention_key_rows.shape[1] // HEAD_SIZE
    heads_per_group = queries.shape[1] // HEAD_SIZE // groups
    key_span = min(512, total_len)
    blocks = total_len // key_span
    last_pos = offset + tokens - 1
    query_grid = queries.reshape(tokens, groups, heads_per_group, HEAD_SIZE)
    cotangent_table = attention_output_cotangent.reshape(tokens, groups, heads_per_group, HEAD_SIZE)

    def block_view(number):
        anchor = number * key_span
        key_blk = lax.dynamic_slice_in_dim(key_all, anchor, key_span, 0).reshape(
            key_span, groups, HEAD_SIZE
        )
        value_blk = lax.dynamic_slice_in_dim(value_all, anchor, key_span, 0).reshape(
            key_span, groups, HEAD_SIZE
        )
        key_pos = anchor + jnp.arange(key_span, dtype=jnp.int32)
        allowed = (key_pos[None, :] <= positions[:, None]) & (
            doc_index(key_pos, doc_lengths)[None, :] == segment[:, None]
        )
        scores = (
            jnp.einsum("tgrd,kgd->grtk", query_grid, key_blk, preferred_element_type=jnp.float32)
            * logit_scale
        )
        scores = jnp.where(allowed[None, None], scores, big_negative)
        return (anchor, key_blk, value_blk, allowed, scores)

    def visit(number, carried, work):
        return lax.cond(
            number * key_span <= last_pos,
            lambda inner: work(number, inner),
            lambda inner: inner,
            carried,
        )

    def stats_step(number, carried):
        row_peak, row_total = carried
        anchor, key_blk, value_blk, allowed, scores = block_view(number)
        new_peak = jnp.maximum(row_peak, jnp.max(scores, axis=-1))
        fresh = jnp.sum(
            jnp.where(allowed[None, None], jnp.exp(scores - new_peak[..., None]), 0.0), axis=-1
        )
        return (new_peak, row_total * jnp.exp(row_peak - new_peak) + fresh)

    stat_shape = (groups, heads_per_group, tokens)
    row_peak, row_total = lax.fori_loop(
        0,
        blocks,
        lambda number, carried: visit(number, carried, stats_step),
        (jnp.full(stat_shape, big_negative, jnp.float32), jnp.zeros(stat_shape, jnp.float32)),
    )
    log_norm = row_peak + jnp.log(row_total)

    def output_step(number, totals):
        anchor, key_blk, value_blk, allowed, scores = block_view(number)
        weights = jnp.where(allowed[None, None], jnp.exp(scores - log_norm[..., None]), 0.0).astype(
            jnp.bfloat16
        )
        return totals + jnp.einsum(
            "grtk,kgd->tgrd", weights, value_blk, preferred_element_type=jnp.float32
        )

    attention_table = lax.fori_loop(
        0,
        blocks,
        lambda number, carried: visit(number, carried, output_step),
        jnp.zeros((tokens, groups, heads_per_group, HEAD_SIZE), jnp.float32),
    ).astype(jnp.bfloat16)
    row_products = jnp.einsum(
        "bkfh,bkfh->kfb", cotangent_table, attention_table, preferred_element_type=jnp.float32
    )

    def grad_terms(allowed, scores, value_blk):
        probs_full = jnp.where(allowed[None, None], jnp.exp(scores - log_norm[..., None]), 0.0)
        grad_prob = jnp.einsum(
            "tgrd,kgd->grtk", cotangent_table, value_blk, preferred_element_type=jnp.float32
        )
        grad_score = (probs_full * (grad_prob - row_products[..., None])).astype(jnp.bfloat16)
        return (probs_full.astype(jnp.bfloat16), grad_score)

    query_zero = jnp.zeros((tokens, groups, heads_per_group, HEAD_SIZE), jnp.float32)

    def full_step(number, carried):
        grad_query, term_key, term_value = carried
        anchor, key_blk, value_blk, allowed, scores = block_view(number)
        weights, grad_score = grad_terms(allowed, scores, value_blk)
        grad_query = grad_query + jnp.einsum(
            "grtk,kgd->tgrd", grad_score, key_blk, preferred_element_type=jnp.float32
        )
        key_part = jnp.einsum(
            "grtk,tgrd->kgd", grad_score, query_grid, preferred_element_type=jnp.float32
        ).reshape(key_span, groups * HEAD_SIZE)
        value_part = jnp.einsum(
            "grtk,tgrd->kgd", weights, cotangent_table, preferred_element_type=jnp.float32
        ).reshape(key_span, groups * HEAD_SIZE)
        term_key = lax.dynamic_update_slice_in_dim(term_key, key_part, anchor, 0)
        term_value = lax.dynamic_update_slice_in_dim(term_value, value_part, anchor, 0)
        return (grad_query, term_key, term_value)

    term_zero = jnp.zeros((total_len, groups * HEAD_SIZE), jnp.float32)
    grad_query, term_key, term_value = lax.fori_loop(
        0,
        blocks,
        lambda number, carried: visit(number, carried, full_step),
        (query_zero, term_zero, term_zero),
    )
    kv_terms = jnp.concatenate([term_key, term_value], axis=1).astype(jnp.bfloat16)
    kv_width = kv_terms.shape[1]
    if by_heads:
        kv_got = lax.all_to_all(
            jnp.concatenate(
                [
                    kv_terms.reshape(seq_count, tokens, kv_width),
                    mixed_own.reshape(seq_count, tokens, own_width),
                ],
                axis=2,
            ),
            "seq",
            split_axis=0,
            concat_axis=0,
            tiled=True,
        )
        sent = jnp.concatenate(
            [
                x_grad_own.reshape(seq_count, tokens, own_width),
                bc_part.astype(jnp.bfloat16).reshape(seq_count, tokens, bc_part.shape[1]),
            ],
            axis=2,
        )
        got = lax.all_to_all(sent, "seq", split_axis=0, concat_axis=0, tiled=True)

        def from_owners(a):
            return a.transpose(1, 0, 2).reshape(tokens, seq_count * own_width)

        mixer_out = from_owners(kv_got[:, :, kv_width:])
        x_grad = from_owners(got[:, :, :own_width])
        kv_total = jnp.sum(kv_got[:, :, :kv_width].astype(jnp.float32), axis=0)
        bc_sum = jnp.sum(got[:, :, own_width:].astype(jnp.float32), axis=0)
        grad_decay = bc_sum[:, 2 * state_width :].T
        bc_sum = bc_sum[:, : 2 * state_width]
        if lax.axis_size("head") == 2:
            bc_sum = bc_sum + lax.ppermute(bc_sum, "head", [(0, 1), (1, 0)])
        else:
            bc_sum = lax.psum(bc_sum, "head")
        grad_b, grad_c = bc_sum[:, :state_width], bc_sum[:, state_width:]
    else:
        kv_terms = lax.all_to_all(
            kv_terms.reshape(seq_count, tokens, kv_width),
            "seq",
            split_axis=0,
            concat_axis=0,
            tiled=True,
        )
        kv_total = jnp.sum(kv_terms.astype(jnp.float32), axis=0)
    key_gradient_total = kv_total[:, : groups * HEAD_SIZE]
    value_gradient_total = kv_total[:, groups * HEAD_SIZE :]
    attn_out = attention_table.reshape(tokens, groups * heads_per_group * HEAD_SIZE)
    q_grad = (
        (grad_query * logit_scale)
        .reshape(tokens, groups * heads_per_group * HEAD_SIZE)
        .astype(jnp.bfloat16)
    )
    key_gradient = (key_gradient_total * logit_scale).astype(jnp.bfloat16)
    value_gradient = value_gradient_total.astype(jnp.bfloat16)
    return (
        mixer_out,
        attn_out,
        x_grad,
        grad_b,
        grad_c,
        grad_decay,
        q_grad,
        key_gradient,
        value_gradient,
    )


def solution(mesh):
    placed = (
        P(("groups", "seq"), "head"),
        P(("groups", "seq"), None),
        P(("groups", "seq"), None),
        P(("groups", "head"), "seq"),
        P("head"),
        P("groups"),
        P(("groups", "seq"), "head"),
        P(("groups", "seq"), "head"),
        P(("groups", "seq"), "head"),
        P(("groups", "seq"), "head"),
        P(("groups", "seq"), "head"),
    )
    return jax.shard_map(
        on_device,
        mesh=mesh,
        in_specs=placed,
        out_specs=(
            P(("groups", "seq"), "head"),
            P(("groups", "seq"), "head"),
            P(("groups", "seq"), "head"),
            P(("groups", "seq"), None),
            P(("groups", "seq"), None),
            P(("groups", "head"), "seq"),
            P(("groups", "seq"), "head"),
            P(("groups", "seq"), "head"),
            P(("groups", "seq"), "head"),
        ),
        check_vma=False,
    )
```

```python
import math

import jax
import jax.numpy as jnp
from jax import lax
from jax.sharding import PartitionSpec as P

P_SIZE = 128
HEAD_SIZE = 128
TOK_SPAN = 128


precise = lax.Precision.DEFAULT
big_negative = -1e30


def entering_2(part, axis, combine, identity, reverse):
    count = lax.axis_size(axis)
    place = lax.axis_index(axis)
    ahead = count - 1 - place if reverse else place
    early = jax.tree.map(lambda a, e: jnp.zeros_like(a) + jnp.asarray(e, a.dtype), part, identity)
    span = part
    shift = 1
    while shift < count:
        if reverse:
            pairs = [(i, i - shift) for i in range(shift, count)]
        else:
            pairs = [(i, i + shift) for i in range(count - shift)]
        got = lax.ppermute(span, axis, pairs)
        have = ahead >= shift
        got = jax.tree.map(lambda g, e: jnp.where(have, g, jnp.asarray(e, g.dtype)), got, identity)
        early = combine(got, early)
        if 2 * shift < count:
            span = combine(got, span)
        shift *= 2
    return early


def doc_index(positions, lengths):
    ends = jnp.cumsum(lengths)
    return jnp.sum((positions[:, None] >= ends[None, :]).astype(jnp.int32), axis=1)


def cumulate(decay):
    return jnp.cumsum(decay, axis=1)


def local_state(inputs, b_float, cumulated, segment):
    weights = (
        jnp.exp(cumulated[:, -1:] - cumulated)
        * (segment == segment[-1]).astype(inputs.dtype)[None, :]
    )
    return jnp.einsum("hs,sn,shp->hnp", weights, b_float, inputs, precision=precise)


def carry_factor(cumulated, segment, before):
    return jnp.exp(cumulated[:, -1]) * (segment[-1] == before).astype(cumulated.dtype)


def mixer_stretch(inputs, b_float, c_float, decay, gains, segment, before, state_in):
    cumulated = cumulate(decay)
    width = inputs.shape[0]
    steps = jnp.arange(width)
    allowed = (steps[:, None] >= steps[None, :]) & (segment[:, None] == segment[None, :])
    gaps = jnp.where(allowed[None], cumulated[:, :, None] - cumulated[:, None, :], big_negative)
    kernel = jnp.exp(gaps) * jnp.dot(c_float, b_float.T, precision=precise)[None]
    inner = jnp.einsum("hts,shp->thp", kernel, inputs, precision=precise)
    keeps = (segment == before).astype(inputs.dtype)
    entering = jnp.einsum("tn,hnp->thp", c_float, state_in, precision=precise)
    reach = jnp.exp(cumulated).T * keeps[:, None]
    outputs = inner + reach[:, :, None] * entering + gains[None, :, None] * inputs
    factor = carry_factor(cumulated, segment, before)
    state_out = factor[:, None, None] * state_in + local_state(inputs, b_float, cumulated, segment)
    return (outputs, state_out)


def combine_states(earlier, later):
    return (earlier[0] * later[0], later[0][:, None, None] * earlier[1] + later[1])


def mixer_whole(inputs, b_float, c_float, decay, gains, segment):
    width = TOK_SPAN
    count = inputs.shape[0] // width
    heads = inputs.shape[1]
    inp = inputs.reshape(count, width, heads, P_SIZE)
    b_blocks = b_float.reshape(count, width, -1)
    c_blocks = c_float.reshape(count, width, -1)
    dec = decay.reshape(heads, count, width).transpose(1, 0, 2)
    seg = segment.reshape(count, width)
    befores = jnp.concatenate([jnp.full((1,), -1, seg.dtype), seg[:-1, -1]])
    cumulated = jnp.cumsum(dec, axis=2)
    factor = jax.vmap(carry_factor)(cumulated, seg, befores)
    summary = jax.vmap(local_state)(inp, b_blocks, cumulated, seg)

    columns = jnp.arange(count)[:, None]
    row = jnp.zeros((count, heads), factor.dtype)
    rows = [row]
    for k in range(1, count):
        row = jnp.where(columns < k - 1, row * factor[k - 1][None, :], (columns == k - 1).astype(factor.dtype))
        rows.append(row)
    reach = jnp.stack(rows)
    state_in = jnp.einsum("kjh,jhnp->khnp", reach, summary, precision=precise)

    def stretch(i, brow, crow, d, sg, bf, st):
        return mixer_stretch(i, brow, crow, d, gains, sg, bf, st)[0]

    outputs = jax.vmap(stretch)(inp, b_blocks, c_blocks, dec, seg, befores, state_in)
    return outputs.reshape(count * width, heads, P_SIZE)


def mamba_by_heads(x_all, cot_all, b_all, c_all, decay, skip_gain, doc_lengths):
    seq_count = lax.axis_size("seq")
    place = lax.axis_index("seq")
    heads_here = skip_gain.shape[0]
    own = heads_here // seq_count
    total = x_all.shape[0]
    gains = lax.dynamic_slice_in_dim(skip_gain, place * own, own)
    segment = doc_index(jnp.arange(total, dtype=jnp.int32), doc_lengths)
    inputs = x_all.astype(jnp.float32).reshape(total, own, P_SIZE)
    cot = cot_all.astype(jnp.float32).reshape(total, own, P_SIZE)

    def whole_of(i, brow, crow, d):
        return mixer_whole(i, brow, crow, d, gains, segment)

    mixed, pull = jax.vjp(
        whole_of, inputs, b_all.astype(jnp.float32), c_all.astype(jnp.float32), decay
    )
    grad_x, grad_b, grad_c, grad_decay = pull(cot)
    decay_cols = lax.dynamic_update_slice_in_dim(
        jnp.zeros((total, heads_here), jnp.float32), grad_decay.T, place * own, 1
    )
    return (
        mixed.reshape(total, own * P_SIZE).astype(jnp.bfloat16),
        grad_x.reshape(total, own * P_SIZE).astype(jnp.bfloat16),
        jnp.concatenate([grad_b, grad_c, decay_cols], axis=1),
    )


def mamba_by_stretch(
    x_input, b_rows, c_rows, decay_log, skip_gain, doc_lengths, mixer_cot, segment, offset
):
    tokens = x_input.shape[0]
    previous = doc_index(jnp.reshape(offset - 1, (1,)), doc_lengths)[0]
    before = jnp.where(offset > 0, previous, -1)
    heads_here = skip_gain.shape[0]
    inputs = x_input.astype(jnp.float32).reshape(tokens, heads_here, P_SIZE)
    b_float = b_rows.astype(jnp.float32)
    c_float = c_rows.astype(jnp.float32)
    cot_float = mixer_cot.astype(jnp.float32).reshape(tokens, heads_here, P_SIZE)

    def stretch_of(inp, brow, crow, decay, state_in):
        return mixer_stretch(inp, brow, crow, decay, skip_gain, segment, before, state_in)

    cumulated = cumulate(decay_log)
    factor = carry_factor(cumulated, segment, before)
    summary = local_state(inputs, b_float, cumulated, segment)
    zero_state = jnp.zeros_like(summary)
    identity = (jnp.ones_like(factor), zero_state)
    state_in = entering_2((factor, summary), "seq", combine_states, identity, False)[1]
    (mixed, state_out), pull = jax.vjp(stretch_of, inputs, b_float, c_float, decay_log, state_in)
    adjoint_local = pull((cot_float, zero_state))[4]
    adjoint_out = entering_2((factor, adjoint_local), "seq", combine_states, identity, True)[1]
    grad_x, grad_b, grad_c, grad_decay, unused = pull((cot_float, adjoint_out))
    head_count = lax.axis_size("head")
    if head_count == 2:
        other_b, other_c = lax.ppermute((grad_b, grad_c), "head", [(0, 1), (1, 0)])
        grad_b, grad_c = grad_b + other_b, grad_c + other_c
    else:
        grad_b, grad_c = lax.psum((grad_b, grad_c), "head")
    mixer_out = mixed.reshape(tokens, heads_here * P_SIZE).astype(jnp.bfloat16)
    x_grad = grad_x.reshape(tokens, heads_here * P_SIZE).astype(jnp.bfloat16)
    return (mixer_out, x_grad, grad_b, grad_c, grad_decay)


def on_device(
    x_input,
    b_rows,
    c_rows,
    decay_log,
    skip_gain,
    doc_lengths,
    queries,
    attention_key_rows,
    values,
    mixer_cot,
    attention_output_cotangent,
):
    tokens = x_input.shape[0]
    offset = lax.axis_index("seq") * tokens
    total_len = tokens * lax.axis_size("seq")
    positions = offset + jnp.arange(tokens, dtype=jnp.int32)
    segment = doc_index(positions, doc_lengths)
    heads_here = skip_gain.shape[0]
    by_heads = heads_here % lax.axis_size("seq") == 0
    key_width = attention_key_rows.shape[1]
    state_width = b_rows.shape[1]
    seq_count = lax.axis_size("seq")
    if by_heads:
        own_width = heads_here // seq_count * P_SIZE

        def by_owner(a):
            return a.reshape(tokens, seq_count, own_width).transpose(1, 0, 2)

        def spread(a):
            return jnp.broadcast_to(a[None], (seq_count,) + a.shape)

        decay_parts = []
        rest = decay_log
        for scale in (2.0**8, 2.0**16, 2.0**24, 2.0**32):
            part = jnp.round(rest * scale) / scale
            rest = rest - part
            decay_parts.append(part)
        decay_sent = jnp.concatenate(decay_parts, axis=0).astype(jnp.bfloat16)
        decay_sent = decay_sent.reshape(len(decay_parts), seq_count, heads_here // seq_count, tokens)
        decay_sent = decay_sent.transpose(1, 3, 0, 2).reshape(seq_count, tokens, -1)
        sent = jnp.concatenate(
            [
                by_owner(x_input),
                by_owner(mixer_cot),
                spread(b_rows),
                spread(c_rows),
                decay_sent,
            ],
            axis=2,
        )
        got = lax.all_to_all(sent, "seq", split_axis=0, concat_axis=0, tiled=True)
        x_all = got[:, :, :own_width].reshape(total_len, own_width)
        cot_all = got[:, :, own_width : 2 * own_width].reshape(total_len, own_width)
        b_all = got[:, :, 2 * own_width : 2 * own_width + state_width].reshape(total_len, -1)
        c_all = got[:, :, 2 * own_width + state_width : 2 * own_width + 2 * state_width]
        c_all = c_all.reshape(total_len, -1)
        decay_got = got[:, :, 2 * own_width + 2 * state_width :].astype(jnp.float32)
        decay_got = decay_got.reshape(total_len, 4, heads_here // seq_count)
        decay_own = ((decay_got[:, 0] + decay_got[:, 1]) + decay_got[:, 2]) + decay_got[:, 3]
        decay_own = decay_own.T
        kv_sent = spread(jnp.concatenate([attention_key_rows, values], axis=1))
        gathered = lax.all_to_all(kv_sent, "seq", split_axis=0, concat_axis=0, tiled=True)
        gathered = gathered.reshape(total_len, 2 * key_width)
    else:
        gathered = lax.all_gather(
            jnp.concatenate([attention_key_rows, values], axis=1), "seq", axis=0, tiled=True
        )
    key_all, value_all = gathered[:, :key_width], gathered[:, key_width : 2 * key_width]
    if by_heads:
        mixed_own, x_grad_own, bc_part = mamba_by_heads(
            x_all, cot_all, b_all, c_all, decay_own, skip_gain, doc_lengths
        )
    else:
        mixer_out, x_grad, grad_b, grad_c, grad_decay = mamba_by_stretch(
            x_input, b_rows, c_rows, decay_log, skip_gain, doc_lengths, mixer_cot, segment, offset
        )
    logit_scale = 1.0 / math.sqrt(HEAD_SIZE)
    groups = attention_key_rows.shape[1] // HEAD_SIZE
    heads_per_group = queries.shape[1] // HEAD_SIZE // groups
    key_span = min(512, total_len)
    blocks = total_len // key_span
    last_pos = offset + tokens - 1
    query_grid = queries.reshape(tokens, groups, heads_per_group, HEAD_SIZE)
    cotangent_table = attention_output_cotangent.reshape(tokens, groups, heads_per_group, HEAD_SIZE)

    def block_view(number):
        anchor = number * key_span
        key_blk = lax.dynamic_slice_in_dim(key_all, anchor, key_span, 0).reshape(
            key_span, groups, HEAD_SIZE
        )
        value_blk = lax.dynamic_slice_in_dim(value_all, anchor, key_span, 0).reshape(
            key_span, groups, HEAD_SIZE
        )
        key_pos = anchor + jnp.arange(key_span, dtype=jnp.int32)
        allowed = (key_pos[None, :] <= positions[:, None]) & (
            doc_index(key_pos, doc_lengths)[None, :] == segment[:, None]
        )
        scores = (
            jnp.einsum("tgrd,kgd->grtk", query_grid, key_blk, preferred_element_type=jnp.float32)
            * logit_scale
        )
        scores = jnp.where(allowed[None, None], scores, big_negative)
        return (anchor, key_blk, value_blk, allowed, scores)

    def visit(number, carried, work):
        return lax.cond(
            number * key_span <= last_pos,
            lambda inner: work(number, inner),
            lambda inner: inner,
            carried,
        )

    def stats_step(number, carried):
        row_peak, row_total = carried
        anchor, key_blk, value_blk, allowed, scores = block_view(number)
        new_peak = jnp.maximum(row_peak, jnp.max(scores, axis=-1))
        fresh = jnp.sum(
            jnp.where(allowed[None, None], jnp.exp(scores - new_peak[..., None]), 0.0), axis=-1
        )
        return (new_peak, row_total * jnp.exp(row_peak - new_peak) + fresh)

    stat_shape = (groups, heads_per_group, tokens)
    row_peak, row_total = lax.fori_loop(
        0,
        blocks,
        lambda number, carried: visit(number, carried, stats_step),
        (jnp.full(stat_shape, big_negative, jnp.float32), jnp.zeros(stat_shape, jnp.float32)),
    )
    log_norm = row_peak + jnp.log(row_total)

    def output_step(number, totals):
        anchor, key_blk, value_blk, allowed, scores = block_view(number)
        weights = jnp.where(allowed[None, None], jnp.exp(scores - log_norm[..., None]), 0.0).astype(
            jnp.bfloat16
        )
        return totals + jnp.einsum(
            "grtk,kgd->tgrd", weights, value_blk, preferred_element_type=jnp.float32
        )

    attention_table = lax.fori_loop(
        0,
        blocks,
        lambda number, carried: visit(number, carried, output_step),
        jnp.zeros((tokens, groups, heads_per_group, HEAD_SIZE), jnp.float32),
    ).astype(jnp.bfloat16)
    row_products = jnp.einsum(
        "bkfh,bkfh->kfb", cotangent_table, attention_table, preferred_element_type=jnp.float32
    )

    def grad_terms(allowed, scores, value_blk):
        probs_full = jnp.where(allowed[None, None], jnp.exp(scores - log_norm[..., None]), 0.0)
        grad_prob = jnp.einsum(
            "tgrd,kgd->grtk", cotangent_table, value_blk, preferred_element_type=jnp.float32
        )
        grad_score = (probs_full * (grad_prob - row_products[..., None])).astype(jnp.bfloat16)
        return (probs_full.astype(jnp.bfloat16), grad_score)

    query_zero = jnp.zeros((tokens, groups, heads_per_group, HEAD_SIZE), jnp.float32)

    def full_step(number, carried):
        grad_query, term_key, term_value = carried
        anchor, key_blk, value_blk, allowed, scores = block_view(number)
        weights, grad_score = grad_terms(allowed, scores, value_blk)
        grad_query = grad_query + jnp.einsum(
            "grtk,kgd->tgrd", grad_score, key_blk, preferred_element_type=jnp.float32
        )
        key_part = jnp.einsum(
            "grtk,tgrd->kgd", grad_score, query_grid, preferred_element_type=jnp.float32
        ).reshape(key_span, groups * HEAD_SIZE)
        value_part = jnp.einsum(
            "grtk,tgrd->kgd", weights, cotangent_table, preferred_element_type=jnp.float32
        ).reshape(key_span, groups * HEAD_SIZE)
        term_key = lax.dynamic_update_slice_in_dim(term_key, key_part, anchor, 0)
        term_value = lax.dynamic_update_slice_in_dim(term_value, value_part, anchor, 0)
        return (grad_query, term_key, term_value)

    term_zero = jnp.zeros((total_len, groups * HEAD_SIZE), jnp.float32)
    grad_query, term_key, term_value = lax.fori_loop(
        0,
        blocks,
        lambda number, carried: visit(number, carried, full_step),
        (query_zero, term_zero, term_zero),
    )
    kv_terms = jnp.concatenate([term_key, term_value], axis=1).astype(jnp.bfloat16)
    kv_width = kv_terms.shape[1]
    if by_heads:
        kv_got = lax.all_to_all(
            jnp.concatenate(
                [
                    kv_terms.reshape(seq_count, tokens, kv_width),
                    mixed_own.reshape(seq_count, tokens, own_width),
                ],
                axis=2,
            ),
            "seq",
            split_axis=0,
            concat_axis=0,
            tiled=True,
        )
        sent = jnp.concatenate(
            [
                x_grad_own.reshape(seq_count, tokens, own_width),
                bc_part.astype(jnp.bfloat16).reshape(seq_count, tokens, bc_part.shape[1]),
            ],
            axis=2,
        )
        got = lax.all_to_all(sent, "seq", split_axis=0, concat_axis=0, tiled=True)

        def from_owners(a):
            return a.transpose(1, 0, 2).reshape(tokens, seq_count * own_width)

        mixer_out = from_owners(kv_got[:, :, kv_width:])
        x_grad = from_owners(got[:, :, :own_width])
        kv_total = jnp.sum(kv_got[:, :, :kv_width].astype(jnp.float32), axis=0)
        bc_sum = jnp.sum(got[:, :, own_width:].astype(jnp.float32), axis=0)
        grad_decay = bc_sum[:, 2 * state_width :].T
        bc_sum = bc_sum[:, : 2 * state_width]
        if lax.axis_size("head") == 2:
            bc_sum = bc_sum + lax.ppermute(bc_sum, "head", [(0, 1), (1, 0)])
        else:
            bc_sum = lax.psum(bc_sum, "head")
        grad_b, grad_c = bc_sum[:, :state_width], bc_sum[:, state_width:]
    else:
        kv_terms = lax.all_to_all(
            kv_terms.reshape(seq_count, tokens, kv_width),
            "seq",
            split_axis=0,
            concat_axis=0,
            tiled=True,
        )
        kv_total = jnp.sum(kv_terms.astype(jnp.float32), axis=0)
    key_gradient_total = kv_total[:, : groups * HEAD_SIZE]
    value_gradient_total = kv_total[:, groups * HEAD_SIZE :]
    attn_out = attention_table.reshape(tokens, groups * heads_per_group * HEAD_SIZE)
    q_grad = (
        (grad_query * logit_scale)
        .reshape(tokens, groups * heads_per_group * HEAD_SIZE)
        .astype(jnp.bfloat16)
    )
    key_gradient = (key_gradient_total * logit_scale).astype(jnp.bfloat16)
    value_gradient = value_gradient_total.astype(jnp.bfloat16)
    return (
        mixer_out,
        attn_out,
        x_grad,
        grad_b,
        grad_c,
        grad_decay,
        q_grad,
        key_gradient,
        value_gradient,
    )


def solution(mesh):
    placed = (
        P(("groups", "seq"), "head"),
        P(("groups", "seq"), None),
        P(("groups", "seq"), None),
        P(("groups", "head"), "seq"),
        P("head"),
        P("groups"),
        P(("groups", "seq"), "head"),
        P(("groups", "seq"), "head"),
        P(("groups", "seq"), "head"),
        P(("groups", "seq"), "head"),
        P(("groups", "seq"), "head"),
    )
    return jax.shard_map(
        on_device,
        mesh=mesh,
        in_specs=placed,
        out_specs=(
            P(("groups", "seq"), "head"),
            P(("groups", "seq"), "head"),
            P(("groups", "seq"), "head"),
            P(("groups", "seq"), None),
            P(("groups", "seq"), None),
            P(("groups", "head"), "seq"),
            P(("groups", "seq"), "head"),
            P(("groups", "seq"), "head"),
            P(("groups", "seq"), "head"),
        ),
        check_vma=False,
    )
```

```python
import math

import jax
import jax.numpy as jnp
from jax import lax
from jax.sharding import PartitionSpec as P

P_SIZE = 128
HEAD_SIZE = 128
TOK_SPAN = 128


precise = lax.Precision.DEFAULT
big_negative = -1e30


def entering_2(part, axis, combine, identity, reverse):
    count = lax.axis_size(axis)
    place = lax.axis_index(axis)
    ahead = count - 1 - place if reverse else place
    early = jax.tree.map(lambda a, e: jnp.zeros_like(a) + jnp.asarray(e, a.dtype), part, identity)
    span = part
    shift = 1
    while shift < count:
        if reverse:
            pairs = [(i, i - shift) for i in range(shift, count)]
        else:
            pairs = [(i, i + shift) for i in range(count - shift)]
        got = lax.ppermute(span, axis, pairs)
        have = ahead >= shift
        got = jax.tree.map(lambda g, e: jnp.where(have, g, jnp.asarray(e, g.dtype)), got, identity)
        early = combine(got, early)
        if 2 * shift < count:
            span = combine(got, span)
        shift *= 2
    return early


def doc_index(positions, lengths):
    ends = jnp.cumsum(lengths)
    return jnp.sum((positions[:, None] >= ends[None, :]).astype(jnp.int32), axis=1)


def cumulate(decay):
    return jnp.cumsum(decay, axis=1)


def local_state(inputs, b_float, cumulated, segment):
    weights = (
        jnp.exp(cumulated[:, -1:] - cumulated)
        * (segment == segment[-1]).astype(inputs.dtype)[None, :]
    )
    return jnp.einsum("hs,sn,shp->hnp", weights, b_float, inputs, precision=precise)


def carry_factor(cumulated, segment, before):
    return jnp.exp(cumulated[:, -1]) * (segment[-1] == before).astype(cumulated.dtype)


def mixer_stretch(inputs, b_float, c_float, decay, gains, segment, before, state_in):
    cumulated = cumulate(decay)
    width = inputs.shape[0]
    steps = jnp.arange(width)
    allowed = (steps[:, None] >= steps[None, :]) & (segment[:, None] == segment[None, :])
    gaps = jnp.where(allowed[None], cumulated[:, :, None] - cumulated[:, None, :], big_negative)
    kernel = jnp.exp(gaps) * jnp.dot(c_float, b_float.T, precision=precise)[None]
    inner = jnp.einsum("hts,shp->thp", kernel, inputs, precision=precise)
    keeps = (segment == before).astype(inputs.dtype)
    entering = jnp.einsum("tn,hnp->thp", c_float, state_in, precision=precise)
    reach = jnp.exp(cumulated).T * keeps[:, None]
    outputs = inner + reach[:, :, None] * entering + gains[None, :, None] * inputs
    factor = carry_factor(cumulated, segment, before)
    state_out = factor[:, None, None] * state_in + local_state(inputs, b_float, cumulated, segment)
    return (outputs, state_out)


def combine_states(earlier, later):
    return (earlier[0] * later[0], later[0][:, None, None] * earlier[1] + later[1])


def mixer_whole(inputs, b_float, c_float, decay, gains, segment):
    width = TOK_SPAN
    count = inputs.shape[0] // width
    heads = inputs.shape[1]
    inp = inputs.reshape(count, width, heads, P_SIZE)
    b_blocks = b_float.reshape(count, width, -1)
    c_blocks = c_float.reshape(count, width, -1)
    dec = decay.reshape(heads, count, width).transpose(1, 0, 2)
    seg = segment.reshape(count, width)
    befores = jnp.concatenate([jnp.full((1,), -1, seg.dtype), seg[:-1, -1]])
    cumulated = jnp.cumsum(dec, axis=2)
    factor = jax.vmap(carry_factor)(cumulated, seg, befores)
    summary = jax.vmap(local_state)(inp, b_blocks, cumulated, seg)

    columns = jnp.arange(count)[:, None]
    row = jnp.zeros((count, heads), factor.dtype)
    rows = [row]
    for k in range(1, count):
        row = jnp.where(columns < k - 1, row * factor[k - 1][None, :], (columns == k - 1).astype(factor.dtype))
        rows.append(row)
    reach = jnp.stack(rows)
    state_in = jnp.einsum("kjh,jhnp->khnp", reach, summary, precision=precise)

    def stretch(i, brow, crow, d, sg, bf, st):
        return mixer_stretch(i, brow, crow, d, gains, sg, bf, st)[0]

    outputs = jax.vmap(stretch)(inp, b_blocks, c_blocks, dec, seg, befores, state_in)
    return outputs.reshape(count * width, heads, P_SIZE)


def mamba_by_heads(x_all, cot_all, b_all, c_all, decay_log, skip_gain, doc_lengths):
    seq_count = lax.axis_size("seq")
    place = lax.axis_index("seq")
    heads_here = skip_gain.shape[0]
    own = heads_here // seq_count
    total = x_all.shape[0]
    decay = lax.all_to_all(decay_log, "seq", split_axis=0, concat_axis=1, tiled=True)
    gains = lax.dynamic_slice_in_dim(skip_gain, place * own, own)
    segment = doc_index(jnp.arange(total, dtype=jnp.int32), doc_lengths)
    inputs = x_all.astype(jnp.float32).reshape(total, own, P_SIZE)
    cot = cot_all.astype(jnp.float32).reshape(total, own, P_SIZE)

    def whole_of(i, brow, crow, d):
        return mixer_whole(i, brow, crow, d, gains, segment)

    mixed, pull = jax.vjp(
        whole_of, inputs, b_all.astype(jnp.float32), c_all.astype(jnp.float32), decay
    )
    grad_x, grad_b, grad_c, grad_decay = pull(cot)
    decay_cols = lax.dynamic_update_slice_in_dim(
        jnp.zeros((total, heads_here), jnp.float32), grad_decay.T, place * own, 1
    )
    return (
        mixed.reshape(total, own * P_SIZE).astype(jnp.bfloat16),
        grad_x.reshape(total, own * P_SIZE).astype(jnp.bfloat16),
        jnp.concatenate([grad_b, grad_c, decay_cols], axis=1),
    )


def mamba_by_stretch(
    x_input, b_rows, c_rows, decay_log, skip_gain, doc_lengths, mixer_cot, segment, offset
):
    tokens = x_input.shape[0]
    previous = doc_index(jnp.reshape(offset - 1, (1,)), doc_lengths)[0]
    before = jnp.where(offset > 0, previous, -1)
    heads_here = skip_gain.shape[0]
    inputs = x_input.astype(jnp.float32).reshape(tokens, heads_here, P_SIZE)
    b_float = b_rows.astype(jnp.float32)
    c_float = c_rows.astype(jnp.float32)
    cot_float = mixer_cot.astype(jnp.float32).reshape(tokens, heads_here, P_SIZE)

    def stretch_of(inp, brow, crow, decay, state_in):
        return mixer_stretch(inp, brow, crow, decay, skip_gain, segment, before, state_in)

    cumulated = cumulate(decay_log)
    factor = carry_factor(cumulated, segment, before)
    summary = local_state(inputs, b_float, cumulated, segment)
    zero_state = jnp.zeros_like(summary)
    identity = (jnp.ones_like(factor), zero_state)
    state_in = entering_2((factor, summary), "seq", combine_states, identity, False)[1]
    (mixed, state_out), pull = jax.vjp(stretch_of, inputs, b_float, c_float, decay_log, state_in)
    adjoint_local = pull((cot_float, zero_state))[4]
    adjoint_out = entering_2((factor, adjoint_local), "seq", combine_states, identity, True)[1]
    grad_x, grad_b, grad_c, grad_decay, unused = pull((cot_float, adjoint_out))
    head_count = lax.axis_size("head")
    if head_count == 2:
        other_b, other_c = lax.ppermute((grad_b, grad_c), "head", [(0, 1), (1, 0)])
        grad_b, grad_c = grad_b + other_b, grad_c + other_c
    else:
        grad_b, grad_c = lax.psum((grad_b, grad_c), "head")
    mixer_out = mixed.reshape(tokens, heads_here * P_SIZE).astype(jnp.bfloat16)
    x_grad = grad_x.reshape(tokens, heads_here * P_SIZE).astype(jnp.bfloat16)
    return (mixer_out, x_grad, grad_b, grad_c, grad_decay)


def on_device(
    x_input,
    b_rows,
    c_rows,
    decay_log,
    skip_gain,
    doc_lengths,
    queries,
    attention_key_rows,
    values,
    mixer_cot,
    attention_output_cotangent,
):
    tokens = x_input.shape[0]
    offset = lax.axis_index("seq") * tokens
    total_len = tokens * lax.axis_size("seq")
    positions = offset + jnp.arange(tokens, dtype=jnp.int32)
    segment = doc_index(positions, doc_lengths)
    heads_here = skip_gain.shape[0]
    by_heads = heads_here % lax.axis_size("seq") == 0
    key_width = attention_key_rows.shape[1]
    state_width = b_rows.shape[1]
    seq_count = lax.axis_size("seq")
    if by_heads:
        own_width = heads_here // seq_count * P_SIZE

        def by_owner(a):
            return a.reshape(tokens, seq_count, own_width).transpose(1, 0, 2)

        def spread(a):
            return jnp.broadcast_to(a[None], (seq_count,) + a.shape)

        sent = jnp.concatenate(
            [by_owner(x_input), by_owner(mixer_cot), spread(b_rows), spread(c_rows)], axis=2
        )
        got = lax.all_to_all(sent, "seq", split_axis=0, concat_axis=0, tiled=True)
        x_all = got[:, :, :own_width].reshape(total_len, own_width)
        cot_all = got[:, :, own_width : 2 * own_width].reshape(total_len, own_width)
        b_all = got[:, :, 2 * own_width : 2 * own_width + state_width].reshape(total_len, -1)
        c_all = got[:, :, 2 * own_width + state_width :].reshape(total_len, -1)
        kv_sent = spread(jnp.concatenate([attention_key_rows, values], axis=1))
        gathered = lax.all_to_all(kv_sent, "seq", split_axis=0, concat_axis=0, tiled=True)
        gathered = gathered.reshape(total_len, 2 * key_width)
    else:
        gathered = lax.all_gather(
            jnp.concatenate([attention_key_rows, values], axis=1), "seq", axis=0, tiled=True
        )
    key_all, value_all = gathered[:, :key_width], gathered[:, key_width : 2 * key_width]
    if by_heads:
        mixed_own, x_grad_own, bc_part = mamba_by_heads(
            x_all, cot_all, b_all, c_all, decay_log, skip_gain, doc_lengths
        )
    else:
        mixer_out, x_grad, grad_b, grad_c, grad_decay = mamba_by_stretch(
            x_input, b_rows, c_rows, decay_log, skip_gain, doc_lengths, mixer_cot, segment, offset
        )
    logit_scale = 1.0 / math.sqrt(HEAD_SIZE)
    groups = attention_key_rows.shape[1] // HEAD_SIZE
    heads_per_group = queries.shape[1] // HEAD_SIZE // groups
    key_span = min(512, total_len)
    blocks = total_len // key_span
    last_pos = offset + tokens - 1
    query_grid = queries.reshape(tokens, groups, heads_per_group, HEAD_SIZE)
    cotangent_table = attention_output_cotangent.reshape(tokens, groups, heads_per_group, HEAD_SIZE)

    def block_view(number):
        anchor = number * key_span
        key_blk = lax.dynamic_slice_in_dim(key_all, anchor, key_span, 0).reshape(
            key_span, groups, HEAD_SIZE
        )
        value_blk = lax.dynamic_slice_in_dim(value_all, anchor, key_span, 0).reshape(
            key_span, groups, HEAD_SIZE
        )
        key_pos = anchor + jnp.arange(key_span, dtype=jnp.int32)
        allowed = (key_pos[None, :] <= positions[:, None]) & (
            doc_index(key_pos, doc_lengths)[None, :] == segment[:, None]
        )
        scores = (
            jnp.einsum("tgrd,kgd->grtk", query_grid, key_blk, preferred_element_type=jnp.float32)
            * logit_scale
        )
        scores = jnp.where(allowed[None, None], scores, big_negative)
        return (anchor, key_blk, value_blk, allowed, scores)

    def visit(number, carried, work):
        return lax.cond(
            number * key_span <= last_pos,
            lambda inner: work(number, inner),
            lambda inner: inner,
            carried,
        )

    def stats_step(number, carried):
        row_peak, row_total = carried
        anchor, key_blk, value_blk, allowed, scores = block_view(number)
        new_peak = jnp.maximum(row_peak, jnp.max(scores, axis=-1))
        fresh = jnp.sum(
            jnp.where(allowed[None, None], jnp.exp(scores - new_peak[..., None]), 0.0), axis=-1
        )
        return (new_peak, row_total * jnp.exp(row_peak - new_peak) + fresh)

    stat_shape = (groups, heads_per_group, tokens)
    row_peak, row_total = lax.fori_loop(
        0,
        blocks,
        lambda number, carried: visit(number, carried, stats_step),
        (jnp.full(stat_shape, big_negative, jnp.float32), jnp.zeros(stat_shape, jnp.float32)),
    )
    log_norm = row_peak + jnp.log(row_total)

    def output_step(number, totals):
        anchor, key_blk, value_blk, allowed, scores = block_view(number)
        weights = jnp.where(allowed[None, None], jnp.exp(scores - log_norm[..., None]), 0.0).astype(
            jnp.bfloat16
        )
        return totals + jnp.einsum(
            "grtk,kgd->tgrd", weights, value_blk, preferred_element_type=jnp.float32
        )

    attention_table = lax.fori_loop(
        0,
        blocks,
        lambda number, carried: visit(number, carried, output_step),
        jnp.zeros((tokens, groups, heads_per_group, HEAD_SIZE), jnp.float32),
    ).astype(jnp.bfloat16)
    row_products = jnp.einsum(
        "bkfh,bkfh->kfb", cotangent_table, attention_table, preferred_element_type=jnp.float32
    )

    def grad_terms(allowed, scores, value_blk):
        probs_full = jnp.where(allowed[None, None], jnp.exp(scores - log_norm[..., None]), 0.0)
        grad_prob = jnp.einsum(
            "tgrd,kgd->grtk", cotangent_table, value_blk, preferred_element_type=jnp.float32
        )
        grad_score = (probs_full * (grad_prob - row_products[..., None])).astype(jnp.bfloat16)
        return (probs_full.astype(jnp.bfloat16), grad_score)

    query_zero = jnp.zeros((tokens, groups, heads_per_group, HEAD_SIZE), jnp.float32)

    def full_step(number, carried):
        grad_query, term_key, term_value = carried
        anchor, key_blk, value_blk, allowed, scores = block_view(number)
        weights, grad_score = grad_terms(allowed, scores, value_blk)
        grad_query = grad_query + jnp.einsum(
            "grtk,kgd->tgrd", grad_score, key_blk, preferred_element_type=jnp.float32
        )
        key_part = jnp.einsum(
            "grtk,tgrd->kgd", grad_score, query_grid, preferred_element_type=jnp.float32
        ).reshape(key_span, groups * HEAD_SIZE)
        value_part = jnp.einsum(
            "grtk,tgrd->kgd", weights, cotangent_table, preferred_element_type=jnp.float32
        ).reshape(key_span, groups * HEAD_SIZE)
        term_key = lax.dynamic_update_slice_in_dim(term_key, key_part, anchor, 0)
        term_value = lax.dynamic_update_slice_in_dim(term_value, value_part, anchor, 0)
        return (grad_query, term_key, term_value)

    term_zero = jnp.zeros((total_len, groups * HEAD_SIZE), jnp.float32)
    grad_query, term_key, term_value = lax.fori_loop(
        0,
        blocks,
        lambda number, carried: visit(number, carried, full_step),
        (query_zero, term_zero, term_zero),
    )
    kv_terms = jnp.concatenate([term_key, term_value], axis=1).astype(jnp.bfloat16)
    kv_width = kv_terms.shape[1]
    if by_heads:
        sent = jnp.concatenate(
            [
                mixed_own.reshape(seq_count, tokens, own_width),
                x_grad_own.reshape(seq_count, tokens, own_width),
                bc_part.astype(jnp.bfloat16).reshape(seq_count, tokens, bc_part.shape[1]),
            ],
            axis=2,
        )
        got = lax.all_to_all(sent, "seq", split_axis=0, concat_axis=0, tiled=True)
        kv_got = lax.all_to_all(
            kv_terms.reshape(seq_count, tokens, kv_width),
            "seq",
            split_axis=0,
            concat_axis=0,
            tiled=True,
        )

        def from_owners(a):
            return a.transpose(1, 0, 2).reshape(tokens, seq_count * own_width)

        mixer_out = from_owners(got[:, :, :own_width])
        x_grad = from_owners(got[:, :, own_width : 2 * own_width])
        kv_total = jnp.sum(kv_got.astype(jnp.float32), axis=0)
        bc_sum = jnp.sum(got[:, :, 2 * own_width :].astype(jnp.float32), axis=0)
        grad_decay = bc_sum[:, 2 * state_width :].T
        bc_sum = bc_sum[:, : 2 * state_width]
        if lax.axis_size("head") == 2:
            bc_sum = bc_sum + lax.ppermute(bc_sum, "head", [(0, 1), (1, 0)])
        else:
            bc_sum = lax.psum(bc_sum, "head")
        grad_b, grad_c = bc_sum[:, :state_width], bc_sum[:, state_width:]
    else:
        kv_terms = lax.all_to_all(
            kv_terms.reshape(seq_count, tokens, kv_width),
            "seq",
            split_axis=0,
            concat_axis=0,
            tiled=True,
        )
        kv_total = jnp.sum(kv_terms.astype(jnp.float32), axis=0)
    key_gradient_total = kv_total[:, : groups * HEAD_SIZE]
    value_gradient_total = kv_total[:, groups * HEAD_SIZE :]
    attn_out = attention_table.reshape(tokens, groups * heads_per_group * HEAD_SIZE)
    q_grad = (
        (grad_query * logit_scale)
        .reshape(tokens, groups * heads_per_group * HEAD_SIZE)
        .astype(jnp.bfloat16)
    )
    key_gradient = (key_gradient_total * logit_scale).astype(jnp.bfloat16)
    value_gradient = value_gradient_total.astype(jnp.bfloat16)
    return (
        mixer_out,
        attn_out,
        x_grad,
        grad_b,
        grad_c,
        grad_decay,
        q_grad,
        key_gradient,
        value_gradient,
    )


def solution(mesh):
    placed = (
        P(("groups", "seq"), "head"),
        P(("groups", "seq"), None),
        P(("groups", "seq"), None),
        P(("groups", "head"), "seq"),
        P("head"),
        P("groups"),
        P(("groups", "seq"), "head"),
        P(("groups", "seq"), "head"),
        P(("groups", "seq"), "head"),
        P(("groups", "seq"), "head"),
        P(("groups", "seq"), "head"),
    )
    return jax.shard_map(
        on_device,
        mesh=mesh,
        in_specs=placed,
        out_specs=(
            P(("groups", "seq"), "head"),
            P(("groups", "seq"), "head"),
            P(("groups", "seq"), "head"),
            P(("groups", "seq"), None),
            P(("groups", "seq"), None),
            P(("groups", "head"), "seq"),
            P(("groups", "seq"), "head"),
            P(("groups", "seq"), "head"),
            P(("groups", "seq"), "head"),
        ),
        check_vma=False,
    )
```
